32 devices in a mesh: parts: 2 (over x), chain: 16 (over z, y, core).
Axes of the slice: x: 2, y: 2, z: 4, core: 2. Of those that a mesh axis runs over, the one named last changes fastest.
Arguments:
- subspace: float32 [64, 8192], P('parts', 'chain'), parts along dimension 0, may hold values from -4 to 4
- s_inv: float32 [8, 32, 2, 256, 256], P('parts', 'chain'), parts along dimension 0, may hold values from -1 to 1
- couple: float32 [32, 512, 256], P('chain', 'parts'), parts along dimension 1, may hold values from -1 to 1
- diag_blocks: float32 [32, 512, 256], P('chain', 'parts'), parts along dimension 1, may hold values from -4 to 4
- weights: float32 [8, 2], P('parts'), parts along dimension 0, may hold values from -1 to 1
Outputs:
- filtered: float32 [64, 8192], P('parts', 'chain'), parts along dimension 0
- applied: float32 [64, 8192], P('parts', 'chain'), parts along dimension 0
- grams: float32 [2, 64, 32], P(None, 'parts'), parts along dimension 1
The draws below stay inside these ranges and needn't reach their ends.
There are 2 independent parts, one for each index of `parts`. The reference program is written for one: setup_inputs(seed, part) draws one part's arguments, and reference() takes and returns one part's arrays. A program takes and returns all parts, laid end to end along the dimension named above; each array names one. Nothing has to cross between parts.
All inputs are finite; a program needn't handle non-finite values.
Results may differ from the reference program's by a relative error of at most 0.00027.
Values sent between devices are 32-bit elements; how exact they have to be, the bound alone decides.
No kernel may reach another device: no remote copies, remote signals or barrier semaphores. Data moves between devices by JAX's collectives and lax.ppermute only.
A program may use at most 192 MiB of HBM per device.

```python
import math
import jax
import jax.numpy as jnp
from jax import lax

KB = 256
NV = 32
QUAD = 4
NB = 32
ORDER = 8192


def draw_s_inv(key, part):
    subkeys = jax.random.split(key, 3)
    full_shape = (QUAD, NB, 2, KB, KB)
    row_ids = lax.broadcasted_iota(jnp.int32, full_shape, 3)
    col_ids = lax.broadcasted_iota(jnp.int32, full_shape, 4)
    identity = (row_ids == col_ids).astype(jnp.float32)
    component = lax.broadcasted_iota(jnp.int32, full_shape, 2)
    spread = jnp.clip(jax.random.normal(subkeys[0], full_shape, jnp.float32), -4.0, 4.0)
    target = math.exp(-2.0 / NB)
    center = math.sqrt(target - 0.21)
    real_diag = center * jax.random.uniform(subkeys[1], (QUAD, NB, 1, KB, 1), jnp.float32, 0.9, 1.1)
    imag_diag = jax.random.uniform(subkeys[2], (QUAD, NB, 1, KB, 1), jnp.float32, -0.3, 0.3)
    diagonal = jnp.where(component == 0, real_diag, imag_diag)
    values = 0.3 * KB ** (-0.5) * spread + identity * diagonal
    return jnp.clip(values, -1.0, 1.0)


def draw_couple(key, part):
    subkeys = jax.random.split(key, 1)
    full_shape = (NB, KB, KB)
    spread = jnp.clip(jax.random.normal(subkeys[0], full_shape, jnp.float32), -4.0, 4.0)
    return jnp.clip(KB ** (-0.5) * spread, -1.0, 1.0)


def draw_diag_blocks(key, part):
    subkeys = jax.random.split(key, 2)
    full_shape = (NB, KB, KB)
    row_ids = lax.broadcasted_iota(jnp.int32, full_shape, 1)
    col_ids = lax.broadcasted_iota(jnp.int32, full_shape, 2)
    identity = (row_ids == col_ids).astype(jnp.float32)
    spread = jnp.clip(jax.random.normal(subkeys[0], full_shape, jnp.float32), -4.0, 4.0)
    diagonal = jnp.exp(jax.random.uniform(subkeys[1], (NB, KB, 1), jnp.float32, -0.6931472, 1.3862944))
    values = 0.5 * KB ** (-0.5) * spread + identity * diagonal
    return jnp.clip(values, -4.0, 4.0)


def draw_subspace(key, part):
    subkeys = jax.random.split(key, 3)
    full_shape = (NV, ORDER)
    position = jnp.arange(ORDER, dtype=jnp.float32) / ORDER
    row_trend = jnp.exp(1.0986123 * (position - 0.5))[None, :]
    row_scale = jnp.exp(jax.random.uniform(subkeys[1], (1, ORDER), jnp.float32, -1.1512925, 1.1512925))
    col_scale = jnp.exp(jax.random.uniform(subkeys[2], (NV, 1), jnp.float32, -1.1512925, 1.1512925))
    base_draw = jnp.clip(jax.random.normal(subkeys[0], full_shape, jnp.float32), -4.0, 4.0)
    return jnp.clip(2.0 / NB * base_draw * row_trend * row_scale * col_scale, -4.0, 4.0)


def setup_inputs(seed: int = 0, part: int = 0) -> dict:
    streams_of = jax.random.split(jax.random.key(seed), 6)
    own_keys = jax.random.split(jax.random.fold_in(streams_of[5], part), 6)
    return {
        "subspace": draw_subspace(jax.random.fold_in(jax.random.fold_in(streams_of[5], part), 71), part),
        "s_inv": draw_s_inv(jax.random.fold_in(jax.random.fold_in(streams_of[5], part), 71), part),
        "couple": draw_couple(jax.random.fold_in(jax.random.fold_in(streams_of[5], part), 71), part),
        "diag_blocks": draw_diag_blocks(jax.random.fold_in(jax.random.fold_in(streams_of[5], part), 71), part),
        "weights": jnp.clip(jax.random.uniform(own_keys[4], (QUAD, 2), jnp.float32, -1.0, 1.0), -1.0, 1.0),
    }


highest = lax.Precision.HIGHEST


def inverse_apply(pivot_inv, vecs):
    real_part = jnp.einsum("qnk,qjk->qnj", vecs[:, 0], pivot_inv[:, 0], precision=highest) - jnp.einsum("qnk,qjk->qnj", vecs[:, 1], pivot_inv[:, 1], precision=highest)
    imag_part = jnp.einsum("qnk,qjk->qnj", vecs[:, 0], pivot_inv[:, 1], precision=highest) + jnp.einsum("qnk,qjk->qnj", vecs[:, 1], pivot_inv[:, 0], precision=highest)
    return jnp.stack([real_part, imag_part], axis=1)


def couple_down(coupling_blk, vecs):
    return jnp.einsum("qcnk,kj->qcnj", vecs, coupling_blk, precision=highest)


def couple_up(coupling_blk, vecs):
    return jnp.einsum("qcnk,jk->qcnj", vecs, coupling_blk, precision=highest)


def reference(subspace, s_inv, couple, diag_blocks, weights):
    points = s_inv.shape[0]
    blocks_all = couple.shape[0]
    block_width = couple.shape[1]
    vectors = subspace.shape[0]
    source = subspace.reshape(vectors, blocks_all, block_width).transpose(1, 0, 2)
    pivots = jnp.moveaxis(s_inv, 1, 0)
    zero_state = jnp.zeros((points, 2, vectors, block_width), jnp.float32)

    def forward(carried, scanned):
        pivot_inv, coupling_blk, rhs_block = scanned
        combined = carried.at[:, 0].add(rhs_block[None])
        solved = inverse_apply(pivot_inv, combined)
        return couple_down(coupling_blk, solved), solved

    _, solved_all = lax.scan(forward, zero_state, (pivots, couple, source))

    def backward(carried, scanned):
        pivot_inv, coupling_blk, known = scanned
        updated = known + inverse_apply(pivot_inv, couple_up(coupling_blk, carried))
        return updated, updated

    _, result = lax.scan(backward, zero_state, (pivots, couple, solved_all), reverse=True)
    signed = weights * jnp.array([1.0, -1.0], jnp.float32)
    filtered_blocks = jnp.einsum("rqcnk,qc->rnk", result, signed, precision=highest)
    diag_term = jnp.einsum("rnk,rjk->rnj", filtered_blocks, diag_blocks, precision=highest)
    upper_rows = jnp.concatenate([filtered_blocks[1:], jnp.zeros_like(filtered_blocks[:1])], axis=0)
    term_up = jnp.einsum("rnk,rjk->rnj", upper_rows, couple, precision=highest)
    down_all = jnp.einsum("rnk,rkj->rnj", filtered_blocks, couple, precision=highest)
    lower_rows = jnp.concatenate([jnp.zeros_like(down_all[:1]), down_all[:-1]], axis=0)
    applied_blocks = diag_term + term_up + lower_rows
    gram_plain = jnp.einsum("rnk,rmk->nm", filtered_blocks, filtered_blocks, precision=highest)
    gram_matrix = jnp.einsum("rnk,rmk->nm", filtered_blocks, applied_blocks, precision=highest)
    order_total = blocks_all * block_width
    grams = jnp.stack([gram_plain, gram_matrix]) / order_total
    filtered = filtered_blocks.transpose(1, 0, 2).reshape(vectors, order_total)
    applied = applied_blocks.transpose(1, 0, 2).reshape(vectors, order_total)
    return filtered, applied, grams
```

```python
import jax
import jax.numpy as jnp
from jax import lax
from jax.sharding import PartitionSpec as P

highest = lax.Precision.HIGHEST


def passed_along(shard, axis, by):
    peers = lax.axis_size(axis)
    pairs = [(i, i + by) for i in range(peers) if 0 <= i + by < peers]
    return lax.ppermute(shard, axis, pairs)


def chain_sum(value, axis):
    peers = lax.axis_size(axis)
    if peers & (peers - 1):
        return lax.psum(value, axis)
    stride = 1
    while stride < peers:
        value = value + lax.ppermute(value, axis, [(i, i ^ stride) for i in range(peers)])
        stride *= 2
    return value


def inverse_apply(pivot_inv, vecs):
    real_part = jnp.einsum(
        "qnk,qjk->qnj", vecs[:, 0], pivot_inv[:, 0], precision=highest
    ) - jnp.einsum("qnk,qjk->qnj", vecs[:, 1], pivot_inv[:, 1], precision=highest)
    imag_part = jnp.einsum(
        "qnk,qjk->qnj", vecs[:, 0], pivot_inv[:, 1], precision=highest
    ) + jnp.einsum("qnk,qjk->qnj", vecs[:, 1], pivot_inv[:, 0], precision=highest)
    return jnp.stack([real_part, imag_part], axis=1)


def couple_down(coupling_blk, vecs):
    return jnp.einsum("qcnk,kj->qcnj", vecs, coupling_blk, precision=highest)


def couple_up(coupling_blk, vecs):
    return jnp.einsum("qcnk,jk->qcnj", vecs, coupling_blk, precision=highest)


def sweep_forward(pivots, couple, start_rows, source, rhs_rows, store_all):
    blocks_dev = couple.shape[0]

    def advance(carried, position):
        pivot_inv = lax.dynamic_index_in_dim(pivots, position, 1, keepdims=False)
        coupling_blk = lax.dynamic_index_in_dim(couple, position, 0, keepdims=False)
        combined = carried
        if source is not None:
            rhs_block = lax.dynamic_index_in_dim(source, position, 0, keepdims=False)
            combined = combined.at[:, 0, rhs_rows:].add(rhs_block[None])
        solved = inverse_apply(pivot_inv, combined)
        return (couple_down(coupling_blk, solved), solved if store_all else None)

    return lax.scan(advance, start_rows, jnp.arange(blocks_dev))


def sweep_backward(pivots, couple, start_rows, solved_all, rhs_rows, store_all):
    blocks_dev = couple.shape[0]

    def retreat(carried, position):
        pivot_inv = lax.dynamic_index_in_dim(pivots, position, 1, keepdims=False)
        coupling_blk = lax.dynamic_index_in_dim(couple, position, 0, keepdims=False)
        correction = inverse_apply(pivot_inv, couple_up(coupling_blk, carried))
        if solved_all is not None:
            known = lax.dynamic_index_in_dim(solved_all, position, 0, keepdims=False)
            correction = correction.at[:, :, rhs_rows:].add(known)
        return (correction, correction if store_all else None)

    return lax.scan(retreat, start_rows, jnp.arange(blocks_dev), reverse=True)


def block_real(matrix):
    top = jnp.concatenate([matrix[:, 0], matrix[:, 1]], axis=2)
    bottom = jnp.concatenate([-matrix[:, 1], matrix[:, 0]], axis=2)
    return jnp.concatenate([top, bottom], axis=1)


def flat_rows(vecs):
    return jnp.concatenate([vecs[:, 0], vecs[:, 1]], axis=2)


def unflat_rows(flat, width):
    return jnp.stack([flat[..., :width], flat[..., width:]], axis=1)


def pipelined_chain(maps, tips, by):
    points = tips.shape[0]
    peers = lax.axis_size("chain")
    rank = lax.axis_index("chain")
    depth = rank if by > 0 else peers - 1 - rank

    def step(stage, inbox):
        point = jnp.clip(stage - depth, 0, points - 1)
        rows = lax.dynamic_index_in_dim(inbox, point, 0, keepdims=False)
        out = jnp.dot(
            rows, lax.dynamic_index_in_dim(maps, point, 0, keepdims=False), precision=highest
        ) + lax.dynamic_index_in_dim(tips, point, 0, keepdims=False)
        got = passed_along(out, "chain", by)
        slot = stage + 1 - depth
        keep = (slot >= 0) & (slot < points)
        slot = jnp.clip(slot, 0, points - 1)
        current = lax.dynamic_index_in_dim(inbox, slot, 0, keepdims=False)
        return lax.dynamic_update_index_in_dim(inbox, jnp.where(keep, got, current), slot, 0)

    return lax.fori_loop(0, peers + points - 2, step, jnp.zeros_like(tips))


def shards(subspace, s_inv, couple, diag_blocks, weights):
    points = s_inv.shape[0]
    blocks_dev = couple.shape[0]
    block_width = couple.shape[1]
    vectors = subspace.shape[0]
    source = subspace.reshape(vectors, blocks_dev, block_width).transpose(1, 0, 2)
    zero_rows = jnp.zeros((points, 2, vectors, block_width), jnp.float32)
    plain_eye = jnp.stack(
        [
            jnp.eye(block_width, dtype=jnp.float32),
            jnp.zeros((block_width, block_width), jnp.float32),
        ]
    )
    identity_map = jnp.broadcast_to(plain_eye, (points, 2, block_width, block_width))
    chain_size = lax.axis_size("chain")

    forward_start = jnp.concatenate([identity_map, zero_rows], axis=2)
    forward_both, _ = sweep_forward(s_inv, couple, forward_start, source, block_width, False)
    forward_map = forward_both[:, :, :block_width]
    forward_tip = forward_both[:, :, block_width:]
    incoming = unflat_rows(
        pipelined_chain(block_real(forward_map), flat_rows(forward_tip), 1), block_width
    )
    _, solved_all = sweep_forward(s_inv, couple, incoming, source, 0, True)

    backward_map, _ = sweep_backward(s_inv, couple, identity_map, None, 0, False)
    backward_tip, _ = sweep_backward(s_inv, couple, zero_rows, solved_all, 0, False)
    outgoing = unflat_rows(
        pipelined_chain(block_real(backward_map), flat_rows(backward_tip), -1), block_width
    )
    _, result = sweep_backward(s_inv, couple, outgoing, solved_all, 0, True)

    signed = weights * jnp.array([1.0, -1.0], jnp.float32)
    filtered_blocks = jnp.einsum("rqcnk,qc->rnk", result, signed, precision=highest)
    down_all = jnp.einsum("rnk,rkj->rnj", filtered_blocks, couple, precision=highest)
    from_next = passed_along(filtered_blocks[0], "chain", -1)
    from_prior = passed_along(down_all[-1], "chain", 1)
    diag_term = jnp.einsum("rnk,rjk->rnj", filtered_blocks, diag_blocks, precision=highest)
    upper_rows = jnp.concatenate([filtered_blocks[1:], from_next[None]], axis=0)
    term_up = jnp.einsum("rnk,rjk->rnj", upper_rows, couple, precision=highest)
    lower_rows = jnp.concatenate([from_prior[None], down_all[:-1]], axis=0)
    applied_blocks = diag_term + term_up + lower_rows
    gram_plain = jnp.einsum("rnk,rmk->nm", filtered_blocks, filtered_blocks, precision=highest)
    gram_matrix = jnp.einsum("rnk,rmk->nm", filtered_blocks, applied_blocks, precision=highest)
    summed = chain_sum(jnp.stack([gram_plain, gram_matrix]), "chain")
    grams = summed / (blocks_dev * block_width * chain_size)
    filtered = filtered_blocks.transpose(1, 0, 2).reshape(vectors, blocks_dev * block_width)
    applied = applied_blocks.transpose(1, 0, 2).reshape(vectors, blocks_dev * block_width)
    return (filtered, applied, grams)


def solution(mesh):
    placed = (
        P("parts", "chain"),
        P("parts", "chain", None, None, None),
        P("chain", "parts", None),
        P("chain", "parts", None),
        P("parts", None),
    )
    return jax.shard_map(
        shards,
        mesh=mesh,
        in_specs=placed,
        out_specs=(P("parts", "chain"), P("parts", "chain"), P(None, "parts", None)),
        check_vma=False,
    )
```

```python
import jax
import jax.numpy as jnp
from jax import lax
from jax.sharding import PartitionSpec as P

highest = lax.Precision.HIGHEST
sweep_precision = lax.Precision.HIGHEST
hop_precision = lax.Precision.HIGHEST


def passed_along(shard, axis, by):
    peers = lax.axis_size(axis)
    pairs = [(i, i + by) for i in range(peers) if 0 <= i + by < peers]
    return lax.ppermute(shard, axis, pairs)


def chain_sum(value, axis):
    peers = lax.axis_size(axis)
    if peers & (peers - 1):
        return lax.psum(value, axis)
    stride = 1
    while stride < peers:
        value = value + lax.ppermute(value, axis, [(i, i ^ stride) for i in range(peers)])
        stride *= 2
    return value


def inverse_apply(pivot_inv, vecs):
    real_part = jnp.einsum(
        "qnk,qjk->qnj", vecs[:, 0], pivot_inv[:, 0], precision=sweep_precision
    ) - jnp.einsum("qnk,qjk->qnj", vecs[:, 1], pivot_inv[:, 1], precision=sweep_precision)
    imag_part = jnp.einsum(
        "qnk,qjk->qnj", vecs[:, 0], pivot_inv[:, 1], precision=sweep_precision
    ) + jnp.einsum("qnk,qjk->qnj", vecs[:, 1], pivot_inv[:, 0], precision=sweep_precision)
    return jnp.stack([real_part, imag_part], axis=1)


def couple_down(coupling_blk, vecs):
    return jnp.einsum("qcnk,kj->qcnj", vecs, coupling_blk, precision=sweep_precision)


def couple_up(coupling_blk, vecs):
    return jnp.einsum("qcnk,jk->qcnj", vecs, coupling_blk, precision=sweep_precision)


def sweep_forward(pivots, couple, start_rows, source, rhs_rows, store_all):
    blocks_dev = couple.shape[0]

    def advance(carried, position):
        pivot_inv = lax.dynamic_index_in_dim(pivots, position, 1, keepdims=False)
        coupling_blk = lax.dynamic_index_in_dim(couple, position, 0, keepdims=False)
        combined = carried
        if source is not None:
            rhs_block = lax.dynamic_index_in_dim(source, position, 0, keepdims=False)
            combined = combined.at[:, 0, rhs_rows:].add(rhs_block[None])
        solved = inverse_apply(pivot_inv, combined)
        return (couple_down(coupling_blk, solved), solved if store_all else None)

    return lax.scan(advance, start_rows, jnp.arange(blocks_dev))


def sweep_backward(pivots, couple, start_rows, solved_all, rhs_rows, store_all):
    blocks_dev = couple.shape[0]

    def retreat(carried, position):
        pivot_inv = lax.dynamic_index_in_dim(pivots, position, 1, keepdims=False)
        coupling_blk = lax.dynamic_index_in_dim(couple, position, 0, keepdims=False)
        correction = inverse_apply(pivot_inv, couple_up(coupling_blk, carried))
        if solved_all is not None:
            known = lax.dynamic_index_in_dim(solved_all, position, 0, keepdims=False)
            correction = correction.at[:, :, rhs_rows:].add(known)
        return (correction, correction if store_all else None)

    return lax.scan(retreat, start_rows, jnp.arange(blocks_dev), reverse=True)


def block_real(matrix):
    top = jnp.concatenate([matrix[:, 0], matrix[:, 1]], axis=2)
    bottom = jnp.concatenate([-matrix[:, 1], matrix[:, 0]], axis=2)
    return jnp.concatenate([top, bottom], axis=1)


def flat_rows(vecs):
    return jnp.concatenate([vecs[:, 0], vecs[:, 1]], axis=2)


def unflat_rows(flat, width):
    return jnp.stack([flat[..., :width], flat[..., width:]], axis=1)


def right_apply(vecs, matrix):
    real_part = jnp.einsum(
        "qnk,qkj->qnj", vecs[:, 0], matrix[:, 0], precision=highest
    ) - jnp.einsum("qnk,qkj->qnj", vecs[:, 1], matrix[:, 1], precision=highest)
    imag_part = jnp.einsum(
        "qnk,qkj->qnj", vecs[:, 0], matrix[:, 1], precision=highest
    ) + jnp.einsum("qnk,qkj->qnj", vecs[:, 1], matrix[:, 0], precision=highest)
    return jnp.stack([real_part, imag_part], axis=1)


def pipelined_chain(maps, tips, pairs, depth, stages):
    points = tips.shape[0]

    def step(stage, inbox):
        point = jnp.clip(stage - depth, 0, points - 1)
        rows = lax.dynamic_index_in_dim(inbox, point, 0, keepdims=False)
        out = jnp.dot(
            rows, lax.dynamic_index_in_dim(maps, point, 0, keepdims=False), precision=hop_precision
        ) + lax.dynamic_index_in_dim(tips, point, 0, keepdims=False)
        got = lax.ppermute(out, "chain", pairs)
        slot = stage + 1 - depth
        keep = (slot >= 0) & (slot < points)
        slot = jnp.clip(slot, 0, points - 1)
        current = lax.dynamic_index_in_dim(inbox, slot, 0, keepdims=False)
        return lax.dynamic_update_index_in_dim(inbox, jnp.where(keep, got, current), slot, 0)

    return lax.fori_loop(0, stages, step, jnp.zeros_like(tips))


def chain_incoming(own_map, own_tip, by):
    points = own_tip.shape[0]
    width = own_tip.shape[-1]
    peers = lax.axis_size("chain")
    rank = lax.axis_index("chain")
    if peers % 2:
        depth = rank if by > 0 else peers - 1 - rank
        pairs = [(i, i + by) for i in range(peers) if 0 <= i + by < peers]
        inbox = pipelined_chain(
            block_real(own_map), flat_rows(own_tip), pairs, depth, peers + points - 2
        )
        return unflat_rows(inbox, width)
    halves = peers // 2
    lead = 0 if by > 0 else 1
    node = 1 - lead
    to_node = [(2 * j + lead, 2 * j + node) for j in range(halves)]
    to_lead = [(2 * j + node, 2 * j + lead) for j in range(halves)]
    prev_map = lax.ppermute(own_map, "chain", to_node)
    prev_tip = lax.ppermute(own_tip, "chain", to_node)
    pair_map = right_apply(prev_map, own_map)
    pair_tip = right_apply(prev_tip, own_map) + own_tip
    pair_rank = rank // 2
    depth = pair_rank if by > 0 else halves - 1 - pair_rank
    pairs = [
        (2 * j + node, 2 * (j + by) + node) for j in range(halves) if 0 <= j + by < halves
    ]
    inbox = pipelined_chain(
        block_real(pair_map), flat_rows(pair_tip), pairs, depth, halves + points - 2
    )
    node_in = unflat_rows(inbox, width)
    lead_in = lax.ppermute(node_in, "chain", to_lead)
    node_own = right_apply(node_in, prev_map) + prev_tip
    return jnp.where(rank % 2 == node, node_own, lead_in)


def shards(subspace, s_inv, couple, diag_blocks, weights):
    points = s_inv.shape[0]
    blocks_dev = couple.shape[0]
    block_width = couple.shape[1]
    vectors = subspace.shape[0]
    source = subspace.reshape(vectors, blocks_dev, block_width).transpose(1, 0, 2)
    zero_rows = jnp.zeros((points, 2, vectors, block_width), jnp.float32)
    plain_eye = jnp.stack(
        [
            jnp.eye(block_width, dtype=jnp.float32),
            jnp.zeros((block_width, block_width), jnp.float32),
        ]
    )
    identity_map = jnp.broadcast_to(plain_eye, (points, 2, block_width, block_width))
    chain_size = lax.axis_size("chain")

    forward_start = jnp.concatenate([identity_map, zero_rows], axis=2)
    forward_both, _ = sweep_forward(s_inv, couple, forward_start, source, block_width, False)
    forward_map = forward_both[:, :, :block_width]
    forward_tip = forward_both[:, :, block_width:]
    incoming = chain_incoming(forward_map, forward_tip, 1)
    _, solved_all = sweep_forward(s_inv, couple, incoming, source, 0, True)

    backward_map, _ = sweep_backward(s_inv, couple, identity_map, None, 0, False)
    backward_tip, _ = sweep_backward(s_inv, couple, zero_rows, solved_all, 0, False)
    outgoing = chain_incoming(backward_map, backward_tip, -1)
    _, result = sweep_backward(s_inv, couple, outgoing, solved_all, 0, True)

    signed = weights * jnp.array([1.0, -1.0], jnp.float32)
    filtered_blocks = jnp.einsum("rqcnk,qc->rnk", result, signed, precision=highest)
    down_all = jnp.einsum("rnk,rkj->rnj", filtered_blocks, couple, precision=highest)
    from_next = passed_along(filtered_blocks[0], "chain", -1)
    from_prior = passed_along(down_all[-1], "chain", 1)
    diag_term = jnp.einsum("rnk,rjk->rnj", filtered_blocks, diag_blocks, precision=highest)
    upper_rows = jnp.concatenate([filtered_blocks[1:], from_next[None]], axis=0)
    term_up = jnp.einsum("rnk,rjk->rnj", upper_rows, couple, precision=highest)
    lower_rows = jnp.concatenate([from_prior[None], down_all[:-1]], axis=0)
    applied_blocks = diag_term + term_up + lower_rows
    gram_plain = jnp.einsum("rnk,rmk->nm", filtered_blocks, filtered_blocks, precision=highest)
    gram_matrix = jnp.einsum("rnk,rmk->nm", filtered_blocks, applied_blocks, precision=highest)
    summed = chain_sum(jnp.stack([gram_plain, gram_matrix]), "chain")
    grams = summed / (blocks_dev * block_width * chain_size)
    filtered = filtered_blocks.transpose(1, 0, 2).reshape(vectors, blocks_dev * block_width)
    applied = applied_blocks.transpose(1, 0, 2).reshape(vectors, blocks_dev * block_width)
    return (filtered, applied, grams)


def solution(mesh):
    placed = (
        P("parts", "chain"),
        P("parts", "chain", None, None, None),
        P("chain", "parts", None),
        P("chain", "parts", None),
        P("parts", None),
    )
    return jax.shard_map(
        shards,
        mesh=mesh,
        in_specs=placed,
        out_specs=(P("parts", "chain"), P("parts", "chain"), P(None, "parts", None)),
        check_vma=False,
    )
```

```python
import jax
import jax.numpy as jnp
from jax import lax
from jax.sharding import PartitionSpec as P

highest = lax.Precision.HIGHEST
sweep_precision = lax.Precision.HIGHEST
hop_precision = lax.Precision.HIGHEST


def passed_along(shard, axis, by):
    peers = lax.axis_size(axis)
    pairs = [(i, i + by) for i in range(peers) if 0 <= i + by < peers]
    return lax.ppermute(shard, axis, pairs)


def chain_sum(value, axis):
    peers = lax.axis_size(axis)
    if peers & (peers - 1):
        return lax.psum(value, axis)
    stride = 1
    while stride < peers:
        value = value + lax.ppermute(value, axis, [(i, i ^ stride) for i in range(peers)])
        stride *= 2
    return value


def inverse_apply(pivot_inv, vecs):
    real_part = jnp.einsum(
        "qnk,qjk->qnj", vecs[:, 0], pivot_inv[:, 0], precision=sweep_precision
    ) - jnp.einsum("qnk,qjk->qnj", vecs[:, 1], pivot_inv[:, 1], precision=sweep_precision)
    imag_part = jnp.einsum(
        "qnk,qjk->qnj", vecs[:, 0], pivot_inv[:, 1], precision=sweep_precision
    ) + jnp.einsum("qnk,qjk->qnj", vecs[:, 1], pivot_inv[:, 0], precision=sweep_precision)
    return jnp.stack([real_part, imag_part], axis=1)


def couple_down(coupling_blk, vecs):
    return jnp.einsum("qcnk,kj->qcnj", vecs, coupling_blk, precision=sweep_precision)


def couple_up(coupling_blk, vecs):
    return jnp.einsum("qcnk,jk->qcnj", vecs, coupling_blk, precision=sweep_precision)


def sweep_forward(pivots, couple, start_rows, source, rhs_rows, store_all):
    blocks_dev = couple.shape[0]

    def advance(carried, position):
        pivot_inv = lax.dynamic_index_in_dim(pivots, position, 1, keepdims=False)
        coupling_blk = lax.dynamic_index_in_dim(couple, position, 0, keepdims=False)
        combined = carried
        if source is not None:
            rhs_block = lax.dynamic_index_in_dim(source, position, 0, keepdims=False)
            combined = combined.at[:, 0, rhs_rows:].add(rhs_block[None])
        solved = inverse_apply(pivot_inv, combined)
        return (couple_down(coupling_blk, solved), solved if store_all else None)

    return lax.scan(advance, start_rows, jnp.arange(blocks_dev))


def sweep_backward(pivots, couple, start_rows, solved_all, rhs_rows, store_all):
    blocks_dev = couple.shape[0]

    def retreat(carried, position):
        pivot_inv = lax.dynamic_index_in_dim(pivots, position, 1, keepdims=False)
        coupling_blk = lax.dynamic_index_in_dim(couple, position, 0, keepdims=False)
        correction = inverse_apply(pivot_inv, couple_up(coupling_blk, carried))
        if solved_all is not None:
            known = lax.dynamic_index_in_dim(solved_all, position, 0, keepdims=False)
            correction = correction.at[:, :, rhs_rows:].add(known)
        return (correction, correction if store_all else None)

    return lax.scan(retreat, start_rows, jnp.arange(blocks_dev), reverse=True)


def block_real(matrix):
    top = jnp.concatenate([matrix[:, 0], matrix[:, 1]], axis=2)
    bottom = jnp.concatenate([-matrix[:, 1], matrix[:, 0]], axis=2)
    return jnp.concatenate([top, bottom], axis=1)


def flat_rows(vecs):
    return jnp.concatenate([vecs[:, 0], vecs[:, 1]], axis=2)


def unflat_rows(flat, width):
    return jnp.stack([flat[..., :width], flat[..., width:]], axis=1)


def right_apply(vecs, matrix):
    real_part = jnp.einsum(
        "qnk,qkj->qnj", vecs[:, 0], matrix[:, 0], precision=highest
    ) - jnp.einsum("qnk,qkj->qnj", vecs[:, 1], matrix[:, 1], precision=highest)
    imag_part = jnp.einsum(
        "qnk,qkj->qnj", vecs[:, 0], matrix[:, 1], precision=highest
    ) + jnp.einsum("qnk,qkj->qnj", vecs[:, 1], matrix[:, 0], precision=highest)
    return jnp.stack([real_part, imag_part], axis=1)


def right_apply_all(vecs, states):
    real_part = jnp.einsum(
        "qnk,rqkj->rqnj", vecs[:, 0], states[:, :, 0], precision=highest
    ) - jnp.einsum("qnk,rqkj->rqnj", vecs[:, 1], states[:, :, 1], precision=highest)
    imag_part = jnp.einsum(
        "qnk,rqkj->rqnj", vecs[:, 0], states[:, :, 1], precision=highest
    ) + jnp.einsum("qnk,rqkj->rqnj", vecs[:, 1], states[:, :, 0], precision=highest)
    return jnp.stack([real_part, imag_part], axis=2)


def pipelined_chain(maps, tips, pairs, depth, stages):
    points = tips.shape[0]

    def step(stage, inbox):
        point = jnp.clip(stage - depth, 0, points - 1)
        rows = lax.dynamic_index_in_dim(inbox, point, 0, keepdims=False)
        out = jnp.dot(
            rows, lax.dynamic_index_in_dim(maps, point, 0, keepdims=False), precision=hop_precision
        ) + lax.dynamic_index_in_dim(tips, point, 0, keepdims=False)
        got = lax.ppermute(out, "chain", pairs)
        slot = stage + 1 - depth
        keep = (slot >= 0) & (slot < points)
        slot = jnp.clip(slot, 0, points - 1)
        current = lax.dynamic_index_in_dim(inbox, slot, 0, keepdims=False)
        return lax.dynamic_update_index_in_dim(inbox, jnp.where(keep, got, current), slot, 0)

    return lax.fori_loop(0, stages, step, jnp.zeros_like(tips))


def chain_incoming(own_map, own_tip, by):
    points = own_tip.shape[0]
    width = own_tip.shape[-1]
    peers = lax.axis_size("chain")
    rank = lax.axis_index("chain")
    if peers % 2:
        depth = rank if by > 0 else peers - 1 - rank
        pairs = [(i, i + by) for i in range(peers) if 0 <= i + by < peers]
        inbox = pipelined_chain(
            block_real(own_map), flat_rows(own_tip), pairs, depth, peers + points - 2
        )
        return unflat_rows(inbox, width)
    halves = peers // 2
    lead = 0 if by > 0 else 1
    node = 1 - lead
    to_node = [(2 * j + lead, 2 * j + node) for j in range(halves)]
    to_lead = [(2 * j + node, 2 * j + lead) for j in range(halves)]
    prev_map = lax.ppermute(own_map, "chain", to_node)
    prev_tip = lax.ppermute(own_tip, "chain", to_node)
    pair_map = right_apply(prev_map, own_map)
    pair_tip = right_apply(prev_tip, own_map) + own_tip
    pair_rank = rank // 2
    depth = pair_rank if by > 0 else halves - 1 - pair_rank
    pairs = [
        (2 * j + node, 2 * (j + by) + node) for j in range(halves) if 0 <= j + by < halves
    ]
    inbox = pipelined_chain(
        block_real(pair_map), flat_rows(pair_tip), pairs, depth, halves + points - 2
    )
    node_in = unflat_rows(inbox, width)
    lead_in = lax.ppermute(node_in, "chain", to_lead)
    node_own = right_apply(node_in, prev_map) + prev_tip
    return jnp.where(rank % 2 == node, node_own, lead_in)


def shards(subspace, s_inv, couple, diag_blocks, weights):
    points = s_inv.shape[0]
    blocks_dev = couple.shape[0]
    block_width = couple.shape[1]
    vectors = subspace.shape[0]
    source = subspace.reshape(vectors, blocks_dev, block_width).transpose(1, 0, 2)
    zero_rows = jnp.zeros((points, 2, vectors, block_width), jnp.float32)
    plain_eye = jnp.stack(
        [
            jnp.eye(block_width, dtype=jnp.float32),
            jnp.zeros((block_width, block_width), jnp.float32),
        ]
    )
    identity_map = jnp.broadcast_to(plain_eye, (points, 2, block_width, block_width))
    chain_size = lax.axis_size("chain")

    forward_start = jnp.concatenate([identity_map, zero_rows], axis=2)
    forward_both, forward_states = sweep_forward(
        s_inv, couple, forward_start, source, block_width, True
    )
    forward_map = forward_both[:, :, :block_width]
    forward_tip = forward_both[:, :, block_width:]
    incoming = chain_incoming(forward_map, forward_tip, 1)
    solved_all = forward_states[:, :, :, block_width:] + right_apply_all(
        incoming, forward_states[:, :, :, :block_width]
    )

    backward_map, backward_states = sweep_backward(s_inv, couple, identity_map, None, 0, True)
    backward_tip, tip_states = sweep_backward(s_inv, couple, zero_rows, solved_all, 0, True)
    outgoing = chain_incoming(backward_map, backward_tip, -1)
    result = tip_states + right_apply_all(outgoing, backward_states)

    signed = weights * jnp.array([1.0, -1.0], jnp.float32)
    filtered_blocks = jnp.einsum("rqcnk,qc->rnk", result, signed, precision=highest)
    down_all = jnp.einsum("rnk,rkj->rnj", filtered_blocks, couple, precision=highest)
    from_next = passed_along(filtered_blocks[0], "chain", -1)
    from_prior = passed_along(down_all[-1], "chain", 1)
    diag_term = jnp.einsum("rnk,rjk->rnj", filtered_blocks, diag_blocks, precision=highest)
    upper_rows = jnp.concatenate([filtered_blocks[1:], from_next[None]], axis=0)
    term_up = jnp.einsum("rnk,rjk->rnj", upper_rows, couple, precision=highest)
    lower_rows = jnp.concatenate([from_prior[None], down_all[:-1]], axis=0)
    applied_blocks = diag_term + term_up + lower_rows
    gram_plain = jnp.einsum("rnk,rmk->nm", filtered_blocks, filtered_blocks, precision=highest)
    gram_matrix = jnp.einsum("rnk,rmk->nm", filtered_blocks, applied_blocks, precision=highest)
    summed = chain_sum(jnp.stack([gram_plain, gram_matrix]), "chain")
    grams = summed / (blocks_dev * block_width * chain_size)
    filtered = filtered_blocks.transpose(1, 0, 2).reshape(vectors, blocks_dev * block_width)
    applied = applied_blocks.transpose(1, 0, 2).reshape(vectors, blocks_dev * block_width)
    return (filtered, applied, grams)


def solution(mesh):
    placed = (
        P("parts", "chain"),
        P("parts", "chain", None, None, None),
        P("chain", "parts", None),
        P("chain", "parts", None),
        P("parts", None),
    )
    return jax.shard_map(
        shards,
        mesh=mesh,
        in_specs=placed,
        out_specs=(P("parts", "chain"), P("parts", "chain"), P(None, "parts", None)),
        check_vma=False,
    )
```

```python
import jax
import jax.numpy as jnp
from jax import lax
from jax.sharding import PartitionSpec as P

highest = lax.Precision.HIGHEST
sweep_precision = lax.Precision.HIGHEST
hop_precision = lax.Precision.HIGHEST


def passed_along(shard, axis, by):
    peers = lax.axis_size(axis)
    pairs = [(i, i + by) for i in range(peers) if 0 <= i + by < peers]
    return lax.ppermute(shard, axis, pairs)


def chain_sum(value, axis):
    peers = lax.axis_size(axis)
    if peers & (peers - 1):
        return lax.psum(value, axis)
    stride = 1
    while stride < peers:
        value = value + lax.ppermute(value, axis, [(i, i ^ stride) for i in range(peers)])
        stride *= 2
    return value


def inverse_apply(pivot_inv, vecs):
    real_part = jnp.einsum(
        "qnk,qjk->qnj", vecs[:, 0], pivot_inv[:, 0], precision=sweep_precision
    ) - jnp.einsum("qnk,qjk->qnj", vecs[:, 1], pivot_inv[:, 1], precision=sweep_precision)
    imag_part = jnp.einsum(
        "qnk,qjk->qnj", vecs[:, 0], pivot_inv[:, 1], precision=sweep_precision
    ) + jnp.einsum("qnk,qjk->qnj", vecs[:, 1], pivot_inv[:, 0], precision=sweep_precision)
    return jnp.stack([real_part, imag_part], axis=1)


def couple_down(coupling_blk, vecs):
    return jnp.einsum("qcnk,kj->qcnj", vecs, coupling_blk, precision=sweep_precision)


def couple_up(coupling_blk, vecs):
    return jnp.einsum("qcnk,jk->qcnj", vecs, coupling_blk, precision=sweep_precision)


def sweep_forward(pivots, couple, start_rows, source, rhs_rows, store_all):
    blocks_dev = couple.shape[0]

    def advance(carried, position):
        pivot_inv = lax.dynamic_index_in_dim(pivots, position, 1, keepdims=False)
        coupling_blk = lax.dynamic_index_in_dim(couple, position, 0, keepdims=False)
        combined = carried
        if source is not None:
            rhs_block = lax.dynamic_index_in_dim(source, position, 0, keepdims=False)
            combined = combined.at[:, 0, rhs_rows:].add(rhs_block[None])
        solved = inverse_apply(pivot_inv, combined)
        return (couple_down(coupling_blk, solved), solved if store_all else None)

    return lax.scan(advance, start_rows, jnp.arange(blocks_dev))


def sweep_backward(pivots, couple, start_rows, solved_all, rhs_rows, store_all):
    blocks_dev = couple.shape[0]

    def retreat(carried, position):
        pivot_inv = lax.dynamic_index_in_dim(pivots, position, 1, keepdims=False)
        coupling_blk = lax.dynamic_index_in_dim(couple, position, 0, keepdims=False)
        correction = inverse_apply(pivot_inv, couple_up(coupling_blk, carried))
        if solved_all is not None:
            known = lax.dynamic_index_in_dim(solved_all, position, 0, keepdims=False)
            correction = correction.at[:, :, rhs_rows:].add(known)
        return (correction, correction if store_all else None)

    return lax.scan(retreat, start_rows, jnp.arange(blocks_dev), reverse=True)


def block_real(matrix):
    top = jnp.concatenate([matrix[:, 0], matrix[:, 1]], axis=2)
    bottom = jnp.concatenate([-matrix[:, 1], matrix[:, 0]], axis=2)
    return jnp.concatenate([top, bottom], axis=1)


def flat_rows(vecs):
    return jnp.concatenate([vecs[:, 0], vecs[:, 1]], axis=2)


def unflat_rows(flat, width):
    return jnp.stack([flat[..., :width], flat[..., width:]], axis=1)


def right_apply(vecs, matrix):
    real_part = jnp.einsum(
        "qnk,qkj->qnj", vecs[:, 0], matrix[:, 0], precision=highest
    ) - jnp.einsum("qnk,qkj->qnj", vecs[:, 1], matrix[:, 1], precision=highest)
    imag_part = jnp.einsum(
        "qnk,qkj->qnj", vecs[:, 0], matrix[:, 1], precision=highest
    ) + jnp.einsum("qnk,qkj->qnj", vecs[:, 1], matrix[:, 0], precision=highest)
    return jnp.stack([real_part, imag_part], axis=1)


def right_apply_all(vecs, states):
    real_part = jnp.einsum(
        "qnk,rqkj->rqnj", vecs[:, 0], states[:, :, 0], precision=highest
    ) - jnp.einsum("qnk,rqkj->rqnj", vecs[:, 1], states[:, :, 1], precision=highest)
    imag_part = jnp.einsum(
        "qnk,rqkj->rqnj", vecs[:, 0], states[:, :, 1], precision=highest
    ) + jnp.einsum("qnk,rqkj->rqnj", vecs[:, 1], states[:, :, 0], precision=highest)
    return jnp.stack([real_part, imag_part], axis=2)


def pipelined_chain(maps, tips, pairs, depth, stages):
    points = tips.shape[0]

    def step(stage, inbox):
        point = jnp.clip(stage - depth, 0, points - 1)
        rows = lax.dynamic_index_in_dim(inbox, point, 0, keepdims=False)
        out = jnp.dot(
            rows, lax.dynamic_index_in_dim(maps, point, 0, keepdims=False), precision=hop_precision
        ) + lax.dynamic_index_in_dim(tips, point, 0, keepdims=False)
        got = lax.ppermute(out, "chain", pairs)
        slot = stage + 1 - depth
        keep = (slot >= 0) & (slot < points)
        slot = jnp.clip(slot, 0, points - 1)
        current = lax.dynamic_index_in_dim(inbox, slot, 0, keepdims=False)
        return lax.dynamic_update_index_in_dim(inbox, jnp.where(keep, got, current), slot, 0)

    return lax.fori_loop(0, stages, step, jnp.zeros_like(tips))


def chain_incoming(own_both, width, by):
    own_map = own_both[:, :, :width]
    own_tip = own_both[:, :, width:]
    points = own_tip.shape[0]
    peers = lax.axis_size("chain")
    rank = lax.axis_index("chain")
    if peers % 2:
        depth = rank if by > 0 else peers - 1 - rank
        pairs = [(i, i + by) for i in range(peers) if 0 <= i + by < peers]
        inbox = pipelined_chain(
            block_real(own_map), flat_rows(own_tip), pairs, depth, peers + points - 2
        )
        return unflat_rows(inbox, width)
    halves = peers // 2
    lead = 0 if by > 0 else 1
    node = 1 - lead
    to_node = [(2 * j + lead, 2 * j + node) for j in range(halves)]
    to_lead = [(2 * j + node, 2 * j + lead) for j in range(halves)]
    prev_both = lax.ppermute(own_both, "chain", to_node)
    pair_both = right_apply(prev_both, own_map)
    prev_map = prev_both[:, :, :width]
    prev_tip = prev_both[:, :, width:]
    pair_map = pair_both[:, :, :width]
    pair_tip = pair_both[:, :, width:] + own_tip
    pair_rank = rank // 2
    depth = pair_rank if by > 0 else halves - 1 - pair_rank
    pairs = [
        (2 * j + node, 2 * (j + by) + node) for j in range(halves) if 0 <= j + by < halves
    ]
    inbox = pipelined_chain(
        block_real(pair_map), flat_rows(pair_tip), pairs, depth, halves + points - 2
    )
    node_in = unflat_rows(inbox, width)
    lead_in = lax.ppermute(node_in, "chain", to_lead)
    node_own = right_apply(node_in, prev_map) + prev_tip
    return jnp.where(rank % 2 == node, node_own, lead_in)


def shards(subspace, s_inv, couple, diag_blocks, weights):
    points = s_inv.shape[0]
    blocks_dev = couple.shape[0]
    block_width = couple.shape[1]
    vectors = subspace.shape[0]
    source = subspace.reshape(vectors, blocks_dev, block_width).transpose(1, 0, 2)
    zero_rows = jnp.zeros((points, 2, vectors, block_width), jnp.float32)
    plain_eye = jnp.stack(
        [
            jnp.eye(block_width, dtype=jnp.float32),
            jnp.zeros((block_width, block_width), jnp.float32),
        ]
    )
    identity_map = jnp.broadcast_to(plain_eye, (points, 2, block_width, block_width))
    chain_size = lax.axis_size("chain")

    forward_start = jnp.concatenate([identity_map, zero_rows], axis=2)
    forward_both, forward_states = sweep_forward(
        s_inv, couple, forward_start, source, block_width, True
    )
    incoming = chain_incoming(forward_both, block_width, 1)
    solved_all = forward_states[:, :, :, block_width:] + right_apply_all(
        incoming, forward_states[:, :, :, :block_width]
    )

    backward_start = jnp.concatenate([identity_map, zero_rows], axis=2)
    backward_both, backward_all = sweep_backward(
        s_inv, couple, backward_start, solved_all, block_width, True
    )
    outgoing = chain_incoming(backward_both, block_width, -1)
    result = backward_all[:, :, :, block_width:] + right_apply_all(
        outgoing, backward_all[:, :, :, :block_width]
    )

    signed = weights * jnp.array([1.0, -1.0], jnp.float32)
    filtered_blocks = jnp.einsum("rqcnk,qc->rnk", result, signed, precision=highest)
    down_all = jnp.einsum("rnk,rkj->rnj", filtered_blocks, couple, precision=highest)
    from_next = passed_along(filtered_blocks[0], "chain", -1)
    from_prior = passed_along(down_all[-1], "chain", 1)
    diag_term = jnp.einsum("rnk,rjk->rnj", filtered_blocks, diag_blocks, precision=highest)
    upper_rows = jnp.concatenate([filtered_blocks[1:], from_next[None]], axis=0)
    term_up = jnp.einsum("rnk,rjk->rnj", upper_rows, couple, precision=highest)
    lower_rows = jnp.concatenate([from_prior[None], down_all[:-1]], axis=0)
    applied_blocks = diag_term + term_up + lower_rows
    gram_plain = jnp.einsum("rnk,rmk->nm", filtered_blocks, filtered_blocks, precision=highest)
    gram_matrix = jnp.einsum("rnk,rmk->nm", filtered_blocks, applied_blocks, precision=highest)
    summed = chain_sum(jnp.stack([gram_plain, gram_matrix]), "chain")
    grams = summed / (blocks_dev * block_width * chain_size)
    filtered = filtered_blocks.transpose(1, 0, 2).reshape(vectors, blocks_dev * block_width)
    applied = applied_blocks.transpose(1, 0, 2).reshape(vectors, blocks_dev * block_width)
    return (filtered, applied, grams)


def solution(mesh):
    placed = (
        P("parts", "chain"),
        P("parts", "chain", None, None, None),
        P("chain", "parts", None),
        P("chain", "parts", None),
        P("parts", None),
    )
    return jax.shard_map(
        shards,
        mesh=mesh,
        in_specs=placed,
        out_specs=(P("parts", "chain"), P("parts", "chain"), P(None, "parts", None)),
        check_vma=False,
    )
```

```python
import jax
import jax.numpy as jnp
from jax import lax
from jax.sharding import PartitionSpec as P

highest = lax.Precision.HIGHEST
sweep_precision = lax.Precision.HIGHEST
hop_precision = lax.Precision.HIGHEST


def passed_along(shard, axis, by):
    peers = lax.axis_size(axis)
    pairs = [(i, i + by) for i in range(peers) if 0 <= i + by < peers]
    return lax.ppermute(shard, axis, pairs)


def chain_sum(value, axis):
    peers = lax.axis_size(axis)
    if peers & (peers - 1):
        return lax.psum(value, axis)
    stride = 1
    while stride < peers:
        value = value + lax.ppermute(value, axis, [(i, i ^ stride) for i in range(peers)])
        stride *= 2
    return value


def inverse_apply(pivot_inv, vecs):
    real_part = jnp.einsum(
        "qnk,qjk->qnj", vecs[:, 0], pivot_inv[:, 0], precision=sweep_precision
    ) - jnp.einsum("qnk,qjk->qnj", vecs[:, 1], pivot_inv[:, 1], precision=sweep_precision)
    imag_part = jnp.einsum(
        "qnk,qjk->qnj", vecs[:, 0], pivot_inv[:, 1], precision=sweep_precision
    ) + jnp.einsum("qnk,qjk->qnj", vecs[:, 1], pivot_inv[:, 0], precision=sweep_precision)
    return jnp.stack([real_part, imag_part], axis=1)


def couple_down(coupling_blk, vecs):
    return jnp.einsum("qcnk,kj->qcnj", vecs, coupling_blk, precision=sweep_precision)


def couple_up(coupling_blk, vecs):
    return jnp.einsum("qcnk,jk->qcnj", vecs, coupling_blk, precision=sweep_precision)


def sweep_forward(pivots, couple, start_rows, source, rhs_rows, store_all):
    blocks_dev = couple.shape[0]

    def advance(carried, position):
        pivot_inv = lax.dynamic_index_in_dim(pivots, position, 1, keepdims=False)
        coupling_blk = lax.dynamic_index_in_dim(couple, position, 0, keepdims=False)
        combined = carried
        if source is not None:
            combined = combined + lax.dynamic_index_in_dim(source, position, 0, keepdims=False)
        solved = inverse_apply(pivot_inv, combined)
        return (couple_down(coupling_blk, solved), solved if store_all else None)

    return lax.scan(advance, start_rows, jnp.arange(blocks_dev))


def sweep_backward(pivots, couple, start_rows, solved_all, rhs_rows, store_all):
    blocks_dev = couple.shape[0]

    def retreat(carried, position):
        pivot_inv = lax.dynamic_index_in_dim(pivots, position, 1, keepdims=False)
        coupling_blk = lax.dynamic_index_in_dim(couple, position, 0, keepdims=False)
        correction = inverse_apply(pivot_inv, couple_up(coupling_blk, carried))
        if solved_all is not None:
            known = lax.dynamic_index_in_dim(solved_all, position, 0, keepdims=False)
            correction = correction.at[:, :, rhs_rows:].add(known)
        return (correction, correction if store_all else None)

    return lax.scan(retreat, start_rows, jnp.arange(blocks_dev), reverse=True)


def block_real(matrix):
    top = jnp.concatenate([matrix[:, 0], matrix[:, 1]], axis=2)
    bottom = jnp.concatenate([-matrix[:, 1], matrix[:, 0]], axis=2)
    return jnp.concatenate([top, bottom], axis=1)


def flat_rows(vecs):
    return jnp.concatenate([vecs[:, 0], vecs[:, 1]], axis=2)


def unflat_rows(flat, width):
    return jnp.stack([flat[..., :width], flat[..., width:]], axis=1)


def right_apply(vecs, matrix):
    real_part = jnp.einsum(
        "qnk,qkj->qnj", vecs[:, 0], matrix[:, 0], precision=highest
    ) - jnp.einsum("qnk,qkj->qnj", vecs[:, 1], matrix[:, 1], precision=highest)
    imag_part = jnp.einsum(
        "qnk,qkj->qnj", vecs[:, 0], matrix[:, 1], precision=highest
    ) + jnp.einsum("qnk,qkj->qnj", vecs[:, 1], matrix[:, 0], precision=highest)
    return jnp.stack([real_part, imag_part], axis=1)


def right_apply_all(vecs, states):
    real_part = jnp.einsum(
        "qnk,rqkj->rqnj", vecs[:, 0], states[:, :, 0], precision=highest
    ) - jnp.einsum("qnk,rqkj->rqnj", vecs[:, 1], states[:, :, 1], precision=highest)
    imag_part = jnp.einsum(
        "qnk,rqkj->rqnj", vecs[:, 0], states[:, :, 1], precision=highest
    ) + jnp.einsum("qnk,rqkj->rqnj", vecs[:, 1], states[:, :, 0], precision=highest)
    return jnp.stack([real_part, imag_part], axis=2)


def pipelined_chain(maps, tips, pairs, depth, stages):
    points = tips.shape[0]

    def step(stage, inbox):
        point = jnp.clip(stage - depth, 0, points - 1)
        rows = lax.dynamic_index_in_dim(inbox, point, 0, keepdims=False)
        out = jnp.dot(
            rows, lax.dynamic_index_in_dim(maps, point, 0, keepdims=False), precision=hop_precision
        ) + lax.dynamic_index_in_dim(tips, point, 0, keepdims=False)
        got = lax.ppermute(out, "chain", pairs)
        slot = stage + 1 - depth
        keep = (slot >= 0) & (slot < points)
        slot = jnp.clip(slot, 0, points - 1)
        current = lax.dynamic_index_in_dim(inbox, slot, 0, keepdims=False)
        return lax.dynamic_update_index_in_dim(inbox, jnp.where(keep, got, current), slot, 0)

    return lax.fori_loop(0, stages, step, jnp.zeros_like(tips))


def chain_incoming(own_both, width, by):
    own_map = own_both[:, :, :width]
    own_tip = own_both[:, :, width:]
    points = own_tip.shape[0]
    peers = lax.axis_size("chain")
    rank = lax.axis_index("chain")
    if peers % 2:
        depth = rank if by > 0 else peers - 1 - rank
        pairs = [(i, i + by) for i in range(peers) if 0 <= i + by < peers]
        inbox = pipelined_chain(
            block_real(own_map), flat_rows(own_tip), pairs, depth, peers + points - 2
        )
        return unflat_rows(inbox, width)
    halves = peers // 2
    lead = 0 if by > 0 else 1
    node = 1 - lead
    to_node = [(2 * j + lead, 2 * j + node) for j in range(halves)]
    to_lead = [(2 * j + node, 2 * j + lead) for j in range(halves)]
    prev_both = lax.ppermute(own_both, "chain", to_node)
    pair_both = right_apply(prev_both, own_map)
    prev_map = prev_both[:, :, :width]
    prev_tip = prev_both[:, :, width:]
    pair_map = pair_both[:, :, :width]
    pair_tip = pair_both[:, :, width:] + own_tip
    pair_rank = rank // 2
    depth = pair_rank if by > 0 else halves - 1 - pair_rank
    pairs = [
        (2 * j + node, 2 * (j + by) + node) for j in range(halves) if 0 <= j + by < halves
    ]
    inbox = pipelined_chain(
        block_real(pair_map), flat_rows(pair_tip), pairs, depth, halves + points - 2
    )
    node_in = unflat_rows(inbox, width)
    lead_in = lax.ppermute(node_in, "chain", to_lead)
    node_own = right_apply(node_in, prev_map) + prev_tip
    return jnp.where(rank % 2 == node, node_own, lead_in)


def shards(subspace, s_inv, couple, diag_blocks, weights):
    points = s_inv.shape[0]
    blocks_dev = couple.shape[0]
    block_width = couple.shape[1]
    vectors = subspace.shape[0]
    source = subspace.reshape(vectors, blocks_dev, block_width).transpose(1, 0, 2)
    zero_rows = jnp.zeros((points, 2, vectors, block_width), jnp.float32)
    plain_eye = jnp.stack(
        [
            jnp.eye(block_width, dtype=jnp.float32),
            jnp.zeros((block_width, block_width), jnp.float32),
        ]
    )
    identity_map = jnp.broadcast_to(plain_eye, (points, 2, block_width, block_width))
    chain_size = lax.axis_size("chain")

    forward_start = jnp.concatenate([identity_map, zero_rows], axis=2)
    addend = jnp.zeros((blocks_dev,) + forward_start.shape, jnp.float32)
    addend = addend.at[:, :, 0, block_width:].set(
        jnp.broadcast_to(source[:, None], (blocks_dev, points, vectors, block_width))
    )
    forward_both, forward_states = sweep_forward(
        s_inv, couple, forward_start, addend, block_width, True
    )
    incoming = chain_incoming(forward_both, block_width, 1)
    solved_all = forward_states[:, :, :, block_width:] + right_apply_all(
        incoming, forward_states[:, :, :, :block_width]
    )

    backward_start = jnp.concatenate([identity_map, zero_rows], axis=2)
    backward_both, backward_all = sweep_backward(
        s_inv, couple, backward_start, solved_all, block_width, True
    )
    outgoing = chain_incoming(backward_both, block_width, -1)
    result = backward_all[:, :, :, block_width:] + right_apply_all(
        outgoing, backward_all[:, :, :, :block_width]
    )

    signed = weights * jnp.array([1.0, -1.0], jnp.float32)
    filtered_blocks = jnp.einsum("rqcnk,qc->rnk", result, signed, precision=highest)
    down_all = jnp.einsum("rnk,rkj->rnj", filtered_blocks, couple, precision=highest)
    from_next = passed_along(filtered_blocks[0], "chain", -1)
    from_prior = passed_along(down_all[-1], "chain", 1)
    diag_term = jnp.einsum("rnk,rjk->rnj", filtered_blocks, diag_blocks, precision=highest)
    upper_rows = jnp.concatenate([filtered_blocks[1:], from_next[None]], axis=0)
    term_up = jnp.einsum("rnk,rjk->rnj", upper_rows, couple, precision=highest)
    lower_rows = jnp.concatenate([from_prior[None], down_all[:-1]], axis=0)
    applied_blocks = diag_term + term_up + lower_rows
    gram_plain = jnp.einsum("rnk,rmk->nm", filtered_blocks, filtered_blocks, precision=highest)
    gram_matrix = jnp.einsum("rnk,rmk->nm", filtered_blocks, applied_blocks, precision=highest)
    summed = chain_sum(jnp.stack([gram_plain, gram_matrix]), "chain")
    grams = summed / (blocks_dev * block_width * chain_size)
    filtered = filtered_blocks.transpose(1, 0, 2).reshape(vectors, blocks_dev * block_width)
    applied = applied_blocks.transpose(1, 0, 2).reshape(vectors, blocks_dev * block_width)
    return (filtered, applied, grams)


def solution(mesh):
    placed = (
        P("parts", "chain"),
        P("parts", "chain", None, None, None),
        P("chain", "parts", None),
        P("chain", "parts", None),
        P("parts", None),
    )
    return jax.shard_map(
        shards,
        mesh=mesh,
        in_specs=placed,
        out_specs=(P("parts", "chain"), P("parts", "chain"), P(None, "parts", None)),
        check_vma=False,
    )
```

```python
import jax
import jax.numpy as jnp
from jax import lax
from jax.sharding import PartitionSpec as P

highest = lax.Precision.HIGHEST
sweep_precision = lax.Precision.HIGHEST
hop_precision = lax.Precision.HIGHEST


def passed_along(shard, axis, by):
    peers = lax.axis_size(axis)
    pairs = [(i, i + by) for i in range(peers) if 0 <= i + by < peers]
    return lax.ppermute(shard, axis, pairs)


def chain_sum(value, axis):
    peers = lax.axis_size(axis)
    if peers % 2:
        return lax.psum(value, axis)
    value = value + lax.ppermute(value, axis, [(i, i ^ 1) for i in range(peers)])
    halves = peers // 2
    gathered = [value]
    for shift in range(1, halves):
        gathered.append(
            lax.ppermute(value, axis, [(i, (i + 2 * shift) % peers) for i in range(peers)])
        )
    gathered = jnp.stack(gathered)
    own = lax.axis_index(axis) // 2
    order = (own - jnp.arange(halves)) % halves
    by_pair = jnp.take(gathered, jnp.argsort(order), axis=0)
    total = by_pair[0]
    for pair in range(1, halves):
        total = total + by_pair[pair]
    return total


def inverse_apply(pivot_inv, vecs):
    real_part = jnp.einsum(
        "qnk,qjk->qnj", vecs[:, 0], pivot_inv[:, 0], precision=sweep_precision
    ) - jnp.einsum("qnk,qjk->qnj", vecs[:, 1], pivot_inv[:, 1], precision=sweep_precision)
    imag_part = jnp.einsum(
        "qnk,qjk->qnj", vecs[:, 0], pivot_inv[:, 1], precision=sweep_precision
    ) + jnp.einsum("qnk,qjk->qnj", vecs[:, 1], pivot_inv[:, 0], precision=sweep_precision)
    return jnp.stack([real_part, imag_part], axis=1)


def couple_down(coupling_blk, vecs):
    return jnp.einsum("qcnk,kj->qcnj", vecs, coupling_blk, precision=sweep_precision)


def couple_up(coupling_blk, vecs):
    return jnp.einsum("qcnk,jk->qcnj", vecs, coupling_blk, precision=sweep_precision)


def sweep_forward(pivots, couple, start_rows, source, rhs_rows, store_all):
    blocks_dev = couple.shape[0]

    def advance(carried, position):
        pivot_inv = lax.dynamic_index_in_dim(pivots, position, 1, keepdims=False)
        coupling_blk = lax.dynamic_index_in_dim(couple, position, 0, keepdims=False)
        combined = carried
        if source is not None:
            rhs_block = lax.dynamic_index_in_dim(source, position, 0, keepdims=False)
            rhs_full = jnp.stack([rhs_block, jnp.zeros_like(rhs_block)])
            rhs_full = jnp.broadcast_to(rhs_full[None], (combined.shape[0],) + rhs_full.shape)
            combined = combined.at[:, :, rhs_rows:].add(rhs_full)
        solved = inverse_apply(pivot_inv, combined)
        return (couple_down(coupling_blk, solved), solved if store_all else None)

    return lax.scan(advance, start_rows, jnp.arange(blocks_dev))


def sweep_backward(pivots, couple, start_rows, solved_all, rhs_rows, store_all):
    blocks_dev = couple.shape[0]

    def retreat(carried, position):
        pivot_inv = lax.dynamic_index_in_dim(pivots, position, 1, keepdims=False)
        coupling_blk = lax.dynamic_index_in_dim(couple, position, 0, keepdims=False)
        correction = inverse_apply(pivot_inv, couple_up(coupling_blk, carried))
        if solved_all is not None:
            known = lax.dynamic_index_in_dim(solved_all, position, 0, keepdims=False)
            correction = correction.at[:, :, rhs_rows:].add(known)
        return (correction, correction if store_all else None)

    return lax.scan(retreat, start_rows, jnp.arange(blocks_dev), reverse=True)


def block_real(matrix):
    top = jnp.concatenate([matrix[:, 0], matrix[:, 1]], axis=2)
    bottom = jnp.concatenate([-matrix[:, 1], matrix[:, 0]], axis=2)
    return jnp.concatenate([top, bottom], axis=1)


def flat_rows(vecs):
    return jnp.concatenate([vecs[:, 0], vecs[:, 1]], axis=2)


def unflat_rows(flat, width):
    return jnp.stack([flat[..., :width], flat[..., width:]], axis=1)


def right_apply(vecs, matrix):
    real_part = jnp.einsum(
        "qnk,qkj->qnj", vecs[:, 0], matrix[:, 0], precision=highest
    ) - jnp.einsum("qnk,qkj->qnj", vecs[:, 1], matrix[:, 1], precision=highest)
    imag_part = jnp.einsum(
        "qnk,qkj->qnj", vecs[:, 0], matrix[:, 1], precision=highest
    ) + jnp.einsum("qnk,qkj->qnj", vecs[:, 1], matrix[:, 0], precision=highest)
    return jnp.stack([real_part, imag_part], axis=1)


def right_apply_all(vecs, states):
    real_part = jnp.einsum(
        "qnk,rqkj->rqnj", vecs[:, 0], states[:, :, 0], precision=highest
    ) - jnp.einsum("qnk,rqkj->rqnj", vecs[:, 1], states[:, :, 1], precision=highest)
    imag_part = jnp.einsum(
        "qnk,rqkj->rqnj", vecs[:, 0], states[:, :, 1], precision=highest
    ) + jnp.einsum("qnk,rqkj->rqnj", vecs[:, 1], states[:, :, 0], precision=highest)
    return jnp.stack([real_part, imag_part], axis=2)


def pipelined_chain(maps, tips, pairs, depth, stages):
    points = tips.shape[0]

    def step(stage, inbox):
        point = jnp.clip(stage - depth, 0, points - 1)
        rows = lax.dynamic_index_in_dim(inbox, point, 0, keepdims=False)
        out = jnp.dot(
            rows, lax.dynamic_index_in_dim(maps, point, 0, keepdims=False), precision=hop_precision
        ) + lax.dynamic_index_in_dim(tips, point, 0, keepdims=False)
        got = lax.ppermute(out, "chain", pairs)
        slot = stage + 1 - depth
        keep = (slot >= 0) & (slot < points)
        slot = jnp.clip(slot, 0, points - 1)
        current = lax.dynamic_index_in_dim(inbox, slot, 0, keepdims=False)
        return lax.dynamic_update_index_in_dim(inbox, jnp.where(keep, got, current), slot, 0)

    return lax.fori_loop(0, stages, step, jnp.zeros_like(tips))


def chain_incoming(own_both, width, by):
    own_map = own_both[:, :, :width]
    own_tip = own_both[:, :, width:]
    points = own_tip.shape[0]
    peers = lax.axis_size("chain")
    rank = lax.axis_index("chain")
    if peers % 2:
        depth = rank if by > 0 else peers - 1 - rank
        pairs = [(i, i + by) for i in range(peers) if 0 <= i + by < peers]
        inbox = pipelined_chain(
            block_real(own_map), flat_rows(own_tip), pairs, depth, peers + points - 2
        )
        return unflat_rows(inbox, width)
    halves = peers // 2
    lead = 0 if by > 0 else 1
    node = 1 - lead
    to_node = [(2 * j + lead, 2 * j + node) for j in range(halves)]
    to_lead = [(2 * j + node, 2 * j + lead) for j in range(halves)]
    prev_both = lax.ppermute(own_both, "chain", to_node)
    pair_both = right_apply(prev_both, own_map)
    prev_map = prev_both[:, :, :width]
    prev_tip = prev_both[:, :, width:]
    pair_map = pair_both[:, :, :width]
    pair_tip = pair_both[:, :, width:] + own_tip
    pair_rank = rank // 2
    depth = pair_rank if by > 0 else halves - 1 - pair_rank
    pairs = [
        (2 * j + node, 2 * (j + by) + node) for j in range(halves) if 0 <= j + by < halves
    ]
    inbox = pipelined_chain(
        block_real(pair_map), flat_rows(pair_tip), pairs, depth, halves + points - 2
    )
    node_in = unflat_rows(inbox, width)
    lead_in = lax.ppermute(node_in, "chain", to_lead)
    node_own = right_apply(node_in, prev_map) + prev_tip
    return jnp.where(rank % 2 == node, node_own, lead_in)


def shards(subspace, s_inv, couple, diag_blocks, weights):
    points = s_inv.shape[0]
    blocks_dev = couple.shape[0]
    block_width = couple.shape[1]
    vectors = subspace.shape[0]
    source = subspace.reshape(vectors, blocks_dev, block_width).transpose(1, 0, 2)
    zero_rows = jnp.zeros((points, 2, vectors, block_width), jnp.float32)
    plain_eye = jnp.stack(
        [
            jnp.eye(block_width, dtype=jnp.float32),
            jnp.zeros((block_width, block_width), jnp.float32),
        ]
    )
    identity_map = jnp.broadcast_to(plain_eye, (points, 2, block_width, block_width))
    chain_size = lax.axis_size("chain")

    forward_start = jnp.concatenate([identity_map, zero_rows], axis=2)
    forward_both, forward_states = sweep_forward(
        s_inv, couple, forward_start, source, block_width, True
    )
    incoming = chain_incoming(forward_both, block_width, 1)
    solved_all = forward_states[:, :, :, block_width:] + right_apply_all(
        incoming, forward_states[:, :, :, :block_width]
    )

    backward_start = jnp.concatenate([identity_map, zero_rows], axis=2)
    backward_both, backward_all = sweep_backward(
        s_inv, couple, backward_start, solved_all, block_width, True
    )
    outgoing = chain_incoming(backward_both, block_width, -1)
    result = backward_all[:, :, :, block_width:] + right_apply_all(
        outgoing, backward_all[:, :, :, :block_width]
    )

    signed = weights * jnp.array([1.0, -1.0], jnp.float32)
    filtered_blocks = jnp.einsum("rqcnk,qc->rnk", result, signed, precision=highest)
    down_all = jnp.einsum("rnk,rkj->rnj", filtered_blocks, couple, precision=highest)
    from_next = passed_along(filtered_blocks[0], "chain", -1)
    from_prior = passed_along(down_all[-1], "chain", 1)
    diag_term = jnp.einsum("rnk,rjk->rnj", filtered_blocks, diag_blocks, precision=highest)
    upper_rows = jnp.concatenate([filtered_blocks[1:], from_next[None]], axis=0)
    term_up = jnp.einsum("rnk,rjk->rnj", upper_rows, couple, precision=highest)
    lower_rows = jnp.concatenate([from_prior[None], down_all[:-1]], axis=0)
    applied_blocks = diag_term + term_up + lower_rows
    gram_plain = jnp.einsum("rnk,rmk->nm", filtered_blocks, filtered_blocks, precision=highest)
    gram_matrix = jnp.einsum("rnk,rmk->nm", filtered_blocks, applied_blocks, precision=highest)
    summed = chain_sum(jnp.stack([gram_plain, gram_matrix]), "chain")
    grams = summed / (blocks_dev * block_width * chain_size)
    filtered = filtered_blocks.transpose(1, 0, 2).reshape(vectors, blocks_dev * block_width)
    applied = applied_blocks.transpose(1, 0, 2).reshape(vectors, blocks_dev * block_width)
    return (filtered, applied, grams)


def solution(mesh):
    placed = (
        P("parts", "chain"),
        P("parts", "chain", None, None, None),
        P("chain", "parts", None),
        P("chain", "parts", None),
        P("parts", None),
    )
    return jax.shard_map(
        shards,
        mesh=mesh,
        in_specs=placed,
        out_specs=(P("parts", "chain"), P("parts", "chain"), P(None, "parts", None)),
        check_vma=False,
    )
```

```python
import jax
import jax.numpy as jnp
from jax import lax
from jax.sharding import PartitionSpec as P

highest = lax.Precision.HIGHEST
sweep_precision = lax.Precision.HIGHEST
hop_precision = lax.Precision.HIGHEST


def passed_along(shard, axis, by):
    peers = lax.axis_size(axis)
    pairs = [(i, i + by) for i in range(peers) if 0 <= i + by < peers]
    return lax.ppermute(shard, axis, pairs)


def chain_sum(value, axis):
    peers = lax.axis_size(axis)
    if peers & (peers - 1):
        return lax.psum(value, axis)
    stride = 1
    while stride < peers:
        value = value + lax.ppermute(value, axis, [(i, i ^ stride) for i in range(peers)])
        stride *= 2
    return value


def inverse_apply(pivot_inv, vecs):
    real_part = jnp.einsum(
        "qnk,qjk->qnj", vecs[:, 0], pivot_inv[:, 0], precision=sweep_precision
    ) - jnp.einsum("qnk,qjk->qnj", vecs[:, 1], pivot_inv[:, 1], precision=sweep_precision)
    imag_part = jnp.einsum(
        "qnk,qjk->qnj", vecs[:, 0], pivot_inv[:, 1], precision=sweep_precision
    ) + jnp.einsum("qnk,qjk->qnj", vecs[:, 1], pivot_inv[:, 0], precision=sweep_precision)
    return jnp.stack([real_part, imag_part], axis=1)


def couple_down(coupling_blk, vecs):
    return jnp.einsum("qcnk,kj->qcnj", vecs, coupling_blk, precision=sweep_precision)


def couple_up(coupling_blk, vecs):
    return jnp.einsum("qcnk,jk->qcnj", vecs, coupling_blk, precision=sweep_precision)


def sweep_forward(pivots, couple, start_rows, source, rhs_rows, store_all):
    blocks_dev = couple.shape[0]

    def advance(carried, position):
        pivot_inv = lax.dynamic_index_in_dim(pivots, position, 1, keepdims=False)
        coupling_blk = lax.dynamic_index_in_dim(couple, position, 0, keepdims=False)
        combined = carried
        if source is not None:
            rhs_block = lax.dynamic_index_in_dim(source, position, 0, keepdims=False)
            rhs_full = jnp.stack([rhs_block, jnp.zeros_like(rhs_block)])
            rhs_full = jnp.broadcast_to(rhs_full[None], (combined.shape[0],) + rhs_full.shape)
            combined = combined.at[:, :, rhs_rows:].add(rhs_full)
        solved = inverse_apply(pivot_inv, combined)
        return (couple_down(coupling_blk, solved), solved if store_all else None)

    return lax.scan(advance, start_rows, jnp.arange(blocks_dev))


def sweep_backward(pivots, couple, start_rows, solved_all, rhs_rows, store_all):
    blocks_dev = couple.shape[0]

    def retreat(carried, position):
        pivot_inv = lax.dynamic_index_in_dim(pivots, position, 1, keepdims=False)
        coupling_blk = lax.dynamic_index_in_dim(couple, position, 0, keepdims=False)
        correction = inverse_apply(pivot_inv, couple_up(coupling_blk, carried))
        if solved_all is not None:
            known = lax.dynamic_index_in_dim(solved_all, position, 0, keepdims=False)
            correction = correction.at[:, :, rhs_rows:].add(known)
        return (correction, correction if store_all else None)

    return lax.scan(retreat, start_rows, jnp.arange(blocks_dev), reverse=True)


def block_real(matrix):
    top = jnp.concatenate([matrix[:, 0], matrix[:, 1]], axis=2)
    bottom = jnp.concatenate([-matrix[:, 1], matrix[:, 0]], axis=2)
    return jnp.concatenate([top, bottom], axis=1)


def flat_rows(vecs):
    return jnp.concatenate([vecs[:, 0], vecs[:, 1]], axis=2)


def unflat_rows(flat, width):
    return jnp.stack([flat[..., :width], flat[..., width:]], axis=1)


def right_apply(vecs, matrix):
    real_part = jnp.einsum(
        "qnk,qkj->qnj", vecs[:, 0], matrix[:, 0], precision=highest
    ) - jnp.einsum("qnk,qkj->qnj", vecs[:, 1], matrix[:, 1], precision=highest)
    imag_part = jnp.einsum(
        "qnk,qkj->qnj", vecs[:, 0], matrix[:, 1], precision=highest
    ) + jnp.einsum("qnk,qkj->qnj", vecs[:, 1], matrix[:, 0], precision=highest)
    return jnp.stack([real_part, imag_part], axis=1)


def right_apply_all(vecs, states):
    real_part = jnp.einsum(
        "qnk,rqkj->rqnj", vecs[:, 0], states[:, :, 0], precision=highest
    ) - jnp.einsum("qnk,rqkj->rqnj", vecs[:, 1], states[:, :, 1], precision=highest)
    imag_part = jnp.einsum(
        "qnk,rqkj->rqnj", vecs[:, 0], states[:, :, 1], precision=highest
    ) + jnp.einsum("qnk,rqkj->rqnj", vecs[:, 1], states[:, :, 0], precision=highest)
    return jnp.stack([real_part, imag_part], axis=2)


def pipelined_chain(maps, tips, pairs, depth, stages):
    points = tips.shape[0]

    def step(stage, inbox):
        point = jnp.clip(stage - depth, 0, points - 1)
        rows = lax.dynamic_index_in_dim(inbox, point, 0, keepdims=False)
        out = jnp.dot(
            rows, lax.dynamic_index_in_dim(maps, point, 0, keepdims=False), precision=hop_precision
        ) + lax.dynamic_index_in_dim(tips, point, 0, keepdims=False)
        got = lax.ppermute(out, "chain", pairs)
        slot = stage + 1 - depth
        keep = (slot >= 0) & (slot < points)
        slot = jnp.clip(slot, 0, points - 1)
        current = lax.dynamic_index_in_dim(inbox, slot, 0, keepdims=False)
        return lax.dynamic_update_index_in_dim(inbox, jnp.where(keep, got, current), slot, 0)

    return lax.fori_loop(0, stages, step, jnp.zeros_like(tips))


def chain_incoming(own_both, width, by):
    own_map = own_both[:, :, :width]
    own_tip = own_both[:, :, width:]
    points = own_tip.shape[0]
    peers = lax.axis_size("chain")
    rank = lax.axis_index("chain")
    if peers % 2:
        depth = rank if by > 0 else peers - 1 - rank
        pairs = [(i, i + by) for i in range(peers) if 0 <= i + by < peers]
        inbox = pipelined_chain(
            block_real(own_map), flat_rows(own_tip), pairs, depth, peers + points - 2
        )
        return unflat_rows(inbox, width)
    halves = peers // 2
    lead = 0 if by > 0 else 1
    node = 1 - lead
    to_node = [(2 * j + lead, 2 * j + node) for j in range(halves)]
    to_lead = [(2 * j + node, 2 * j + lead) for j in range(halves)]
    prev_both = lax.ppermute(own_both, "chain", to_node)
    pair_both = right_apply(prev_both, own_map)
    prev_map = prev_both[:, :, :width]
    prev_tip = prev_both[:, :, width:]
    pair_map = pair_both[:, :, :width]
    pair_tip = pair_both[:, :, width:] + own_tip
    pair_rank = rank // 2
    depth = pair_rank if by > 0 else halves - 1 - pair_rank
    pairs = [
        (2 * j + node, 2 * (j + by) + node) for j in range(halves) if 0 <= j + by < halves
    ]
    inbox = pipelined_chain(
        block_real(pair_map), flat_rows(pair_tip), pairs, depth, halves + points - 2
    )
    node_in = unflat_rows(inbox, width)
    lead_in = lax.ppermute(node_in, "chain", to_lead)
    node_own = right_apply(node_in, prev_map) + prev_tip
    return jnp.where(rank % 2 == node, node_own, lead_in)


def shards(subspace, s_inv, couple, diag_blocks, weights):
    points = s_inv.shape[0]
    blocks_dev = couple.shape[0]
    block_width = couple.shape[1]
    vectors = subspace.shape[0]
    source = subspace.reshape(vectors, blocks_dev, block_width).transpose(1, 0, 2)
    zero_rows = jnp.zeros((points, 2, vectors, block_width), jnp.float32)
    plain_eye = jnp.stack(
        [
            jnp.eye(block_width, dtype=jnp.float32),
            jnp.zeros((block_width, block_width), jnp.float32),
        ]
    )
    identity_map = jnp.broadcast_to(plain_eye, (points, 2, block_width, block_width))
    chain_size = lax.axis_size("chain")

    forward_start = jnp.concatenate([identity_map, zero_rows], axis=2)
    forward_both, forward_states = sweep_forward(
        s_inv, couple, forward_start, source, block_width, True
    )
    incoming = chain_incoming(forward_both, block_width, 1)
    solved_all = forward_states[:, :, :, block_width:] + right_apply_all(
        incoming, forward_states[:, :, :, :block_width]
    )

    backward_start = jnp.concatenate([identity_map, zero_rows], axis=2)
    backward_both, backward_all = sweep_backward(
        s_inv, couple, backward_start, solved_all, block_width, True
    )
    outgoing = chain_incoming(backward_both, block_width, -1)
    result = backward_all[:, :, :, block_width:] + right_apply_all(
        outgoing, backward_all[:, :, :, :block_width]
    )

    signed = weights * jnp.array([1.0, -1.0], jnp.float32)
    filtered_blocks = jnp.einsum("rqcnk,qc->rnk", result, signed, precision=highest)
    down_all = jnp.einsum("rnk,rkj->rnj", filtered_blocks, couple, precision=highest)
    from_next = passed_along(filtered_blocks[0], "chain", -1)
    from_prior = passed_along(down_all[-1], "chain", 1)
    diag_term = jnp.einsum("rnk,rjk->rnj", filtered_blocks, diag_blocks, precision=highest)
    upper_rows = jnp.concatenate([filtered_blocks[1:], from_next[None]], axis=0)
    term_up = jnp.einsum("rnk,rjk->rnj", upper_rows, couple, precision=highest)
    lower_rows = jnp.concatenate([from_prior[None], down_all[:-1]], axis=0)
    applied_blocks = diag_term + term_up + lower_rows
    gram_plain = jnp.einsum("rnk,rmk->nm", filtered_blocks, filtered_blocks, precision=highest)
    gram_matrix = jnp.einsum("rnk,rmk->nm", filtered_blocks, applied_blocks, precision=highest)
    summed = chain_sum(jnp.stack([gram_plain, gram_matrix]), "chain")
    grams = summed / (blocks_dev * block_width * chain_size)
    filtered = filtered_blocks.transpose(1, 0, 2).reshape(vectors, blocks_dev * block_width)
    applied = applied_blocks.transpose(1, 0, 2).reshape(vectors, blocks_dev * block_width)
    return (filtered, applied, grams)


def solution(mesh):
    placed = (
        P("parts", "chain"),
        P("parts", "chain", None, None, None),
        P("chain", "parts", None),
        P("chain", "parts", None),
        P("parts", None),
    )
    return jax.shard_map(
        shards,
        mesh=mesh,
        in_specs=placed,
        out_specs=(P("parts", "chain"), P("parts", "chain"), P(None, "parts", None)),
        check_vma=False,
    )
```

```python
import jax
import jax.numpy as jnp
from jax import lax
from jax.sharding import PartitionSpec as P

highest = lax.Precision.HIGHEST
sweep_precision = lax.Precision.HIGHEST
hop_precision = lax.Precision.HIGHEST


def passed_along(shard, axis, by):
    peers = lax.axis_size(axis)
    pairs = [(i, i + by) for i in range(peers) if 0 <= i + by < peers]
    return lax.ppermute(shard, axis, pairs)


def chain_sum(value, axis):
    peers = lax.axis_size(axis)
    if peers & (peers - 1):
        return lax.psum(value, axis)
    stride = 1
    while stride < peers:
        value = value + lax.ppermute(value, axis, [(i, i ^ stride) for i in range(peers)])
        stride *= 2
    return value


def inverse_apply(pivot_inv, vecs):
    real_part = jnp.einsum(
        "qnk,qjk->qnj", vecs[:, 0], pivot_inv[:, 0], precision=sweep_precision
    ) - jnp.einsum("qnk,qjk->qnj", vecs[:, 1], pivot_inv[:, 1], precision=sweep_precision)
    imag_part = jnp.einsum(
        "qnk,qjk->qnj", vecs[:, 0], pivot_inv[:, 1], precision=sweep_precision
    ) + jnp.einsum("qnk,qjk->qnj", vecs[:, 1], pivot_inv[:, 0], precision=sweep_precision)
    return jnp.stack([real_part, imag_part], axis=1)


def couple_down(coupling_blk, vecs):
    return jnp.einsum("qcnk,kj->qcnj", vecs, coupling_blk, precision=sweep_precision)


def couple_up(coupling_blk, vecs):
    return jnp.einsum("qcnk,jk->qcnj", vecs, coupling_blk, precision=sweep_precision)


def sweep_forward(pivots, couple, start_rows, source, rhs_rows, store_all):
    blocks_dev = couple.shape[0]

    def advance(carried, position):
        pivot_inv = lax.dynamic_index_in_dim(pivots, position, 1, keepdims=False)
        coupling_blk = lax.dynamic_index_in_dim(couple, position, 0, keepdims=False)
        combined = carried
        if source is not None:
            rhs_block = lax.dynamic_index_in_dim(source, position, 0, keepdims=False)
            rhs_full = jnp.stack([rhs_block, jnp.zeros_like(rhs_block)])
            rhs_full = jnp.broadcast_to(rhs_full[None], (combined.shape[0],) + rhs_full.shape)
            combined = combined.at[:, :, rhs_rows:].add(rhs_full)
        solved = inverse_apply(pivot_inv, combined)
        return (couple_down(coupling_blk, solved), solved if store_all else None)

    return lax.scan(advance, start_rows, jnp.arange(blocks_dev))


def sweep_backward(pivots, couple, start_rows, solved_all, rhs_rows, store_all):
    blocks_dev = couple.shape[0]

    def retreat(carried, position):
        pivot_inv = lax.dynamic_index_in_dim(pivots, position, 1, keepdims=False)
        coupling_blk = lax.dynamic_index_in_dim(couple, position, 0, keepdims=False)
        correction = inverse_apply(pivot_inv, couple_up(coupling_blk, carried))
        if solved_all is not None:
            known = lax.dynamic_index_in_dim(solved_all, position, 0, keepdims=False)
            correction = correction.at[:, :, rhs_rows:].add(known)
        return (correction, correction if store_all else None)

    return lax.scan(retreat, start_rows, jnp.arange(blocks_dev), reverse=True)


def block_real(matrix):
    top = jnp.concatenate([matrix[:, 0], matrix[:, 1]], axis=2)
    bottom = jnp.concatenate([-matrix[:, 1], matrix[:, 0]], axis=2)
    return jnp.concatenate([top, bottom], axis=1)


def flat_rows(vecs):
    return jnp.concatenate([vecs[:, 0], vecs[:, 1]], axis=2)


def unflat_rows(flat, width):
    return jnp.stack([flat[..., :width], flat[..., width:]], axis=1)


def right_apply(vecs, matrix):
    real_part = jnp.einsum(
        "qnk,qkj->qnj", vecs[:, 0], matrix[:, 0], precision=highest
    ) - jnp.einsum("qnk,qkj->qnj", vecs[:, 1], matrix[:, 1], precision=highest)
    imag_part = jnp.einsum(
        "qnk,qkj->qnj", vecs[:, 0], matrix[:, 1], precision=highest
    ) + jnp.einsum("qnk,qkj->qnj", vecs[:, 1], matrix[:, 0], precision=highest)
    return jnp.stack([real_part, imag_part], axis=1)


def right_apply_all(vecs, states):
    real_part = jnp.einsum(
        "qnk,rqkj->rqnj", vecs[:, 0], states[:, :, 0], precision=highest
    ) - jnp.einsum("qnk,rqkj->rqnj", vecs[:, 1], states[:, :, 1], precision=highest)
    imag_part = jnp.einsum(
        "qnk,rqkj->rqnj", vecs[:, 0], states[:, :, 1], precision=highest
    ) + jnp.einsum("qnk,rqkj->rqnj", vecs[:, 1], states[:, :, 0], precision=highest)
    return jnp.stack([real_part, imag_part], axis=2)


def pipelined_chain(maps, tips, pairs, depth, stages, active=True):
    points = tips.shape[0]

    def step(stage, inbox):
        point = jnp.clip(stage - depth, 0, points - 1)
        rows = lax.dynamic_index_in_dim(inbox, point, 0, keepdims=False)

        def hop():
            return jnp.dot(
                rows,
                lax.dynamic_index_in_dim(maps, point, 0, keepdims=False),
                precision=hop_precision,
            ) + lax.dynamic_index_in_dim(tips, point, 0, keepdims=False)

        out = lax.cond(active, hop, lambda: jnp.zeros_like(rows))
        got = lax.ppermute(out, "chain", pairs)
        slot = stage + 1 - depth
        keep = (slot >= 0) & (slot < points)
        slot = jnp.clip(slot, 0, points - 1)
        current = lax.dynamic_index_in_dim(inbox, slot, 0, keepdims=False)
        return lax.dynamic_update_index_in_dim(inbox, jnp.where(keep, got, current), slot, 0)

    return lax.fori_loop(0, stages, step, jnp.zeros_like(tips))


def chain_incoming(own_both, width, by):
    own_map = own_both[:, :, :width]
    own_tip = own_both[:, :, width:]
    points = own_tip.shape[0]
    peers = lax.axis_size("chain")
    rank = lax.axis_index("chain")
    if peers % 2:
        depth = rank if by > 0 else peers - 1 - rank
        pairs = [(i, i + by) for i in range(peers) if 0 <= i + by < peers]
        inbox = pipelined_chain(
            block_real(own_map), flat_rows(own_tip), pairs, depth, peers + points - 2
        )
        return unflat_rows(inbox, width)
    halves = peers // 2
    lead = 0 if by > 0 else 1
    node = 1 - lead
    to_node = [(2 * j + lead, 2 * j + node) for j in range(halves)]
    to_lead = [(2 * j + node, 2 * j + lead) for j in range(halves)]
    prev_both = lax.ppermute(own_both, "chain", to_node)
    prev_map = prev_both[:, :, :width]
    prev_tip = prev_both[:, :, width:]
    is_node = rank % 2 == node

    def compose():
        pair_both = right_apply(prev_both, own_map)
        pair_tip = pair_both[:, :, width:] + own_tip
        return block_real(pair_both[:, :, :width]), flat_rows(pair_tip)

    def idle():
        return (
            jnp.zeros((points, 2 * width, 2 * width), jnp.float32),
            jnp.zeros(own_tip.shape[:1] + own_tip.shape[2:3] + (2 * width,), jnp.float32),
        )

    pair_maps, pair_tips = lax.cond(is_node, compose, idle)
    pair_rank = rank // 2
    depth = pair_rank if by > 0 else halves - 1 - pair_rank
    pairs = [
        (2 * j + node, 2 * (j + by) + node) for j in range(halves) if 0 <= j + by < halves
    ]
    inbox = pipelined_chain(pair_maps, pair_tips, pairs, depth, halves + points - 2, is_node)
    node_in = unflat_rows(inbox, width)
    lead_in = lax.ppermute(node_in, "chain", to_lead)
    return lax.cond(is_node, lambda: right_apply(node_in, prev_map) + prev_tip, lambda: lead_in)


def shards(subspace, s_inv, couple, diag_blocks, weights):
    points = s_inv.shape[0]
    blocks_dev = couple.shape[0]
    block_width = couple.shape[1]
    vectors = subspace.shape[0]
    source = subspace.reshape(vectors, blocks_dev, block_width).transpose(1, 0, 2)
    zero_rows = jnp.zeros((points, 2, vectors, block_width), jnp.float32)
    plain_eye = jnp.stack(
        [
            jnp.eye(block_width, dtype=jnp.float32),
            jnp.zeros((block_width, block_width), jnp.float32),
        ]
    )
    identity_map = jnp.broadcast_to(plain_eye, (points, 2, block_width, block_width))
    chain_size = lax.axis_size("chain")

    forward_start = jnp.concatenate([identity_map, zero_rows], axis=2)
    forward_both, forward_states = sweep_forward(
        s_inv, couple, forward_start, source, block_width, True
    )
    incoming = chain_incoming(forward_both, block_width, 1)
    solved_all = forward_states[:, :, :, block_width:] + right_apply_all(
        incoming, forward_states[:, :, :, :block_width]
    )

    backward_start = jnp.concatenate([identity_map, zero_rows], axis=2)
    backward_both, backward_all = sweep_backward(
        s_inv, couple, backward_start, solved_all, block_width, True
    )
    outgoing = chain_incoming(backward_both, block_width, -1)
    result = backward_all[:, :, :, block_width:] + right_apply_all(
        outgoing, backward_all[:, :, :, :block_width]
    )

    signed = weights * jnp.array([1.0, -1.0], jnp.float32)
    filtered_blocks = jnp.einsum("rqcnk,qc->rnk", result, signed, precision=highest)
    down_all = jnp.einsum("rnk,rkj->rnj", filtered_blocks, couple, precision=highest)
    from_next = passed_along(filtered_blocks[0], "chain", -1)
    from_prior = passed_along(down_all[-1], "chain", 1)
    diag_term = jnp.einsum("rnk,rjk->rnj", filtered_blocks, diag_blocks, precision=highest)
    upper_rows = jnp.concatenate([filtered_blocks[1:], from_next[None]], axis=0)
    term_up = jnp.einsum("rnk,rjk->rnj", upper_rows, couple, precision=highest)
    lower_rows = jnp.concatenate([from_prior[None], down_all[:-1]], axis=0)
    applied_blocks = diag_term + term_up + lower_rows
    gram_plain = jnp.einsum("rnk,rmk->nm", filtered_blocks, filtered_blocks, precision=highest)
    gram_matrix = jnp.einsum("rnk,rmk->nm", filtered_blocks, applied_blocks, precision=highest)
    summed = chain_sum(jnp.stack([gram_plain, gram_matrix]), "chain")
    grams = summed / (blocks_dev * block_width * chain_size)
    filtered = filtered_blocks.transpose(1, 0, 2).reshape(vectors, blocks_dev * block_width)
    applied = applied_blocks.transpose(1, 0, 2).reshape(vectors, blocks_dev * block_width)
    return (filtered, applied, grams)


def solution(mesh):
    placed = (
        P("parts", "chain"),
        P("parts", "chain", None, None, None),
        P("chain", "parts", None),
        P("chain", "parts", None),
        P("parts", None),
    )
    return jax.shard_map(
        shards,
        mesh=mesh,
        in_specs=placed,
        out_specs=(P("parts", "chain"), P("parts", "chain"), P(None, "parts", None)),
        check_vma=False,
    )
```

```python
import jax
import jax.numpy as jnp
from jax import lax
from jax.sharding import PartitionSpec as P

highest = lax.Precision.HIGHEST
sweep_precision = lax.Precision.HIGHEST
hop_precision = lax.Precision.HIGHEST


def passed_along(shard, axis, by):
    peers = lax.axis_size(axis)
    pairs = [(i, i + by) for i in range(peers) if 0 <= i + by < peers]
    return lax.ppermute(shard, axis, pairs)


def chain_sum(value, axis):
    peers = lax.axis_size(axis)
    if peers & (peers - 1):
        return lax.psum(value, axis)
    stride = 1
    while stride < peers:
        value = value + lax.ppermute(value, axis, [(i, i ^ stride) for i in range(peers)])
        stride *= 2
    return value


def inverse_apply(pivot_inv, vecs):
    real_part = jnp.einsum(
        "qnk,qjk->qnj", vecs[:, 0], pivot_inv[:, 0], precision=sweep_precision
    ) - jnp.einsum("qnk,qjk->qnj", vecs[:, 1], pivot_inv[:, 1], precision=sweep_precision)
    imag_part = jnp.einsum(
        "qnk,qjk->qnj", vecs[:, 0], pivot_inv[:, 1], precision=sweep_precision
    ) + jnp.einsum("qnk,qjk->qnj", vecs[:, 1], pivot_inv[:, 0], precision=sweep_precision)
    return jnp.stack([real_part, imag_part], axis=1)


def couple_down(coupling_blk, vecs):
    return jnp.einsum("qcnk,kj->qcnj", vecs, coupling_blk, precision=sweep_precision)


def couple_up(coupling_blk, vecs):
    return jnp.einsum("qcnk,jk->qcnj", vecs, coupling_blk, precision=sweep_precision)


def sweep_forward(pivots, couple, start_rows, source, rhs_rows, store_all):
    blocks_dev = couple.shape[0]

    def advance(carried, position):
        pivot_inv = lax.dynamic_index_in_dim(pivots, position, 1, keepdims=False)
        coupling_blk = lax.dynamic_index_in_dim(couple, position, 0, keepdims=False)
        combined = carried
        if source is not None:
            rhs_block = lax.dynamic_index_in_dim(source, position, 0, keepdims=False)
            rhs_full = jnp.stack([rhs_block, jnp.zeros_like(rhs_block)])
            rhs_full = jnp.broadcast_to(rhs_full[None], (combined.shape[0],) + rhs_full.shape)
            combined = combined.at[:, :, rhs_rows:].add(rhs_full)
        solved = inverse_apply(pivot_inv, combined)
        return (couple_down(coupling_blk, solved), solved if store_all else None)

    return lax.scan(advance, start_rows, jnp.arange(blocks_dev))


def sweep_backward(pivots, couple, start_rows, solved_all, rhs_rows, store_all):
    blocks_dev = couple.shape[0]

    def retreat(carried, position):
        pivot_inv = lax.dynamic_index_in_dim(pivots, position, 1, keepdims=False)
        coupling_blk = lax.dynamic_index_in_dim(couple, position, 0, keepdims=False)
        correction = inverse_apply(pivot_inv, couple_up(coupling_blk, carried))
        if solved_all is not None:
            known = lax.dynamic_index_in_dim(solved_all, position, 0, keepdims=False)
            correction = correction.at[:, :, rhs_rows:].add(known)
        return (correction, correction if store_all else None)

    return lax.scan(retreat, start_rows, jnp.arange(blocks_dev), reverse=True)


def block_real(matrix):
    top = jnp.concatenate([matrix[:, 0], matrix[:, 1]], axis=2)
    bottom = jnp.concatenate([-matrix[:, 1], matrix[:, 0]], axis=2)
    return jnp.concatenate([top, bottom], axis=1)


def flat_rows(vecs):
    return jnp.concatenate([vecs[:, 0], vecs[:, 1]], axis=2)


def unflat_rows(flat, width):
    return jnp.stack([flat[..., :width], flat[..., width:]], axis=1)


def right_apply(vecs, matrix):
    real_part = jnp.einsum(
        "qnk,qkj->qnj", vecs[:, 0], matrix[:, 0], precision=highest
    ) - jnp.einsum("qnk,qkj->qnj", vecs[:, 1], matrix[:, 1], precision=highest)
    imag_part = jnp.einsum(
        "qnk,qkj->qnj", vecs[:, 0], matrix[:, 1], precision=highest
    ) + jnp.einsum("qnk,qkj->qnj", vecs[:, 1], matrix[:, 0], precision=highest)
    return jnp.stack([real_part, imag_part], axis=1)


def right_apply_all(vecs, states):
    real_part = jnp.einsum(
        "qnk,rqkj->rqnj", vecs[:, 0], states[:, :, 0], precision=highest
    ) - jnp.einsum("qnk,rqkj->rqnj", vecs[:, 1], states[:, :, 1], precision=highest)
    imag_part = jnp.einsum(
        "qnk,rqkj->rqnj", vecs[:, 0], states[:, :, 1], precision=highest
    ) + jnp.einsum("qnk,rqkj->rqnj", vecs[:, 1], states[:, :, 0], precision=highest)
    return jnp.stack([real_part, imag_part], axis=2)


def pipelined_chain(maps, tips, pairs, depth, stages, active=True):
    points = tips.shape[0]

    def step(stage, inbox):
        point = jnp.clip(stage - depth, 0, points - 1)
        rows = lax.dynamic_index_in_dim(inbox, point, 0, keepdims=False)

        def hop():
            return jnp.dot(
                rows,
                lax.dynamic_index_in_dim(maps, point, 0, keepdims=False),
                precision=hop_precision,
            ) + lax.dynamic_index_in_dim(tips, point, 0, keepdims=False)

        out = lax.cond(active, hop, lambda: jnp.zeros_like(rows))
        got = lax.ppermute(out, "chain", pairs)
        slot = stage + 1 - depth
        keep = (slot >= 0) & (slot < points)
        slot = jnp.clip(slot, 0, points - 1)
        current = lax.dynamic_index_in_dim(inbox, slot, 0, keepdims=False)
        return lax.dynamic_update_index_in_dim(inbox, jnp.where(keep, got, current), slot, 0)

    return lax.fori_loop(0, stages, step, jnp.zeros_like(tips))


def chain_incoming(own_both, width, by):
    own_map = own_both[:, :, :width]
    own_tip = own_both[:, :, width:]
    points = own_tip.shape[0]
    peers = lax.axis_size("chain")
    rank = lax.axis_index("chain")
    if peers % 2:
        depth = rank if by > 0 else peers - 1 - rank
        pairs = [(i, i + by) for i in range(peers) if 0 <= i + by < peers]
        inbox = pipelined_chain(
            block_real(own_map), flat_rows(own_tip), pairs, depth, peers + points - 2
        )
        return unflat_rows(inbox, width)
    halves = peers // 2
    lead = 0 if by > 0 else 1
    node = 1 - lead
    to_node = [(2 * j + lead, 2 * j + node) for j in range(halves)]
    to_lead = [(2 * j + node, 2 * j + lead) for j in range(halves)]
    prev_both = lax.ppermute(own_both, "chain", to_node)
    pair_both = right_apply(prev_both, own_map)
    prev_map = prev_both[:, :, :width]
    prev_tip = prev_both[:, :, width:]
    pair_map = pair_both[:, :, :width]
    pair_tip = pair_both[:, :, width:] + own_tip
    pair_rank = rank // 2
    depth = pair_rank if by > 0 else halves - 1 - pair_rank
    pairs = [
        (2 * j + node, 2 * (j + by) + node) for j in range(halves) if 0 <= j + by < halves
    ]
    inbox = pipelined_chain(
        block_real(pair_map),
        flat_rows(pair_tip),
        pairs,
        depth,
        halves + points - 2,
        rank % 2 == node,
    )
    node_in = unflat_rows(inbox, width)
    lead_in = lax.ppermute(node_in, "chain", to_lead)
    node_own = right_apply(node_in, prev_map) + prev_tip
    return jnp.where(rank % 2 == node, node_own, lead_in)


def shards(subspace, s_inv, couple, diag_blocks, weights):
    points = s_inv.shape[0]
    blocks_dev = couple.shape[0]
    block_width = couple.shape[1]
    vectors = subspace.shape[0]
    source = subspace.reshape(vectors, blocks_dev, block_width).transpose(1, 0, 2)
    zero_rows = jnp.zeros((points, 2, vectors, block_width), jnp.float32)
    plain_eye = jnp.stack(
        [
            jnp.eye(block_width, dtype=jnp.float32),
            jnp.zeros((block_width, block_width), jnp.float32),
        ]
    )
    identity_map = jnp.broadcast_to(plain_eye, (points, 2, block_width, block_width))
    chain_size = lax.axis_size("chain")

    forward_start = jnp.concatenate([identity_map, zero_rows], axis=2)
    forward_both, forward_states = sweep_forward(
        s_inv, couple, forward_start, source, block_width, True
    )
    incoming = chain_incoming(forward_both, block_width, 1)
    solved_all = forward_states[:, :, :, block_width:] + right_apply_all(
        incoming, forward_states[:, :, :, :block_width]
    )

    backward_start = jnp.concatenate([identity_map, zero_rows], axis=2)
    backward_both, backward_all = sweep_backward(
        s_inv, couple, backward_start, solved_all, block_width, True
    )
    outgoing = chain_incoming(backward_both, block_width, -1)
    result = backward_all[:, :, :, block_width:] + right_apply_all(
        outgoing, backward_all[:, :, :, :block_width]
    )

    signed = weights * jnp.array([1.0, -1.0], jnp.float32)
    filtered_blocks = jnp.einsum("rqcnk,qc->rnk", result, signed, precision=highest)
    down_all = jnp.einsum("rnk,rkj->rnj", filtered_blocks, couple, precision=highest)
    from_next = passed_along(filtered_blocks[0], "chain", -1)
    from_prior = passed_along(down_all[-1], "chain", 1)
    diag_term = jnp.einsum("rnk,rjk->rnj", filtered_blocks, diag_blocks, precision=highest)
    upper_rows = jnp.concatenate([filtered_blocks[1:], from_next[None]], axis=0)
    term_up = jnp.einsum("rnk,rjk->rnj", upper_rows, couple, precision=highest)
    lower_rows = jnp.concatenate([from_prior[None], down_all[:-1]], axis=0)
    applied_blocks = diag_term + term_up + lower_rows
    gram_plain = jnp.einsum("rnk,rmk->nm", filtered_blocks, filtered_blocks, precision=highest)
    gram_matrix = jnp.einsum("rnk,rmk->nm", filtered_blocks, applied_blocks, precision=highest)
    summed = chain_sum(jnp.stack([gram_plain, gram_matrix]), "chain")
    grams = summed / (blocks_dev * block_width * chain_size)
    filtered = filtered_blocks.transpose(1, 0, 2).reshape(vectors, blocks_dev * block_width)
    applied = applied_blocks.transpose(1, 0, 2).reshape(vectors, blocks_dev * block_width)
    return (filtered, applied, grams)


def solution(mesh):
    placed = (
        P("parts", "chain"),
        P("parts", "chain", None, None, None),
        P("chain", "parts", None),
        P("chain", "parts", None),
        P("parts", None),
    )
    return jax.shard_map(
        shards,
        mesh=mesh,
        in_specs=placed,
        out_specs=(P("parts", "chain"), P("parts", "chain"), P(None, "parts", None)),
        check_vma=False,
    )
```

```python
import jax
import jax.numpy as jnp
from jax import lax
from jax.sharding import PartitionSpec as P

highest = lax.Precision.HIGHEST
sweep_precision = lax.Precision.HIGHEST
hop_precision = lax.Precision.HIGHEST


def passed_along(shard, axis, by):
    peers = lax.axis_size(axis)
    pairs = [(i, i + by) for i in range(peers) if 0 <= i + by < peers]
    return lax.ppermute(shard, axis, pairs)


def chain_sum(value, axis):
    peers = lax.axis_size(axis)
    if peers & (peers - 1):
        return lax.psum(value, axis)
    stride = 1
    while stride < peers:
        value = value + lax.ppermute(value, axis, [(i, i ^ stride) for i in range(peers)])
        stride *= 2
    return value


def inverse_apply(pivot_inv, vecs):
    real_part = jnp.einsum(
        "qnk,qjk->qnj", vecs[:, 0], pivot_inv[:, 0], precision=sweep_precision
    ) - jnp.einsum("qnk,qjk->qnj", vecs[:, 1], pivot_inv[:, 1], precision=sweep_precision)
    imag_part = jnp.einsum(
        "qnk,qjk->qnj", vecs[:, 0], pivot_inv[:, 1], precision=sweep_precision
    ) + jnp.einsum("qnk,qjk->qnj", vecs[:, 1], pivot_inv[:, 0], precision=sweep_precision)
    return jnp.stack([real_part, imag_part], axis=1)


def couple_down(coupling_blk, vecs):
    return jnp.einsum("qcnk,kj->qcnj", vecs, coupling_blk, precision=sweep_precision)


def couple_up(coupling_blk, vecs):
    return jnp.einsum("qcnk,jk->qcnj", vecs, coupling_blk, precision=sweep_precision)


def sweep_forward(pivots, couple, start_rows, source, rhs_rows, store_all):
    blocks_dev = couple.shape[0]

    def advance(carried, position):
        pivot_inv = lax.dynamic_index_in_dim(pivots, position, 1, keepdims=False)
        coupling_blk = lax.dynamic_index_in_dim(couple, position, 0, keepdims=False)
        combined = carried
        if source is not None:
            rhs_block = lax.dynamic_index_in_dim(source, position, 0, keepdims=False)
            rhs_full = jnp.stack([rhs_block, jnp.zeros_like(rhs_block)])
            rhs_full = jnp.broadcast_to(rhs_full[None], (combined.shape[0],) + rhs_full.shape)
            combined = combined.at[:, :, rhs_rows:].add(rhs_full)
        solved = inverse_apply(pivot_inv, combined)
        return (couple_down(coupling_blk, solved), solved if store_all else None)

    return lax.scan(advance, start_rows, jnp.arange(blocks_dev))


def sweep_backward(pivots, couple, start_rows, solved_all, rhs_rows, store_all):
    blocks_dev = couple.shape[0]

    def retreat(carried, position):
        pivot_inv = lax.dynamic_index_in_dim(pivots, position, 1, keepdims=False)
        coupling_blk = lax.dynamic_index_in_dim(couple, position, 0, keepdims=False)
        correction = inverse_apply(pivot_inv, couple_up(coupling_blk, carried))
        if solved_all is not None:
            known = lax.dynamic_index_in_dim(solved_all, position, 0, keepdims=False)
            correction = correction.at[:, :, rhs_rows:].add(known)
        return (correction, correction if store_all else None)

    return lax.scan(retreat, start_rows, jnp.arange(blocks_dev), reverse=True)


def block_real(matrix):
    top = jnp.concatenate([matrix[:, 0], matrix[:, 1]], axis=2)
    bottom = jnp.concatenate([-matrix[:, 1], matrix[:, 0]], axis=2)
    return jnp.concatenate([top, bottom], axis=1)


def flat_rows(vecs):
    return jnp.concatenate([vecs[:, 0], vecs[:, 1]], axis=2)


def unflat_rows(flat, width):
    return jnp.stack([flat[..., :width], flat[..., width:]], axis=1)


def right_apply(vecs, matrix):
    real_part = jnp.einsum(
        "qnk,qkj->qnj", vecs[:, 0], matrix[:, 0], precision=highest
    ) - jnp.einsum("qnk,qkj->qnj", vecs[:, 1], matrix[:, 1], precision=highest)
    imag_part = jnp.einsum(
        "qnk,qkj->qnj", vecs[:, 0], matrix[:, 1], precision=highest
    ) + jnp.einsum("qnk,qkj->qnj", vecs[:, 1], matrix[:, 0], precision=highest)
    return jnp.stack([real_part, imag_part], axis=1)


def right_apply_all(vecs, states):
    real_part = jnp.einsum(
        "qnk,rqkj->rqnj", vecs[:, 0], states[:, :, 0], precision=highest
    ) - jnp.einsum("qnk,rqkj->rqnj", vecs[:, 1], states[:, :, 1], precision=highest)
    imag_part = jnp.einsum(
        "qnk,rqkj->rqnj", vecs[:, 0], states[:, :, 1], precision=highest
    ) + jnp.einsum("qnk,rqkj->rqnj", vecs[:, 1], states[:, :, 0], precision=highest)
    return jnp.stack([real_part, imag_part], axis=2)


def pipelined_chain(maps, tips, pairs, depth, stages, active=True):
    points = tips.shape[0]

    def step(stage, inbox):
        point = jnp.clip(stage - depth, 0, points - 1)
        rows = lax.dynamic_index_in_dim(inbox, point, 0, keepdims=False)

        def hop():
            return jnp.dot(
                rows,
                lax.dynamic_index_in_dim(maps, point, 0, keepdims=False),
                precision=hop_precision,
            ) + lax.dynamic_index_in_dim(tips, point, 0, keepdims=False)

        out = lax.cond(active, hop, lambda: jnp.zeros_like(rows))
        got = lax.ppermute(out, "chain", pairs)
        slot = stage + 1 - depth
        keep = (slot >= 0) & (slot < points)
        slot = jnp.clip(slot, 0, points - 1)
        current = lax.dynamic_index_in_dim(inbox, slot, 0, keepdims=False)
        return lax.dynamic_update_index_in_dim(inbox, jnp.where(keep, got, current), slot, 0)

    return lax.fori_loop(0, stages, step, jnp.zeros_like(tips))


def chain_incoming(own_both, width, by):
    own_map = own_both[:, :, :width]
    own_tip = own_both[:, :, width:]
    points = own_tip.shape[0]
    peers = lax.axis_size("chain")
    rank = lax.axis_index("chain")
    if peers % 2:
        depth = rank if by > 0 else peers - 1 - rank
        pairs = [(i, i + by) for i in range(peers) if 0 <= i + by < peers]
        inbox = pipelined_chain(
            block_real(own_map), flat_rows(own_tip), pairs, depth, peers + points - 2
        )
        return unflat_rows(inbox, width)
    halves = peers // 2
    lead = 0 if by > 0 else 1
    node = 1 - lead
    to_node = [(2 * j + lead, 2 * j + node) for j in range(halves)]
    to_lead = [(2 * j + node, 2 * j + lead) for j in range(halves)]
    prev_both = lax.ppermute(own_both, "chain", to_node)
    prev_map = prev_both[:, :, :width]
    prev_tip = prev_both[:, :, width:]
    is_node = rank % 2 == node

    def compose():
        pair_both = right_apply(prev_both, own_map)
        pair_tip = pair_both[:, :, width:] + own_tip
        return block_real(pair_both[:, :, :width]), flat_rows(pair_tip)

    def idle():
        return (
            jnp.zeros((points, 2 * width, 2 * width), jnp.float32),
            jnp.zeros(own_tip.shape[:1] + own_tip.shape[2:3] + (2 * width,), jnp.float32),
        )

    pair_maps, pair_tips = lax.cond(is_node, compose, idle)
    pair_rank = rank // 2
    depth = pair_rank if by > 0 else halves - 1 - pair_rank
    pairs = [
        (2 * j + node, 2 * (j + by) + node) for j in range(halves) if 0 <= j + by < halves
    ]
    inbox = pipelined_chain(pair_maps, pair_tips, pairs, depth, halves + points - 2, is_node)
    node_in = unflat_rows(inbox, width)
    lead_in = lax.ppermute(node_in, "chain", to_lead)
    node_own = right_apply(node_in, prev_map) + prev_tip
    return jnp.where(is_node, node_own, lead_in)


def shards(subspace, s_inv, couple, diag_blocks, weights):
    points = s_inv.shape[0]
    blocks_dev = couple.shape[0]
    block_width = couple.shape[1]
    vectors = subspace.shape[0]
    source = subspace.reshape(vectors, blocks_dev, block_width).transpose(1, 0, 2)
    zero_rows = jnp.zeros((points, 2, vectors, block_width), jnp.float32)
    plain_eye = jnp.stack(
        [
            jnp.eye(block_width, dtype=jnp.float32),
            jnp.zeros((block_width, block_width), jnp.float32),
        ]
    )
    identity_map = jnp.broadcast_to(plain_eye, (points, 2, block_width, block_width))
    chain_size = lax.axis_size("chain")

    forward_start = jnp.concatenate([identity_map, zero_rows], axis=2)
    forward_both, forward_states = sweep_forward(
        s_inv, couple, forward_start, source, block_width, True
    )
    incoming = chain_incoming(forward_both, block_width, 1)
    solved_all = forward_states[:, :, :, block_width:] + right_apply_all(
        incoming, forward_states[:, :, :, :block_width]
    )

    backward_start = jnp.concatenate([identity_map, zero_rows], axis=2)
    backward_both, backward_all = sweep_backward(
        s_inv, couple, backward_start, solved_all, block_width, True
    )
    outgoing = chain_incoming(backward_both, block_width, -1)
    result = backward_all[:, :, :, block_width:] + right_apply_all(
        outgoing, backward_all[:, :, :, :block_width]
    )

    signed = weights * jnp.array([1.0, -1.0], jnp.float32)
    filtered_blocks = jnp.einsum("rqcnk,qc->rnk", result, signed, precision=highest)
    down_all = jnp.einsum("rnk,rkj->rnj", filtered_blocks, couple, precision=highest)
    from_next = passed_along(filtered_blocks[0], "chain", -1)
    from_prior = passed_along(down_all[-1], "chain", 1)
    diag_term = jnp.einsum("rnk,rjk->rnj", filtered_blocks, diag_blocks, precision=highest)
    upper_rows = jnp.concatenate([filtered_blocks[1:], from_next[None]], axis=0)
    term_up = jnp.einsum("rnk,rjk->rnj", upper_rows, couple, precision=highest)
    lower_rows = jnp.concatenate([from_prior[None], down_all[:-1]], axis=0)
    applied_blocks = diag_term + term_up + lower_rows
    gram_plain = jnp.einsum("rnk,rmk->nm", filtered_blocks, filtered_blocks, precision=highest)
    gram_matrix = jnp.einsum("rnk,rmk->nm", filtered_blocks, applied_blocks, precision=highest)
    summed = chain_sum(jnp.stack([gram_plain, gram_matrix]), "chain")
    grams = summed / (blocks_dev * block_width * chain_size)
    filtered = filtered_blocks.transpose(1, 0, 2).reshape(vectors, blocks_dev * block_width)
    applied = applied_blocks.transpose(1, 0, 2).reshape(vectors, blocks_dev * block_width)
    return (filtered, applied, grams)


def solution(mesh):
    placed = (
        P("parts", "chain"),
        P("parts", "chain", None, None, None),
        P("chain", "parts", None),
        P("chain", "parts", None),
        P("parts", None),
    )
    return jax.shard_map(
        shards,
        mesh=mesh,
        in_specs=placed,
        out_specs=(P("parts", "chain"), P("parts", "chain"), P(None, "parts", None)),
        check_vma=False,
    )
```

```python
import jax
import jax.numpy as jnp
from jax import lax
from jax.sharding import PartitionSpec as P

highest = lax.Precision.HIGHEST
sweep_precision = lax.Precision.HIGHEST
hop_precision = lax.Precision.HIGHEST


def passed_along(shard, axis, by):
    peers = lax.axis_size(axis)
    pairs = [(i, i + by) for i in range(peers) if 0 <= i + by < peers]
    return lax.ppermute(shard, axis, pairs)


def chain_sum(value, axis):
    peers = lax.axis_size(axis)
    if peers & (peers - 1):
        return lax.psum(value, axis)
    stride = 1
    while stride < peers:
        value = value + lax.ppermute(value, axis, [(i, i ^ stride) for i in range(peers)])
        stride *= 2
    return value


def inverse_apply(pivot_inv, vecs):
    real_part = jnp.einsum(
        "qnk,qjk->qnj", vecs[:, 0], pivot_inv[:, 0], precision=sweep_precision
    ) - jnp.einsum("qnk,qjk->qnj", vecs[:, 1], pivot_inv[:, 1], precision=sweep_precision)
    imag_part = jnp.einsum(
        "qnk,qjk->qnj", vecs[:, 0], pivot_inv[:, 1], precision=sweep_precision
    ) + jnp.einsum("qnk,qjk->qnj", vecs[:, 1], pivot_inv[:, 0], precision=sweep_precision)
    return jnp.stack([real_part, imag_part], axis=1)


def couple_down(coupling_blk, vecs):
    return jnp.einsum("qcnk,kj->qcnj", vecs, coupling_blk, precision=sweep_precision)


def couple_up(coupling_blk, vecs):
    return jnp.einsum("qcnk,jk->qcnj", vecs, coupling_blk, precision=sweep_precision)


def sweep_forward(pivots, couple, start_rows, source, rhs_rows, store_all):
    blocks_dev = couple.shape[0]

    def advance(carried, position):
        pivot_inv = lax.dynamic_index_in_dim(pivots, position, 1, keepdims=False)
        coupling_blk = lax.dynamic_index_in_dim(couple, position, 0, keepdims=False)
        combined = carried
        if source is not None:
            rhs_block = lax.dynamic_index_in_dim(source, position, 0, keepdims=False)
            rhs_full = jnp.stack([rhs_block, jnp.zeros_like(rhs_block)])
            rhs_full = jnp.broadcast_to(rhs_full[None], (combined.shape[0],) + rhs_full.shape)
            combined = combined.at[:, :, rhs_rows:].add(rhs_full)
        solved = inverse_apply(pivot_inv, combined)
        return (couple_down(coupling_blk, solved), solved if store_all else None)

    return lax.scan(advance, start_rows, jnp.arange(blocks_dev))


def sweep_backward(pivots, couple, start_rows, solved_all, rhs_rows, store_all):
    blocks_dev = couple.shape[0]

    def retreat(carried, position):
        pivot_inv = lax.dynamic_index_in_dim(pivots, position, 1, keepdims=False)
        coupling_blk = lax.dynamic_index_in_dim(couple, position, 0, keepdims=False)
        correction = inverse_apply(pivot_inv, couple_up(coupling_blk, carried))
        if solved_all is not None:
            known = lax.dynamic_index_in_dim(solved_all, position, 0, keepdims=False)
            correction = correction.at[:, :, rhs_rows:].add(known)
        return (correction, correction if store_all else None)

    return lax.scan(retreat, start_rows, jnp.arange(blocks_dev), reverse=True)


def block_real(matrix):
    top = jnp.concatenate([matrix[:, 0], matrix[:, 1]], axis=2)
    bottom = jnp.concatenate([-matrix[:, 1], matrix[:, 0]], axis=2)
    return jnp.concatenate([top, bottom], axis=1)


def flat_rows(vecs):
    return jnp.concatenate([vecs[:, 0], vecs[:, 1]], axis=2)


def unflat_rows(flat, width):
    return jnp.stack([flat[..., :width], flat[..., width:]], axis=1)


def right_apply(vecs, matrix):
    real_part = jnp.einsum(
        "qnk,qkj->qnj", vecs[:, 0], matrix[:, 0], precision=highest
    ) - jnp.einsum("qnk,qkj->qnj", vecs[:, 1], matrix[:, 1], precision=highest)
    imag_part = jnp.einsum(
        "qnk,qkj->qnj", vecs[:, 0], matrix[:, 1], precision=highest
    ) + jnp.einsum("qnk,qkj->qnj", vecs[:, 1], matrix[:, 0], precision=highest)
    return jnp.stack([real_part, imag_part], axis=1)


def right_apply_all(vecs, states):
    real_part = jnp.einsum(
        "qnk,rqkj->rqnj", vecs[:, 0], states[:, :, 0], precision=highest
    ) - jnp.einsum("qnk,rqkj->rqnj", vecs[:, 1], states[:, :, 1], precision=highest)
    imag_part = jnp.einsum(
        "qnk,rqkj->rqnj", vecs[:, 0], states[:, :, 1], precision=highest
    ) + jnp.einsum("qnk,rqkj->rqnj", vecs[:, 1], states[:, :, 0], precision=highest)
    return jnp.stack([real_part, imag_part], axis=2)


def pipelined_chain(maps, tips, pairs, depth, stages, active=True):
    points = tips.shape[0]

    def step(stage, inbox):
        point = jnp.clip(stage - depth, 0, points - 1)
        rows = lax.dynamic_index_in_dim(inbox, point, 0, keepdims=False)

        def hop():
            return jnp.dot(
                rows,
                lax.dynamic_index_in_dim(maps, point, 0, keepdims=False),
                precision=hop_precision,
            ) + lax.dynamic_index_in_dim(tips, point, 0, keepdims=False)

        out = lax.cond(active, hop, lambda: jnp.zeros_like(rows))
        got = lax.ppermute(out, "chain", pairs)
        slot = stage + 1 - depth
        keep = (slot >= 0) & (slot < points)
        slot = jnp.clip(slot, 0, points - 1)
        current = lax.dynamic_index_in_dim(inbox, slot, 0, keepdims=False)
        return lax.dynamic_update_index_in_dim(inbox, jnp.where(keep, got, current), slot, 0)

    return lax.fori_loop(0, stages, step, jnp.zeros_like(tips))


def chain_incoming(own_both, width, by):
    own_map = own_both[:, :, :width]
    own_tip = own_both[:, :, width:]
    points = own_tip.shape[0]
    peers = lax.axis_size("chain")
    rank = lax.axis_index("chain")
    if peers % 2:
        depth = rank if by > 0 else peers - 1 - rank
        pairs = [(i, i + by) for i in range(peers) if 0 <= i + by < peers]
        inbox = pipelined_chain(
            block_real(own_map), flat_rows(own_tip), pairs, depth, peers + points - 2
        )
        return unflat_rows(inbox, width)
    halves = peers // 2
    lead = 0 if by > 0 else 1
    node = 1 - lead
    to_node = [(2 * j + lead, 2 * j + node) for j in range(halves)]
    to_lead = [(2 * j + node, 2 * j + lead) for j in range(halves)]
    prev_both = lax.ppermute(own_both, "chain", to_node)
    prev_map = prev_both[:, :, :width]
    prev_tip = prev_both[:, :, width:]
    is_node = rank % 2 == node

    def compose():
        pair_both = right_apply(prev_both, own_map)
        pair_tip = pair_both[:, :, width:] + own_tip
        return block_real(pair_both[:, :, :width]), flat_rows(pair_tip)

    def idle():
        return (
            jnp.zeros((points, 2 * width, 2 * width), jnp.float32),
            jnp.zeros(own_tip.shape[:1] + own_tip.shape[2:3] + (2 * width,), jnp.float32),
        )

    if by > 0:
        pair_maps, pair_tips = lax.cond(is_node, compose, idle)
    else:
        pair_maps, pair_tips = compose()
    pair_rank = rank // 2
    depth = pair_rank if by > 0 else halves - 1 - pair_rank
    pairs = [
        (2 * j + node, 2 * (j + by) + node) for j in range(halves) if 0 <= j + by < halves
    ]
    inbox = pipelined_chain(pair_maps, pair_tips, pairs, depth, halves + points - 2, is_node)
    node_in = unflat_rows(inbox, width)
    lead_in = lax.ppermute(node_in, "chain", to_lead)
    node_own = right_apply(node_in, prev_map) + prev_tip
    return jnp.where(is_node, node_own, lead_in)


def shards(subspace, s_inv, couple, diag_blocks, weights):
    points = s_inv.shape[0]
    blocks_dev = couple.shape[0]
    block_width = couple.shape[1]
    vectors = subspace.shape[0]
    source = subspace.reshape(vectors, blocks_dev, block_width).transpose(1, 0, 2)
    zero_rows = jnp.zeros((points, 2, vectors, block_width), jnp.float32)
    plain_eye = jnp.stack(
        [
            jnp.eye(block_width, dtype=jnp.float32),
            jnp.zeros((block_width, block_width), jnp.float32),
        ]
    )
    identity_map = jnp.broadcast_to(plain_eye, (points, 2, block_width, block_width))
    chain_size = lax.axis_size("chain")

    forward_start = jnp.concatenate([identity_map, zero_rows], axis=2)
    forward_both, forward_states = sweep_forward(
        s_inv, couple, forward_start, source, block_width, True
    )
    incoming = chain_incoming(forward_both, block_width, 1)
    solved_all = forward_states[:, :, :, block_width:] + right_apply_all(
        incoming, forward_states[:, :, :, :block_width]
    )

    backward_start = jnp.concatenate([identity_map, zero_rows], axis=2)
    backward_both, backward_all = sweep_backward(
        s_inv, couple, backward_start, solved_all, block_width, True
    )
    outgoing = chain_incoming(backward_both, block_width, -1)
    result = backward_all[:, :, :, block_width:] + right_apply_all(
        outgoing, backward_all[:, :, :, :block_width]
    )

    signed = weights * jnp.array([1.0, -1.0], jnp.float32)
    filtered_blocks = jnp.einsum("rqcnk,qc->rnk", result, signed, precision=highest)
    down_all = jnp.einsum("rnk,rkj->rnj", filtered_blocks, couple, precision=highest)
    from_next = passed_along(filtered_blocks[0], "chain", -1)
    from_prior = passed_along(down_all[-1], "chain", 1)
    diag_term = jnp.einsum("rnk,rjk->rnj", filtered_blocks, diag_blocks, precision=highest)
    upper_rows = jnp.concatenate([filtered_blocks[1:], from_next[None]], axis=0)
    term_up = jnp.einsum("rnk,rjk->rnj", upper_rows, couple, precision=highest)
    lower_rows = jnp.concatenate([from_prior[None], down_all[:-1]], axis=0)
    applied_blocks = diag_term + term_up + lower_rows
    gram_plain = jnp.einsum("rnk,rmk->nm", filtered_blocks, filtered_blocks, precision=highest)
    gram_matrix = jnp.einsum("rnk,rmk->nm", filtered_blocks, applied_blocks, precision=highest)
    summed = chain_sum(jnp.stack([gram_plain, gram_matrix]), "chain")
    grams = summed / (blocks_dev * block_width * chain_size)
    filtered = filtered_blocks.transpose(1, 0, 2).reshape(vectors, blocks_dev * block_width)
    applied = applied_blocks.transpose(1, 0, 2).reshape(vectors, blocks_dev * block_width)
    return (filtered, applied, grams)


def solution(mesh):
    placed = (
        P("parts", "chain"),
        P("parts", "chain", None, None, None),
        P("chain", "parts", None),
        P("chain", "parts", None),
        P("parts", None),
    )
    return jax.shard_map(
        shards,
        mesh=mesh,
        in_specs=placed,
        out_specs=(P("parts", "chain"), P("parts", "chain"), P(None, "parts", None)),
        check_vma=False,
    )
```

```python
import jax
import jax.numpy as jnp
from jax import lax
from jax.sharding import PartitionSpec as P

highest = lax.Precision.HIGHEST
sweep_precision = lax.Precision.HIGHEST
hop_precision = lax.Precision.HIGHEST


def passed_along(shard, axis, by):
    peers = lax.axis_size(axis)
    pairs = [(i, i + by) for i in range(peers) if 0 <= i + by < peers]
    return lax.ppermute(shard, axis, pairs)


def chain_sum(value, axis):
    peers = lax.axis_size(axis)
    if peers & (peers - 1):
        return lax.psum(value, axis)
    stride = 1
    while stride < peers:
        value = value + lax.ppermute(value, axis, [(i, i ^ stride) for i in range(peers)])
        stride *= 2
    return value


def split_signs(vecs, axis):
    real_rows = jnp.stack(
        [lax.index_in_dim(vecs, 0, axis, False), -lax.index_in_dim(vecs, 1, axis, False)], axis
    )
    imag_rows = jnp.stack(
        [lax.index_in_dim(vecs, 1, axis, False), lax.index_in_dim(vecs, 0, axis, False)], axis
    )
    return real_rows, imag_rows


def inverse_apply(pivot_inv, vecs):
    real_rows, imag_rows = split_signs(vecs, 1)
    real_part = jnp.einsum("qcnk,qcjk->qnj", real_rows, pivot_inv, precision=sweep_precision)
    imag_part = jnp.einsum("qcnk,qcjk->qnj", imag_rows, pivot_inv, precision=sweep_precision)
    return jnp.stack([real_part, imag_part], axis=1)


def couple_down(coupling_blk, vecs):
    return jnp.einsum("qcnk,kj->qcnj", vecs, coupling_blk, precision=sweep_precision)


def couple_up(coupling_blk, vecs):
    return jnp.einsum("qcnk,jk->qcnj", vecs, coupling_blk, precision=sweep_precision)


def sweep_forward(pivots, couple, start_rows, source, rhs_rows, store_all):
    blocks_dev = couple.shape[0]

    def advance(carried, position):
        pivot_inv = lax.dynamic_index_in_dim(pivots, position, 1, keepdims=False)
        coupling_blk = lax.dynamic_index_in_dim(couple, position, 0, keepdims=False)
        combined = carried
        if source is not None:
            rhs_block = lax.dynamic_index_in_dim(source, position, 0, keepdims=False)
            rhs_full = jnp.stack([rhs_block, jnp.zeros_like(rhs_block)])
            rhs_full = jnp.broadcast_to(rhs_full[None], (combined.shape[0],) + rhs_full.shape)
            combined = combined.at[:, :, rhs_rows:].add(rhs_full)
        solved = inverse_apply(pivot_inv, combined)
        return (couple_down(coupling_blk, solved), solved if store_all else None)

    return lax.scan(advance, start_rows, jnp.arange(blocks_dev))


def sweep_backward(pivots, couple, start_rows, solved_all, rhs_rows, store_all):
    blocks_dev = couple.shape[0]

    def retreat(carried, position):
        pivot_inv = lax.dynamic_index_in_dim(pivots, position, 1, keepdims=False)
        coupling_blk = lax.dynamic_index_in_dim(couple, position, 0, keepdims=False)
        correction = inverse_apply(pivot_inv, couple_up(coupling_blk, carried))
        if solved_all is not None:
            known = lax.dynamic_index_in_dim(solved_all, position, 0, keepdims=False)
            correction = correction.at[:, :, rhs_rows:].add(known)
        return (correction, correction if store_all else None)

    return lax.scan(retreat, start_rows, jnp.arange(blocks_dev), reverse=True)


def block_real(matrix):
    top = jnp.concatenate([matrix[:, 0], matrix[:, 1]], axis=2)
    bottom = jnp.concatenate([-matrix[:, 1], matrix[:, 0]], axis=2)
    return jnp.concatenate([top, bottom], axis=1)


def flat_rows(vecs):
    return jnp.concatenate([vecs[:, 0], vecs[:, 1]], axis=2)


def unflat_rows(flat, width):
    return jnp.stack([flat[..., :width], flat[..., width:]], axis=1)


def right_apply(vecs, matrix):
    real_rows, imag_rows = split_signs(vecs, 1)
    real_part = jnp.einsum("qcnk,qckj->qnj", real_rows, matrix, precision=highest)
    imag_part = jnp.einsum("qcnk,qckj->qnj", imag_rows, matrix, precision=highest)
    return jnp.stack([real_part, imag_part], axis=1)


def right_apply_all(vecs, states):
    real_rows, imag_rows = split_signs(vecs, 1)
    real_part = jnp.einsum("qcnk,rqckj->rqnj", real_rows, states, precision=highest)
    imag_part = jnp.einsum("qcnk,rqckj->rqnj", imag_rows, states, precision=highest)
    return jnp.stack([real_part, imag_part], axis=2)


def pipelined_chain(maps, tips, pairs, depth, stages, active=True):
    points = tips.shape[0]

    def step(stage, inbox):
        point = jnp.clip(stage - depth, 0, points - 1)
        rows = lax.dynamic_index_in_dim(inbox, point, 0, keepdims=False)

        def hop():
            return jnp.dot(
                rows,
                lax.dynamic_index_in_dim(maps, point, 0, keepdims=False),
                precision=hop_precision,
            ) + lax.dynamic_index_in_dim(tips, point, 0, keepdims=False)

        out = lax.cond(active, hop, lambda: jnp.zeros_like(rows))
        got = lax.ppermute(out, "chain", pairs)
        slot = stage + 1 - depth
        keep = (slot >= 0) & (slot < points)
        slot = jnp.clip(slot, 0, points - 1)
        current = lax.dynamic_index_in_dim(inbox, slot, 0, keepdims=False)
        return lax.dynamic_update_index_in_dim(inbox, jnp.where(keep, got, current), slot, 0)

    return lax.fori_loop(0, stages, step, jnp.zeros_like(tips))


def chain_incoming(own_both, width, by):
    own_map = own_both[:, :, :width]
    own_tip = own_both[:, :, width:]
    points = own_tip.shape[0]
    peers = lax.axis_size("chain")
    rank = lax.axis_index("chain")
    if peers % 2:
        depth = rank if by > 0 else peers - 1 - rank
        pairs = [(i, i + by) for i in range(peers) if 0 <= i + by < peers]
        inbox = pipelined_chain(
            block_real(own_map), flat_rows(own_tip), pairs, depth, peers + points - 2
        )
        return unflat_rows(inbox, width)
    halves = peers // 2
    lead = 0 if by > 0 else 1
    node = 1 - lead
    to_node = [(2 * j + lead, 2 * j + node) for j in range(halves)]
    to_lead = [(2 * j + node, 2 * j + lead) for j in range(halves)]
    prev_both = lax.ppermute(own_both, "chain", to_node)
    prev_map = prev_both[:, :, :width]
    prev_tip = prev_both[:, :, width:]
    is_node = rank % 2 == node

    def compose():
        pair_both = right_apply(prev_both, own_map)
        pair_tip = pair_both[:, :, width:] + own_tip
        return block_real(pair_both[:, :, :width]), flat_rows(pair_tip)

    def idle():
        return (
            jnp.zeros((points, 2 * width, 2 * width), jnp.float32),
            jnp.zeros(own_tip.shape[:1] + own_tip.shape[2:3] + (2 * width,), jnp.float32),
        )

    pair_maps, pair_tips = lax.cond(is_node, compose, idle)
    pair_rank = rank // 2
    depth = pair_rank if by > 0 else halves - 1 - pair_rank
    pairs = [
        (2 * j + node, 2 * (j + by) + node) for j in range(halves) if 0 <= j + by < halves
    ]
    inbox = pipelined_chain(pair_maps, pair_tips, pairs, depth, halves + points - 2, is_node)
    node_in = unflat_rows(inbox, width)
    lead_in = lax.ppermute(node_in, "chain", to_lead)
    node_own = right_apply(node_in, prev_map) + prev_tip
    return jnp.where(is_node, node_own, lead_in)


def shards(subspace, s_inv, couple, diag_blocks, weights):
    points = s_inv.shape[0]
    blocks_dev = couple.shape[0]
    block_width = couple.shape[1]
    vectors = subspace.shape[0]
    source = subspace.reshape(vectors, blocks_dev, block_width).transpose(1, 0, 2)
    zero_rows = jnp.zeros((points, 2, vectors, block_width), jnp.float32)
    plain_eye = jnp.stack(
        [
            jnp.eye(block_width, dtype=jnp.float32),
            jnp.zeros((block_width, block_width), jnp.float32),
        ]
    )
    identity_map = jnp.broadcast_to(plain_eye, (points, 2, block_width, block_width))
    chain_size = lax.axis_size("chain")

    forward_start = jnp.concatenate([identity_map, zero_rows], axis=2)
    forward_both, forward_states = sweep_forward(
        s_inv, couple, forward_start, source, block_width, True
    )
    incoming = chain_incoming(forward_both, block_width, 1)
    solved_all = forward_states[:, :, :, block_width:] + right_apply_all(
        incoming, forward_states[:, :, :, :block_width]
    )

    backward_start = jnp.concatenate([identity_map, zero_rows], axis=2)
    backward_both, backward_all = sweep_backward(
        s_inv, couple, backward_start, solved_all, block_width, True
    )
    outgoing = chain_incoming(backward_both, block_width, -1)
    result = backward_all[:, :, :, block_width:] + right_apply_all(
        outgoing, backward_all[:, :, :, :block_width]
    )

    signed = weights * jnp.array([1.0, -1.0], jnp.float32)
    filtered_blocks = jnp.einsum("rqcnk,qc->rnk", result, signed, precision=highest)
    down_all = jnp.einsum("rnk,rkj->rnj", filtered_blocks, couple, precision=highest)
    from_next = passed_along(filtered_blocks[0], "chain", -1)
    from_prior = passed_along(down_all[-1], "chain", 1)
    diag_term = jnp.einsum("rnk,rjk->rnj", filtered_blocks, diag_blocks, precision=highest)
    upper_rows = jnp.concatenate([filtered_blocks[1:], from_next[None]], axis=0)
    term_up = jnp.einsum("rnk,rjk->rnj", upper_rows, couple, precision=highest)
    lower_rows = jnp.concatenate([from_prior[None], down_all[:-1]], axis=0)
    applied_blocks = diag_term + term_up + lower_rows
    gram_plain = jnp.einsum("rnk,rmk->nm", filtered_blocks, filtered_blocks, precision=highest)
    gram_matrix = jnp.einsum("rnk,rmk->nm", filtered_blocks, applied_blocks, precision=highest)
    summed = chain_sum(jnp.stack([gram_plain, gram_matrix]), "chain")
    grams = summed / (blocks_dev * block_width * chain_size)
    filtered = filtered_blocks.transpose(1, 0, 2).reshape(vectors, blocks_dev * block_width)
    applied = applied_blocks.transpose(1, 0, 2).reshape(vectors, blocks_dev * block_width)
    return (filtered, applied, grams)


def solution(mesh):
    placed = (
        P("parts", "chain"),
        P("parts", "chain", None, None, None),
        P("chain", "parts", None),
        P("chain", "parts", None),
        P("parts", None),
    )
    return jax.shard_map(
        shards,
        mesh=mesh,
        in_specs=placed,
        out_specs=(P("parts", "chain"), P("parts", "chain"), P(None, "parts", None)),
        check_vma=False,
    )
```

```python
import jax
import jax.numpy as jnp
from jax import lax
from jax.sharding import PartitionSpec as P

highest = lax.Precision.HIGHEST
sweep_precision = lax.Precision.HIGHEST
hop_precision = lax.Precision.HIGHEST


def passed_along(shard, axis, by):
    peers = lax.axis_size(axis)
    pairs = [(i, i + by) for i in range(peers) if 0 <= i + by < peers]
    return lax.ppermute(shard, axis, pairs)


def chain_sum(value, axis):
    peers = lax.axis_size(axis)
    if peers & (peers - 1):
        return lax.psum(value, axis)
    stride = 1
    while stride < peers:
        value = value + lax.ppermute(value, axis, [(i, i ^ stride) for i in range(peers)])
        stride *= 2
    return value


def split_signs(vecs, axis):
    real_rows = jnp.stack(
        [lax.index_in_dim(vecs, 0, axis, False), -lax.index_in_dim(vecs, 1, axis, False)], axis
    )
    imag_rows = jnp.stack(
        [lax.index_in_dim(vecs, 1, axis, False), lax.index_in_dim(vecs, 0, axis, False)], axis
    )
    return real_rows, imag_rows


def inverse_apply(pivot_inv, vecs):
    real_rows, imag_rows = split_signs(vecs, 1)
    real_part = jnp.einsum("qcnk,qcjk->qnj", real_rows, pivot_inv, precision=sweep_precision)
    imag_part = jnp.einsum("qcnk,qcjk->qnj", imag_rows, pivot_inv, precision=sweep_precision)
    return jnp.stack([real_part, imag_part], axis=1)


def couple_down(coupling_blk, vecs):
    return jnp.einsum("qcnk,kj->qcnj", vecs, coupling_blk, precision=sweep_precision)


def couple_up(coupling_blk, vecs):
    return jnp.einsum("qcnk,jk->qcnj", vecs, coupling_blk, precision=sweep_precision)


def sweep_forward(pivots, couple, start_rows, source, rhs_rows, store_all):
    blocks_dev = couple.shape[0]

    def advance(carried, position):
        pivot_inv = lax.dynamic_index_in_dim(pivots, position, 1, keepdims=False)
        coupling_blk = lax.dynamic_index_in_dim(couple, position, 0, keepdims=False)
        combined = carried
        if source is not None:
            rhs_block = lax.dynamic_index_in_dim(source, position, 0, keepdims=False)
            rhs_full = jnp.stack([rhs_block, jnp.zeros_like(rhs_block)])
            rhs_full = jnp.broadcast_to(rhs_full[None], (combined.shape[0],) + rhs_full.shape)
            combined = combined.at[:, :, rhs_rows:].add(rhs_full)
        solved = inverse_apply(pivot_inv, combined)
        return (couple_down(coupling_blk, solved), solved if store_all else None)

    return lax.scan(advance, start_rows, jnp.arange(blocks_dev))


def sweep_backward(pivots, couple, start_rows, solved_all, rhs_rows, store_all):
    blocks_dev = couple.shape[0]

    def retreat(carried, position):
        pivot_inv = lax.dynamic_index_in_dim(pivots, position, 1, keepdims=False)
        coupling_blk = lax.dynamic_index_in_dim(couple, position, 0, keepdims=False)
        correction = inverse_apply(pivot_inv, couple_up(coupling_blk, carried))
        if solved_all is not None:
            known = lax.dynamic_index_in_dim(solved_all, position, 0, keepdims=False)
            correction = correction.at[:, :, rhs_rows:].add(known)
        return (correction, correction if store_all else None)

    return lax.scan(retreat, start_rows, jnp.arange(blocks_dev), reverse=True)


def right_apply(vecs, matrix):
    real_rows, imag_rows = split_signs(vecs, 1)
    real_part = jnp.einsum("qcnk,qckj->qnj", real_rows, matrix, precision=highest)
    imag_part = jnp.einsum("qcnk,qckj->qnj", imag_rows, matrix, precision=highest)
    return jnp.stack([real_part, imag_part], axis=1)


def right_apply_all(vecs, states):
    real_rows, imag_rows = split_signs(vecs, 1)
    real_part = jnp.einsum("qcnk,rqckj->rqnj", real_rows, states, precision=highest)
    imag_part = jnp.einsum("qcnk,rqckj->rqnj", imag_rows, states, precision=highest)
    return jnp.stack([real_part, imag_part], axis=2)


def pipelined_chain(maps, tips, pairs, depth, stages, active=True):
    points = tips.shape[0]

    def step(stage, inbox):
        point = jnp.clip(stage - depth, 0, points - 1)
        rows = lax.dynamic_index_in_dim(inbox, point, 0, keepdims=False)

        def hop():
            matrix = lax.dynamic_index_in_dim(maps, point, 0, keepdims=False)
            real_rows, imag_rows = split_signs(rows, 0)
            real_part = jnp.einsum("cnk,ckj->nj", real_rows, matrix, precision=hop_precision)
            imag_part = jnp.einsum("cnk,ckj->nj", imag_rows, matrix, precision=hop_precision)
            return jnp.stack([real_part, imag_part]) + lax.dynamic_index_in_dim(
                tips, point, 0, keepdims=False
            )

        out = lax.cond(active, hop, lambda: jnp.zeros_like(rows))
        got = lax.ppermute(out, "chain", pairs)
        slot = stage + 1 - depth
        keep = (slot >= 0) & (slot < points)
        slot = jnp.clip(slot, 0, points - 1)
        current = lax.dynamic_index_in_dim(inbox, slot, 0, keepdims=False)
        return lax.dynamic_update_index_in_dim(inbox, jnp.where(keep, got, current), slot, 0)

    return lax.fori_loop(0, stages, step, jnp.zeros_like(tips))


def chain_incoming(own_both, width, by):
    own_map = own_both[:, :, :width]
    own_tip = own_both[:, :, width:]
    points = own_tip.shape[0]
    peers = lax.axis_size("chain")
    rank = lax.axis_index("chain")
    if peers % 2:
        depth = rank if by > 0 else peers - 1 - rank
        pairs = [(i, i + by) for i in range(peers) if 0 <= i + by < peers]
        return pipelined_chain(own_map, own_tip, pairs, depth, peers + points - 2)
    halves = peers // 2
    lead = 0 if by > 0 else 1
    node = 1 - lead
    to_node = [(2 * j + lead, 2 * j + node) for j in range(halves)]
    to_lead = [(2 * j + node, 2 * j + lead) for j in range(halves)]
    prev_both = lax.ppermute(own_both, "chain", to_node)
    prev_map = prev_both[:, :, :width]
    prev_tip = prev_both[:, :, width:]
    is_node = rank % 2 == node

    def compose():
        pair_both = right_apply(prev_both, own_map)
        pair_tip = pair_both[:, :, width:] + own_tip
        return pair_both[:, :, :width], pair_tip

    def idle():
        return jnp.zeros_like(own_map), jnp.zeros_like(own_tip)

    pair_maps, pair_tips = lax.cond(is_node, compose, idle)
    pair_rank = rank // 2
    depth = pair_rank if by > 0 else halves - 1 - pair_rank
    pairs = [
        (2 * j + node, 2 * (j + by) + node) for j in range(halves) if 0 <= j + by < halves
    ]
    node_in = pipelined_chain(pair_maps, pair_tips, pairs, depth, halves + points - 2, is_node)
    lead_in = lax.ppermute(node_in, "chain", to_lead)
    node_own = right_apply(node_in, prev_map) + prev_tip
    return jnp.where(is_node, node_own, lead_in)


def shards(subspace, s_inv, couple, diag_blocks, weights):
    points = s_inv.shape[0]
    blocks_dev = couple.shape[0]
    block_width = couple.shape[1]
    vectors = subspace.shape[0]
    source = subspace.reshape(vectors, blocks_dev, block_width).transpose(1, 0, 2)
    zero_rows = jnp.zeros((points, 2, vectors, block_width), jnp.float32)
    plain_eye = jnp.stack(
        [
            jnp.eye(block_width, dtype=jnp.float32),
            jnp.zeros((block_width, block_width), jnp.float32),
        ]
    )
    identity_map = jnp.broadcast_to(plain_eye, (points, 2, block_width, block_width))
    chain_size = lax.axis_size("chain")

    forward_start = jnp.concatenate([identity_map, zero_rows], axis=2)
    forward_both, forward_states = sweep_forward(
        s_inv, couple, forward_start, source, block_width, True
    )
    incoming = chain_incoming(forward_both, block_width, 1)
    solved_all = forward_states[:, :, :, block_width:] + right_apply_all(
        incoming, forward_states[:, :, :, :block_width]
    )

    backward_start = jnp.concatenate([identity_map, zero_rows], axis=2)
    backward_both, backward_all = sweep_backward(
        s_inv, couple, backward_start, solved_all, block_width, True
    )
    outgoing = chain_incoming(backward_both, block_width, -1)
    result = backward_all[:, :, :, block_width:] + right_apply_all(
        outgoing, backward_all[:, :, :, :block_width]
    )

    signed = weights * jnp.array([1.0, -1.0], jnp.float32)
    filtered_blocks = jnp.einsum("rqcnk,qc->rnk", result, signed, precision=highest)
    down_all = jnp.einsum("rnk,rkj->rnj", filtered_blocks, couple, precision=highest)
    from_next = passed_along(filtered_blocks[0], "chain", -1)
    from_prior = passed_along(down_all[-1], "chain", 1)
    diag_term = jnp.einsum("rnk,rjk->rnj", filtered_blocks, diag_blocks, precision=highest)
    upper_rows = jnp.concatenate([filtered_blocks[1:], from_next[None]], axis=0)
    term_up = jnp.einsum("rnk,rjk->rnj", upper_rows, couple, precision=highest)
    lower_rows = jnp.concatenate([from_prior[None], down_all[:-1]], axis=0)
    applied_blocks = diag_term + term_up + lower_rows
    gram_plain = jnp.einsum("rnk,rmk->nm", filtered_blocks, filtered_blocks, precision=highest)
    gram_matrix = jnp.einsum("rnk,rmk->nm", filtered_blocks, applied_blocks, precision=highest)
    summed = chain_sum(jnp.stack([gram_plain, gram_matrix]), "chain")
    grams = summed / (blocks_dev * block_width * chain_size)
    filtered = filtered_blocks.transpose(1, 0, 2).reshape(vectors, blocks_dev * block_width)
    applied = applied_blocks.transpose(1, 0, 2).reshape(vectors, blocks_dev * block_width)
    return (filtered, applied, grams)


def solution(mesh):
    placed = (
        P("parts", "chain"),
        P("parts", "chain", None, None, None),
        P("chain", "parts", None),
        P("chain", "parts", None),
        P("parts", None),
    )
    return jax.shard_map(
        shards,
        mesh=mesh,
        in_specs=placed,
        out_specs=(P("parts", "chain"), P("parts", "chain"), P(None, "parts", None)),
        check_vma=False,
    )
```

```python
import jax
import jax.numpy as jnp
from jax import lax
from jax.sharding import PartitionSpec as P

highest = lax.Precision.HIGHEST
sweep_precision = lax.Precision.HIGHEST
hop_precision = lax.Precision.HIGHEST


def passed_along(shard, axis, by):
    peers = lax.axis_size(axis)
    pairs = [(i, i + by) for i in range(peers) if 0 <= i + by < peers]
    return lax.ppermute(shard, axis, pairs)


def chain_sum(value, axis):
    peers = lax.axis_size(axis)
    if peers & (peers - 1):
        return lax.psum(value, axis)
    stride = 1
    while stride < peers:
        value = value + lax.ppermute(value, axis, [(i, i ^ stride) for i in range(peers)])
        stride *= 2
    return value


def split_signs(vecs, axis):
    real_rows = jnp.stack(
        [lax.index_in_dim(vecs, 0, axis, False), -lax.index_in_dim(vecs, 1, axis, False)], axis
    )
    imag_rows = jnp.stack(
        [lax.index_in_dim(vecs, 1, axis, False), lax.index_in_dim(vecs, 0, axis, False)], axis
    )
    return real_rows, imag_rows


def signed_rows(vecs):
    real_rows, imag_rows = split_signs(vecs, 1)
    return jnp.stack([real_rows, imag_rows], axis=1)


def inverse_apply(pivot_inv, vecs):
    return jnp.einsum(
        "qocnk,qcjk->qonj", signed_rows(vecs), pivot_inv, precision=sweep_precision
    )


def couple_down(coupling_blk, vecs):
    return jnp.einsum("qcnk,kj->qcnj", vecs, coupling_blk, precision=sweep_precision)


def couple_up(coupling_blk, vecs):
    return jnp.einsum("qcnk,jk->qcnj", vecs, coupling_blk, precision=sweep_precision)


def sweep_forward(pivots, couple, start_rows, source, rhs_rows, store_all):
    blocks_dev = couple.shape[0]

    def advance(carried, position):
        pivot_inv = lax.dynamic_index_in_dim(pivots, position, 1, keepdims=False)
        coupling_blk = lax.dynamic_index_in_dim(couple, position, 0, keepdims=False)
        combined = carried
        if source is not None:
            rhs_block = lax.dynamic_index_in_dim(source, position, 0, keepdims=False)
            rhs_full = jnp.stack([rhs_block, jnp.zeros_like(rhs_block)])
            rhs_full = jnp.broadcast_to(rhs_full[None], (combined.shape[0],) + rhs_full.shape)
            combined = combined.at[:, :, rhs_rows:].add(rhs_full)
        solved = inverse_apply(pivot_inv, combined)
        return (couple_down(coupling_blk, solved), solved if store_all else None)

    return lax.scan(advance, start_rows, jnp.arange(blocks_dev))


def sweep_backward(pivots, couple, start_rows, solved_all, rhs_rows, store_all):
    blocks_dev = couple.shape[0]

    def retreat(carried, position):
        pivot_inv = lax.dynamic_index_in_dim(pivots, position, 1, keepdims=False)
        coupling_blk = lax.dynamic_index_in_dim(couple, position, 0, keepdims=False)
        correction = inverse_apply(pivot_inv, couple_up(coupling_blk, carried))
        if solved_all is not None:
            known = lax.dynamic_index_in_dim(solved_all, position, 0, keepdims=False)
            correction = correction.at[:, :, rhs_rows:].add(known)
        return (correction, correction if store_all else None)

    return lax.scan(retreat, start_rows, jnp.arange(blocks_dev), reverse=True)


def block_real(matrix):
    top = jnp.concatenate([matrix[:, 0], matrix[:, 1]], axis=2)
    bottom = jnp.concatenate([-matrix[:, 1], matrix[:, 0]], axis=2)
    return jnp.concatenate([top, bottom], axis=1)


def flat_rows(vecs):
    return jnp.concatenate([vecs[:, 0], vecs[:, 1]], axis=2)


def unflat_rows(flat, width):
    return jnp.stack([flat[..., :width], flat[..., width:]], axis=1)


def right_apply(vecs, matrix):
    return jnp.einsum("qocnk,qckj->qonj", signed_rows(vecs), matrix, precision=highest)


def right_apply_all(vecs, states):
    return jnp.einsum("qocnk,rqckj->rqonj", signed_rows(vecs), states, precision=highest)


def pipelined_chain(maps, tips, pairs, depth, stages, active=True):
    points = tips.shape[0]

    def step(stage, inbox):
        point = jnp.clip(stage - depth, 0, points - 1)
        rows = lax.dynamic_index_in_dim(inbox, point, 0, keepdims=False)

        def hop():
            return jnp.dot(
                rows,
                lax.dynamic_index_in_dim(maps, point, 0, keepdims=False),
                precision=hop_precision,
            ) + lax.dynamic_index_in_dim(tips, point, 0, keepdims=False)

        out = lax.cond(active, hop, lambda: jnp.zeros_like(rows))
        got = lax.ppermute(out, "chain", pairs)
        slot = stage + 1 - depth
        keep = (slot >= 0) & (slot < points)
        slot = jnp.clip(slot, 0, points - 1)
        current = lax.dynamic_index_in_dim(inbox, slot, 0, keepdims=False)
        return lax.dynamic_update_index_in_dim(inbox, jnp.where(keep, got, current), slot, 0)

    return lax.fori_loop(0, stages, step, jnp.zeros_like(tips))


def chain_incoming(own_both, width, by):
    own_map = own_both[:, :, :width]
    own_tip = own_both[:, :, width:]
    points = own_tip.shape[0]
    peers = lax.axis_size("chain")
    rank = lax.axis_index("chain")
    if peers % 2:
        depth = rank if by > 0 else peers - 1 - rank
        pairs = [(i, i + by) for i in range(peers) if 0 <= i + by < peers]
        inbox = pipelined_chain(
            block_real(own_map), flat_rows(own_tip), pairs, depth, peers + points - 2
        )
        return unflat_rows(inbox, width)
    halves = peers // 2
    lead = 0 if by > 0 else 1
    node = 1 - lead
    to_node = [(2 * j + lead, 2 * j + node) for j in range(halves)]
    to_lead = [(2 * j + node, 2 * j + lead) for j in range(halves)]
    prev_both = lax.ppermute(own_both, "chain", to_node)
    prev_map = prev_both[:, :, :width]
    prev_tip = prev_both[:, :, width:]
    is_node = rank % 2 == node

    def compose():
        pair_both = right_apply(prev_both, own_map)
        pair_tip = pair_both[:, :, width:] + own_tip
        return block_real(pair_both[:, :, :width]), flat_rows(pair_tip)

    def idle():
        return (
            jnp.zeros((points, 2 * width, 2 * width), jnp.float32),
            jnp.zeros(own_tip.shape[:1] + own_tip.shape[2:3] + (2 * width,), jnp.float32),
        )

    pair_maps, pair_tips = lax.cond(is_node, compose, idle)
    pair_rank = rank // 2
    depth = pair_rank if by > 0 else halves - 1 - pair_rank
    pairs = [
        (2 * j + node, 2 * (j + by) + node) for j in range(halves) if 0 <= j + by < halves
    ]
    inbox = pipelined_chain(pair_maps, pair_tips, pairs, depth, halves + points - 2, is_node)
    node_in = unflat_rows(inbox, width)
    lead_in = lax.ppermute(node_in, "chain", to_lead)
    node_own = right_apply(node_in, prev_map) + prev_tip
    return jnp.where(is_node, node_own, lead_in)


def shards(subspace, s_inv, couple, diag_blocks, weights):
    points = s_inv.shape[0]
    blocks_dev = couple.shape[0]
    block_width = couple.shape[1]
    vectors = subspace.shape[0]
    source = subspace.reshape(vectors, blocks_dev, block_width).transpose(1, 0, 2)
    zero_rows = jnp.zeros((points, 2, vectors, block_width), jnp.float32)
    plain_eye = jnp.stack(
        [
            jnp.eye(block_width, dtype=jnp.float32),
            jnp.zeros((block_width, block_width), jnp.float32),
        ]
    )
    identity_map = jnp.broadcast_to(plain_eye, (points, 2, block_width, block_width))
    chain_size = lax.axis_size("chain")

    forward_start = jnp.concatenate([identity_map, zero_rows], axis=2)
    forward_both, forward_states = sweep_forward(
        s_inv, couple, forward_start, source, block_width, True
    )
    incoming = chain_incoming(forward_both, block_width, 1)
    solved_all = forward_states[:, :, :, block_width:] + right_apply_all(
        incoming, forward_states[:, :, :, :block_width]
    )

    backward_start = jnp.concatenate([identity_map, zero_rows], axis=2)
    backward_both, backward_all = sweep_backward(
        s_inv, couple, backward_start, solved_all, block_width, True
    )
    outgoing = chain_incoming(backward_both, block_width, -1)
    result = backward_all[:, :, :, block_width:] + right_apply_all(
        outgoing, backward_all[:, :, :, :block_width]
    )

    signed = weights * jnp.array([1.0, -1.0], jnp.float32)
    filtered_blocks = jnp.einsum("rqcnk,qc->rnk", result, signed, precision=highest)
    down_all = jnp.einsum("rnk,rkj->rnj", filtered_blocks, couple, precision=highest)
    from_next = passed_along(filtered_blocks[0], "chain", -1)
    from_prior = passed_along(down_all[-1], "chain", 1)
    diag_term = jnp.einsum("rnk,rjk->rnj", filtered_blocks, diag_blocks, precision=highest)
    upper_rows = jnp.concatenate([filtered_blocks[1:], from_next[None]], axis=0)
    term_up = jnp.einsum("rnk,rjk->rnj", upper_rows, couple, precision=highest)
    lower_rows = jnp.concatenate([from_prior[None], down_all[:-1]], axis=0)
    applied_blocks = diag_term + term_up + lower_rows
    gram_plain = jnp.einsum("rnk,rmk->nm", filtered_blocks, filtered_blocks, precision=highest)
    gram_matrix = jnp.einsum("rnk,rmk->nm", filtered_blocks, applied_blocks, precision=highest)
    summed = chain_sum(jnp.stack([gram_plain, gram_matrix]), "chain")
    grams = summed / (blocks_dev * block_width * chain_size)
    filtered = filtered_blocks.transpose(1, 0, 2).reshape(vectors, blocks_dev * block_width)
    applied = applied_blocks.transpose(1, 0, 2).reshape(vectors, blocks_dev * block_width)
    return (filtered, applied, grams)


def solution(mesh):
    placed = (
        P("parts", "chain"),
        P("parts", "chain", None, None, None),
        P("chain", "parts", None),
        P("chain", "parts", None),
        P("parts", None),
    )
    return jax.shard_map(
        shards,
        mesh=mesh,
        in_specs=placed,
        out_specs=(P("parts", "chain"), P("parts", "chain"), P(None, "parts", None)),
        check_vma=False,
    )
```

```python
import jax
import jax.numpy as jnp
from jax import lax
from jax.sharding import PartitionSpec as P

highest = lax.Precision.HIGHEST
sweep_precision = lax.Precision.HIGHEST
hop_precision = lax.Precision.HIGHEST


def passed_along(shard, axis, by):
    peers = lax.axis_size(axis)
    pairs = [(i, i + by) for i in range(peers) if 0 <= i + by < peers]
    return lax.ppermute(shard, axis, pairs)


def chain_sum(value, axis):
    peers = lax.axis_size(axis)
    if peers & (peers - 1):
        return lax.psum(value, axis)
    stride = 1
    while stride < peers:
        value = value + lax.ppermute(value, axis, [(i, i ^ stride) for i in range(peers)])
        stride *= 2
    return value


def split_signs(vecs, axis):
    real_rows = jnp.stack(
        [lax.index_in_dim(vecs, 0, axis, False), -lax.index_in_dim(vecs, 1, axis, False)], axis
    )
    imag_rows = jnp.stack(
        [lax.index_in_dim(vecs, 1, axis, False), lax.index_in_dim(vecs, 0, axis, False)], axis
    )
    return real_rows, imag_rows


def signed_rows(vecs):
    real_rows, imag_rows = split_signs(vecs, 1)
    return jnp.stack([real_rows, imag_rows], axis=1)


def inverse_apply(pivot_inv, vecs):
    return jnp.einsum(
        "qocnk,qcjk->qonj", signed_rows(vecs), pivot_inv, precision=sweep_precision
    )


def couple_down(coupling_blk, vecs):
    return jnp.einsum("qcnk,kj->qcnj", vecs, coupling_blk, precision=sweep_precision)


def couple_up(coupling_blk, vecs):
    return jnp.einsum("qcnk,jk->qcnj", vecs, coupling_blk, precision=sweep_precision)


def sweep_forward(pivots, couple, start_rows, source, rhs_rows, store_all, first=0):
    blocks_dev = couple.shape[0]

    def advance(carried, position):
        pivot_inv = lax.dynamic_index_in_dim(pivots, position, 1, keepdims=False)
        coupling_blk = lax.dynamic_index_in_dim(couple, position, 0, keepdims=False)
        combined = carried
        if source is not None:
            rhs_block = lax.dynamic_index_in_dim(source, position, 0, keepdims=False)
            rhs_full = jnp.stack([rhs_block, jnp.zeros_like(rhs_block)])
            rhs_full = jnp.broadcast_to(rhs_full[None], (combined.shape[0],) + rhs_full.shape)
            combined = combined.at[:, :, rhs_rows:].add(rhs_full)
        solved = inverse_apply(pivot_inv, combined)
        return (couple_down(coupling_blk, solved), solved if store_all else None)

    return lax.scan(advance, start_rows, jnp.arange(first, blocks_dev))


def sweep_backward(pivots, couple, start_rows, solved_all, rhs_rows, store_all):
    blocks_dev = couple.shape[0]

    def retreat(carried, position):
        pivot_inv = lax.dynamic_index_in_dim(pivots, position, 1, keepdims=False)
        coupling_blk = lax.dynamic_index_in_dim(couple, position, 0, keepdims=False)
        correction = inverse_apply(pivot_inv, couple_up(coupling_blk, carried))
        if solved_all is not None:
            known = lax.dynamic_index_in_dim(solved_all, position, 0, keepdims=False)
            correction = correction.at[:, :, rhs_rows:].add(known)
        return (correction, correction if store_all else None)

    return lax.scan(retreat, start_rows, jnp.arange(blocks_dev), reverse=True)


def block_real(matrix):
    top = jnp.concatenate([matrix[:, 0], matrix[:, 1]], axis=2)
    bottom = jnp.concatenate([-matrix[:, 1], matrix[:, 0]], axis=2)
    return jnp.concatenate([top, bottom], axis=1)


def flat_rows(vecs):
    return jnp.concatenate([vecs[:, 0], vecs[:, 1]], axis=2)


def unflat_rows(flat, width):
    return jnp.stack([flat[..., :width], flat[..., width:]], axis=1)


def right_apply(vecs, matrix):
    return jnp.einsum("qocnk,qckj->qonj", signed_rows(vecs), matrix, precision=highest)


def right_apply_all(vecs, states):
    return jnp.einsum("qocnk,rqckj->rqonj", signed_rows(vecs), states, precision=highest)


def pipelined_chain(maps, tips, pairs, depth, stages, active=True):
    points = tips.shape[0]

    def step(stage, inbox):
        point = jnp.clip(stage - depth, 0, points - 1)
        rows = lax.dynamic_index_in_dim(inbox, point, 0, keepdims=False)

        def hop():
            return jnp.dot(
                rows,
                lax.dynamic_index_in_dim(maps, point, 0, keepdims=False),
                precision=hop_precision,
            ) + lax.dynamic_index_in_dim(tips, point, 0, keepdims=False)

        out = lax.cond(active, hop, lambda: jnp.zeros_like(rows))
        got = lax.ppermute(out, "chain", pairs)
        slot = stage + 1 - depth
        keep = (slot >= 0) & (slot < points)
        slot = jnp.clip(slot, 0, points - 1)
        current = lax.dynamic_index_in_dim(inbox, slot, 0, keepdims=False)
        return lax.dynamic_update_index_in_dim(inbox, jnp.where(keep, got, current), slot, 0)

    return lax.fori_loop(0, stages, step, jnp.zeros_like(tips))


def chain_incoming(own_both, width, by):
    own_map = own_both[:, :, :width]
    own_tip = own_both[:, :, width:]
    points = own_tip.shape[0]
    peers = lax.axis_size("chain")
    rank = lax.axis_index("chain")
    if peers % 2:
        depth = rank if by > 0 else peers - 1 - rank
        pairs = [(i, i + by) for i in range(peers) if 0 <= i + by < peers]
        inbox = pipelined_chain(
            block_real(own_map), flat_rows(own_tip), pairs, depth, peers + points - 2
        )
        return unflat_rows(inbox, width)
    halves = peers // 2
    lead = 0 if by > 0 else 1
    node = 1 - lead
    to_node = [(2 * j + lead, 2 * j + node) for j in range(halves)]
    to_lead = [(2 * j + node, 2 * j + lead) for j in range(halves)]
    prev_both = lax.ppermute(own_both, "chain", to_node)
    prev_map = prev_both[:, :, :width]
    prev_tip = prev_both[:, :, width:]
    is_node = rank % 2 == node

    def compose():
        pair_both = right_apply(prev_both, own_map)
        pair_tip = pair_both[:, :, width:] + own_tip
        return block_real(pair_both[:, :, :width]), flat_rows(pair_tip)

    def idle():
        return (
            jnp.zeros((points, 2 * width, 2 * width), jnp.float32),
            jnp.zeros(own_tip.shape[:1] + own_tip.shape[2:3] + (2 * width,), jnp.float32),
        )

    pair_maps, pair_tips = lax.cond(is_node, compose, idle)
    pair_rank = rank // 2
    depth = pair_rank if by > 0 else halves - 1 - pair_rank
    pairs = [
        (2 * j + node, 2 * (j + by) + node) for j in range(halves) if 0 <= j + by < halves
    ]
    inbox = pipelined_chain(pair_maps, pair_tips, pairs, depth, halves + points - 2, is_node)
    node_in = unflat_rows(inbox, width)
    lead_in = lax.ppermute(node_in, "chain", to_lead)
    node_own = right_apply(node_in, prev_map) + prev_tip
    return jnp.where(is_node, node_own, lead_in)


def shards(subspace, s_inv, couple, diag_blocks, weights):
    points = s_inv.shape[0]
    blocks_dev = couple.shape[0]
    block_width = couple.shape[1]
    vectors = subspace.shape[0]
    source = subspace.reshape(vectors, blocks_dev, block_width).transpose(1, 0, 2)
    zero_rows = jnp.zeros((points, 2, vectors, block_width), jnp.float32)
    plain_eye = jnp.stack(
        [
            jnp.eye(block_width, dtype=jnp.float32),
            jnp.zeros((block_width, block_width), jnp.float32),
        ]
    )
    identity_map = jnp.broadcast_to(plain_eye, (points, 2, block_width, block_width))
    chain_size = lax.axis_size("chain")

    forward_start = jnp.concatenate([identity_map, zero_rows], axis=2)
    first_pivot = s_inv[:, 0]
    first_rhs = jnp.broadcast_to(
        jnp.stack([source[0], jnp.zeros_like(source[0])])[None], zero_rows.shape
    )
    first_solved = jnp.concatenate(
        [jnp.swapaxes(first_pivot, -1, -2), inverse_apply(first_pivot, first_rhs)], axis=2
    )
    forward_both, rest_states = sweep_forward(
        s_inv, couple, couple_down(couple[0], first_solved), source, block_width, True, 1
    )
    forward_states = jnp.concatenate([first_solved[None], rest_states], axis=0)
    incoming = chain_incoming(forward_both, block_width, 1)
    solved_all = forward_states[:, :, :, block_width:] + right_apply_all(
        incoming, forward_states[:, :, :, :block_width]
    )

    backward_start = jnp.concatenate([identity_map, zero_rows], axis=2)
    backward_both, backward_all = sweep_backward(
        s_inv, couple, backward_start, solved_all, block_width, True
    )
    outgoing = chain_incoming(backward_both, block_width, -1)
    result = backward_all[:, :, :, block_width:] + right_apply_all(
        outgoing, backward_all[:, :, :, :block_width]
    )

    signed = weights * jnp.array([1.0, -1.0], jnp.float32)
    filtered_blocks = jnp.einsum("rqcnk,qc->rnk", result, signed, precision=highest)
    down_all = jnp.einsum("rnk,rkj->rnj", filtered_blocks, couple, precision=highest)
    from_next = passed_along(filtered_blocks[0], "chain", -1)
    from_prior = passed_along(down_all[-1], "chain", 1)
    diag_term = jnp.einsum("rnk,rjk->rnj", filtered_blocks, diag_blocks, precision=highest)
    upper_rows = jnp.concatenate([filtered_blocks[1:], from_next[None]], axis=0)
    term_up = jnp.einsum("rnk,rjk->rnj", upper_rows, couple, precision=highest)
    lower_rows = jnp.concatenate([from_prior[None], down_all[:-1]], axis=0)
    applied_blocks = diag_term + term_up + lower_rows
    gram_plain = jnp.einsum("rnk,rmk->nm", filtered_blocks, filtered_blocks, precision=highest)
    gram_matrix = jnp.einsum("rnk,rmk->nm", filtered_blocks, applied_blocks, precision=highest)
    summed = chain_sum(jnp.stack([gram_plain, gram_matrix]), "chain")
    grams = summed / (blocks_dev * block_width * chain_size)
    filtered = filtered_blocks.transpose(1, 0, 2).reshape(vectors, blocks_dev * block_width)
    applied = applied_blocks.transpose(1, 0, 2).reshape(vectors, blocks_dev * block_width)
    return (filtered, applied, grams)


def solution(mesh):
    placed = (
        P("parts", "chain"),
        P("parts", "chain", None, None, None),
        P("chain", "parts", None),
        P("chain", "parts", None),
        P("parts", None),
    )
    return jax.shard_map(
        shards,
        mesh=mesh,
        in_specs=placed,
        out_specs=(P("parts", "chain"), P("parts", "chain"), P(None, "parts", None)),
        check_vma=False,
    )
```

```python
import jax
import jax.numpy as jnp
from jax import lax
from jax.sharding import PartitionSpec as P

highest = lax.Precision.HIGHEST
sweep_precision = lax.Precision.HIGHEST
hop_precision = lax.Precision.HIGHEST


def passed_along(shard, axis, by):
    peers = lax.axis_size(axis)
    pairs = [(i, i + by) for i in range(peers) if 0 <= i + by < peers]
    return lax.ppermute(shard, axis, pairs)


def chain_sum(value, axis):
    peers = lax.axis_size(axis)
    if peers & (peers - 1):
        return lax.psum(value, axis)
    stride = 1
    while stride < peers:
        value = value + lax.ppermute(value, axis, [(i, i ^ stride) for i in range(peers)])
        stride *= 2
    return value


def split_signs(vecs, axis):
    real_rows = jnp.stack(
        [lax.index_in_dim(vecs, 0, axis, False), -lax.index_in_dim(vecs, 1, axis, False)], axis
    )
    imag_rows = jnp.stack(
        [lax.index_in_dim(vecs, 1, axis, False), lax.index_in_dim(vecs, 0, axis, False)], axis
    )
    return real_rows, imag_rows


def signed_rows(vecs):
    real_rows, imag_rows = split_signs(vecs, 1)
    return jnp.stack([real_rows, imag_rows], axis=1)


def inverse_apply(pivot_inv, vecs):
    return jnp.einsum(
        "qocnk,qcjk->qonj", signed_rows(vecs), pivot_inv, precision=sweep_precision
    )


def couple_down(coupling_blk, vecs):
    return jnp.einsum("qcnk,kj->qcnj", vecs, coupling_blk, precision=sweep_precision)


def couple_up(coupling_blk, vecs):
    return jnp.einsum("qcnk,jk->qcnj", vecs, coupling_blk, precision=sweep_precision)


def sweep_forward(pivots, couple, start_rows, source, rhs_rows, store_all, first=0):
    blocks_dev = couple.shape[0]

    def advance(carried, position):
        pivot_inv = lax.dynamic_index_in_dim(pivots, position, 1, keepdims=False)
        coupling_blk = lax.dynamic_index_in_dim(couple, position, 0, keepdims=False)
        combined = carried
        if source is not None:
            rhs_block = lax.dynamic_index_in_dim(source, position, 0, keepdims=False)
            rhs_full = jnp.stack([rhs_block, jnp.zeros_like(rhs_block)])
            rhs_full = jnp.broadcast_to(rhs_full[None], (combined.shape[0],) + rhs_full.shape)
            combined = combined.at[:, :, rhs_rows:].add(rhs_full)
        solved = inverse_apply(pivot_inv, combined)
        return (couple_down(coupling_blk, solved), solved if store_all else None)

    return lax.scan(advance, start_rows, jnp.arange(first, blocks_dev))


def sweep_backward(pivots, couple, start_rows, solved_all, rhs_rows, store_all, upto=None):
    blocks_dev = couple.shape[0] if upto is None else upto

    def retreat(carried, position):
        pivot_inv = lax.dynamic_index_in_dim(pivots, position, 1, keepdims=False)
        coupling_blk = lax.dynamic_index_in_dim(couple, position, 0, keepdims=False)
        correction = inverse_apply(pivot_inv, couple_up(coupling_blk, carried))
        if solved_all is not None:
            known = lax.dynamic_index_in_dim(solved_all, position, 0, keepdims=False)
            correction = correction.at[:, :, rhs_rows:].add(known)
        return (correction, correction if store_all else None)

    return lax.scan(retreat, start_rows, jnp.arange(blocks_dev), reverse=True)


def block_real(matrix):
    top = jnp.concatenate([matrix[:, 0], matrix[:, 1]], axis=2)
    bottom = jnp.concatenate([-matrix[:, 1], matrix[:, 0]], axis=2)
    return jnp.concatenate([top, bottom], axis=1)


def flat_rows(vecs):
    return jnp.concatenate([vecs[:, 0], vecs[:, 1]], axis=2)


def unflat_rows(flat, width):
    return jnp.stack([flat[..., :width], flat[..., width:]], axis=1)


def right_apply(vecs, matrix):
    return jnp.einsum("qocnk,qckj->qonj", signed_rows(vecs), matrix, precision=highest)


def right_apply_all(vecs, states):
    return jnp.einsum("qocnk,rqckj->rqonj", signed_rows(vecs), states, precision=highest)


def pipelined_chain(maps, tips, pairs, depth, stages, active=True):
    points = tips.shape[0]

    def step(stage, inbox):
        point = jnp.clip(stage - depth, 0, points - 1)
        rows = lax.dynamic_index_in_dim(inbox, point, 0, keepdims=False)

        def hop():
            return jnp.dot(
                rows,
                lax.dynamic_index_in_dim(maps, point, 0, keepdims=False),
                precision=hop_precision,
            ) + lax.dynamic_index_in_dim(tips, point, 0, keepdims=False)

        out = lax.cond(active, hop, lambda: jnp.zeros_like(rows))
        got = lax.ppermute(out, "chain", pairs)
        slot = stage + 1 - depth
        keep = (slot >= 0) & (slot < points)
        slot = jnp.clip(slot, 0, points - 1)
        current = lax.dynamic_index_in_dim(inbox, slot, 0, keepdims=False)
        return lax.dynamic_update_index_in_dim(inbox, jnp.where(keep, got, current), slot, 0)

    return lax.fori_loop(0, stages, step, jnp.zeros_like(tips))


def chain_incoming(own_both, width, by):
    own_map = own_both[:, :, :width]
    own_tip = own_both[:, :, width:]
    points = own_tip.shape[0]
    peers = lax.axis_size("chain")
    rank = lax.axis_index("chain")
    if peers % 2:
        depth = rank if by > 0 else peers - 1 - rank
        pairs = [(i, i + by) for i in range(peers) if 0 <= i + by < peers]
        inbox = pipelined_chain(
            block_real(own_map), flat_rows(own_tip), pairs, depth, peers + points - 2
        )
        return unflat_rows(inbox, width)
    halves = peers // 2
    lead = 0 if by > 0 else 1
    node = 1 - lead
    to_node = [(2 * j + lead, 2 * j + node) for j in range(halves)]
    to_lead = [(2 * j + node, 2 * j + lead) for j in range(halves)]
    prev_both = lax.ppermute(own_both, "chain", to_node)
    prev_map = prev_both[:, :, :width]
    prev_tip = prev_both[:, :, width:]
    is_node = rank % 2 == node

    def compose():
        pair_both = right_apply(prev_both, own_map)
        pair_tip = pair_both[:, :, width:] + own_tip
        return block_real(pair_both[:, :, :width]), flat_rows(pair_tip)

    def idle():
        return (
            jnp.zeros((points, 2 * width, 2 * width), jnp.float32),
            jnp.zeros(own_tip.shape[:1] + own_tip.shape[2:3] + (2 * width,), jnp.float32),
        )

    pair_maps, pair_tips = lax.cond(is_node, compose, idle)
    pair_rank = rank // 2
    depth = pair_rank if by > 0 else halves - 1 - pair_rank
    pairs = [
        (2 * j + node, 2 * (j + by) + node) for j in range(halves) if 0 <= j + by < halves
    ]
    inbox = pipelined_chain(pair_maps, pair_tips, pairs, depth, halves + points - 2, is_node)
    node_in = unflat_rows(inbox, width)
    lead_in = lax.ppermute(node_in, "chain", to_lead)
    node_own = right_apply(node_in, prev_map) + prev_tip
    return jnp.where(is_node, node_own, lead_in)


def shards(subspace, s_inv, couple, diag_blocks, weights):
    points = s_inv.shape[0]
    blocks_dev = couple.shape[0]
    block_width = couple.shape[1]
    vectors = subspace.shape[0]
    source = subspace.reshape(vectors, blocks_dev, block_width).transpose(1, 0, 2)
    zero_rows = jnp.zeros((points, 2, vectors, block_width), jnp.float32)
    plain_eye = jnp.stack(
        [
            jnp.eye(block_width, dtype=jnp.float32),
            jnp.zeros((block_width, block_width), jnp.float32),
        ]
    )
    identity_map = jnp.broadcast_to(plain_eye, (points, 2, block_width, block_width))
    chain_size = lax.axis_size("chain")

    forward_start = jnp.concatenate([identity_map, zero_rows], axis=2)
    first_pivot = s_inv[:, 0]
    first_rhs = jnp.broadcast_to(
        jnp.stack([source[0], jnp.zeros_like(source[0])])[None], zero_rows.shape
    )
    first_solved = jnp.concatenate(
        [jnp.swapaxes(first_pivot, -1, -2), inverse_apply(first_pivot, first_rhs)], axis=2
    )
    forward_both, rest_states = sweep_forward(
        s_inv, couple, couple_down(couple[0], first_solved), source, block_width, True, 1
    )
    forward_states = jnp.concatenate([first_solved[None], rest_states], axis=0)
    incoming = chain_incoming(forward_both, block_width, 1)
    solved_all = forward_states[:, :, :, block_width:] + right_apply_all(
        incoming, forward_states[:, :, :, :block_width]
    )

    last = blocks_dev - 1
    last_coupled = jnp.broadcast_to(
        jnp.stack([couple[last].T, jnp.zeros_like(couple[last])])[None], identity_map.shape
    )
    last_rows = jnp.concatenate(
        [inverse_apply(s_inv[:, last], last_coupled), solved_all[last]], axis=2
    )
    backward_both, rest_all = sweep_backward(
        s_inv, couple, last_rows, solved_all, block_width, True, last
    )
    backward_all = jnp.concatenate([rest_all, last_rows[None]], axis=0)
    outgoing = chain_incoming(backward_both, block_width, -1)
    result = backward_all[:, :, :, block_width:] + right_apply_all(
        outgoing, backward_all[:, :, :, :block_width]
    )

    signed = weights * jnp.array([1.0, -1.0], jnp.float32)
    filtered_blocks = jnp.einsum("rqcnk,qc->rnk", result, signed, precision=highest)
    down_all = jnp.einsum("rnk,rkj->rnj", filtered_blocks, couple, precision=highest)
    from_next = passed_along(filtered_blocks[0], "chain", -1)
    from_prior = passed_along(down_all[-1], "chain", 1)
    diag_term = jnp.einsum("rnk,rjk->rnj", filtered_blocks, diag_blocks, precision=highest)
    upper_rows = jnp.concatenate([filtered_blocks[1:], from_next[None]], axis=0)
    term_up = jnp.einsum("rnk,rjk->rnj", upper_rows, couple, precision=highest)
    lower_rows = jnp.concatenate([from_prior[None], down_all[:-1]], axis=0)
    applied_blocks = diag_term + term_up + lower_rows
    gram_plain = jnp.einsum("rnk,rmk->nm", filtered_blocks, filtered_blocks, precision=highest)
    gram_matrix = jnp.einsum("rnk,rmk->nm", filtered_blocks, applied_blocks, precision=highest)
    summed = chain_sum(jnp.stack([gram_plain, gram_matrix]), "chain")
    grams = summed / (blocks_dev * block_width * chain_size)
    filtered = filtered_blocks.transpose(1, 0, 2).reshape(vectors, blocks_dev * block_width)
    applied = applied_blocks.transpose(1, 0, 2).reshape(vectors, blocks_dev * block_width)
    return (filtered, applied, grams)


def solution(mesh):
    placed = (
        P("parts", "chain"),
        P("parts", "chain", None, None, None),
        P("chain", "parts", None),
        P("chain", "parts", None),
        P("parts", None),
    )
    return jax.shard_map(
        shards,
        mesh=mesh,
        in_specs=placed,
        out_specs=(P("parts", "chain"), P("parts", "chain"), P(None, "parts", None)),
        check_vma=False,
    )
```

```python
import jax
import jax.numpy as jnp
from jax import lax
from jax.sharding import PartitionSpec as P

highest = lax.Precision.HIGHEST
sweep_precision = lax.Precision.HIGHEST
hop_precision = lax.Precision.HIGHEST


def passed_along(shard, axis, by):
    peers = lax.axis_size(axis)
    pairs = [(i, i + by) for i in range(peers) if 0 <= i + by < peers]
    return lax.ppermute(shard, axis, pairs)


def chain_sum(value, axis):
    peers = lax.axis_size(axis)
    if peers & (peers - 1):
        return lax.psum(value, axis)
    stride = 1
    while stride < peers:
        value = value + lax.ppermute(value, axis, [(i, i ^ stride) for i in range(peers)])
        stride *= 2
    return value


def split_signs(vecs, axis):
    real_rows = jnp.stack(
        [lax.index_in_dim(vecs, 0, axis, False), -lax.index_in_dim(vecs, 1, axis, False)], axis
    )
    imag_rows = jnp.stack(
        [lax.index_in_dim(vecs, 1, axis, False), lax.index_in_dim(vecs, 0, axis, False)], axis
    )
    return real_rows, imag_rows


def signed_rows(vecs):
    real_rows, imag_rows = split_signs(vecs, 1)
    return jnp.stack([real_rows, imag_rows], axis=1)


def inverse_apply(pivot_inv, vecs):
    return jnp.einsum(
        "qocnk,qcjk->qonj", signed_rows(vecs), pivot_inv, precision=sweep_precision
    )


def couple_down(coupling_blk, vecs):
    return jnp.einsum("qcnk,kj->qcnj", vecs, coupling_blk, precision=sweep_precision)


def couple_up(coupling_blk, vecs):
    return jnp.einsum("qcnk,jk->qcnj", vecs, coupling_blk, precision=sweep_precision)


def sweep_forward(pivots, couple, start_rows, source, rhs_rows, store_all, first=0):
    blocks_dev = couple.shape[0]

    def advance(carried, position):
        pivot_inv = lax.dynamic_index_in_dim(pivots, position, 1, keepdims=False)
        coupling_blk = lax.dynamic_index_in_dim(couple, position, 0, keepdims=False)
        combined = carried
        if source is not None:
            rhs_block = lax.dynamic_index_in_dim(source, position, 0, keepdims=False)
            rhs_full = jnp.stack([rhs_block, jnp.zeros_like(rhs_block)])
            rhs_full = jnp.broadcast_to(rhs_full[None], (combined.shape[0],) + rhs_full.shape)
            combined = combined.at[:, :, rhs_rows:].add(rhs_full)
        solved = inverse_apply(pivot_inv, combined)
        return (couple_down(coupling_blk, solved), solved if store_all else None)

    return lax.scan(advance, start_rows, jnp.arange(first, blocks_dev), unroll=True)


def sweep_backward(pivots, couple, start_rows, solved_all, rhs_rows, store_all):
    blocks_dev = couple.shape[0]

    def retreat(carried, position):
        pivot_inv = lax.dynamic_index_in_dim(pivots, position, 1, keepdims=False)
        coupling_blk = lax.dynamic_index_in_dim(couple, position, 0, keepdims=False)
        correction = inverse_apply(pivot_inv, couple_up(coupling_blk, carried))
        if solved_all is not None:
            known = lax.dynamic_index_in_dim(solved_all, position, 0, keepdims=False)
            correction = correction.at[:, :, rhs_rows:].add(known)
        return (correction, correction if store_all else None)

    return lax.scan(retreat, start_rows, jnp.arange(blocks_dev), reverse=True, unroll=True)


def block_real(matrix):
    top = jnp.concatenate([matrix[:, 0], matrix[:, 1]], axis=2)
    bottom = jnp.concatenate([-matrix[:, 1], matrix[:, 0]], axis=2)
    return jnp.concatenate([top, bottom], axis=1)


def flat_rows(vecs):
    return jnp.concatenate([vecs[:, 0], vecs[:, 1]], axis=2)


def unflat_rows(flat, width):
    return jnp.stack([flat[..., :width], flat[..., width:]], axis=1)


def right_apply(vecs, matrix):
    return jnp.einsum("qocnk,qckj->qonj", signed_rows(vecs), matrix, precision=highest)


def right_apply_all(vecs, states):
    return jnp.einsum("qocnk,rqckj->rqonj", signed_rows(vecs), states, precision=highest)


def pipelined_chain(maps, tips, pairs, depth, stages, active=True):
    points = tips.shape[0]

    def step(stage, inbox):
        point = jnp.clip(stage - depth, 0, points - 1)
        rows = lax.dynamic_index_in_dim(inbox, point, 0, keepdims=False)

        def hop():
            return jnp.dot(
                rows,
                lax.dynamic_index_in_dim(maps, point, 0, keepdims=False),
                precision=hop_precision,
            ) + lax.dynamic_index_in_dim(tips, point, 0, keepdims=False)

        out = lax.cond(active, hop, lambda: jnp.zeros_like(rows))
        got = lax.ppermute(out, "chain", pairs)
        slot = stage + 1 - depth
        keep = (slot >= 0) & (slot < points)
        slot = jnp.clip(slot, 0, points - 1)
        current = lax.dynamic_index_in_dim(inbox, slot, 0, keepdims=False)
        return lax.dynamic_update_index_in_dim(inbox, jnp.where(keep, got, current), slot, 0)

    return lax.fori_loop(0, stages, step, jnp.zeros_like(tips))


def chain_incoming(own_both, width, by):
    own_map = own_both[:, :, :width]
    own_tip = own_both[:, :, width:]
    points = own_tip.shape[0]
    peers = lax.axis_size("chain")
    rank = lax.axis_index("chain")
    if peers % 2:
        depth = rank if by > 0 else peers - 1 - rank
        pairs = [(i, i + by) for i in range(peers) if 0 <= i + by < peers]
        inbox = pipelined_chain(
            block_real(own_map), flat_rows(own_tip), pairs, depth, peers + points - 2
        )
        return unflat_rows(inbox, width)
    halves = peers // 2
    lead = 0 if by > 0 else 1
    node = 1 - lead
    to_node = [(2 * j + lead, 2 * j + node) for j in range(halves)]
    to_lead = [(2 * j + node, 2 * j + lead) for j in range(halves)]
    prev_both = lax.ppermute(own_both, "chain", to_node)
    prev_map = prev_both[:, :, :width]
    prev_tip = prev_both[:, :, width:]
    is_node = rank % 2 == node

    def compose():
        pair_both = right_apply(prev_both, own_map)
        pair_tip = pair_both[:, :, width:] + own_tip
        return block_real(pair_both[:, :, :width]), flat_rows(pair_tip)

    def idle():
        return (
            jnp.zeros((points, 2 * width, 2 * width), jnp.float32),
            jnp.zeros(own_tip.shape[:1] + own_tip.shape[2:3] + (2 * width,), jnp.float32),
        )

    pair_maps, pair_tips = lax.cond(is_node, compose, idle)
    pair_rank = rank // 2
    depth = pair_rank if by > 0 else halves - 1 - pair_rank
    pairs = [
        (2 * j + node, 2 * (j + by) + node) for j in range(halves) if 0 <= j + by < halves
    ]
    inbox = pipelined_chain(pair_maps, pair_tips, pairs, depth, halves + points - 2, is_node)
    node_in = unflat_rows(inbox, width)
    lead_in = lax.ppermute(node_in, "chain", to_lead)
    node_own = right_apply(node_in, prev_map) + prev_tip
    return jnp.where(is_node, node_own, lead_in)


def shards(subspace, s_inv, couple, diag_blocks, weights):
    points = s_inv.shape[0]
    blocks_dev = couple.shape[0]
    block_width = couple.shape[1]
    vectors = subspace.shape[0]
    source = subspace.reshape(vectors, blocks_dev, block_width).transpose(1, 0, 2)
    zero_rows = jnp.zeros((points, 2, vectors, block_width), jnp.float32)
    plain_eye = jnp.stack(
        [
            jnp.eye(block_width, dtype=jnp.float32),
            jnp.zeros((block_width, block_width), jnp.float32),
        ]
    )
    identity_map = jnp.broadcast_to(plain_eye, (points, 2, block_width, block_width))
    chain_size = lax.axis_size("chain")

    forward_start = jnp.concatenate([identity_map, zero_rows], axis=2)
    first_pivot = s_inv[:, 0]
    first_rhs = jnp.broadcast_to(
        jnp.stack([source[0], jnp.zeros_like(source[0])])[None], zero_rows.shape
    )
    first_solved = jnp.concatenate(
        [jnp.swapaxes(first_pivot, -1, -2), inverse_apply(first_pivot, first_rhs)], axis=2
    )
    forward_both, rest_states = sweep_forward(
        s_inv, couple, couple_down(couple[0], first_solved), source, block_width, True, 1
    )
    forward_states = jnp.concatenate([first_solved[None], rest_states], axis=0)
    incoming = chain_incoming(forward_both, block_width, 1)
    solved_all = forward_states[:, :, :, block_width:] + right_apply_all(
        incoming, forward_states[:, :, :, :block_width]
    )

    backward_start = jnp.concatenate([identity_map, zero_rows], axis=2)
    backward_both, backward_all = sweep_backward(
        s_inv, couple, backward_start, solved_all, block_width, True
    )
    outgoing = chain_incoming(backward_both, block_width, -1)
    result = backward_all[:, :, :, block_width:] + right_apply_all(
        outgoing, backward_all[:, :, :, :block_width]
    )

    signed = weights * jnp.array([1.0, -1.0], jnp.float32)
    filtered_blocks = jnp.einsum("rqcnk,qc->rnk", result, signed, precision=highest)
    down_all = jnp.einsum("rnk,rkj->rnj", filtered_blocks, couple, precision=highest)
    from_next = passed_along(filtered_blocks[0], "chain", -1)
    from_prior = passed_along(down_all[-1], "chain", 1)
    diag_term = jnp.einsum("rnk,rjk->rnj", filtered_blocks, diag_blocks, precision=highest)
    upper_rows = jnp.concatenate([filtered_blocks[1:], from_next[None]], axis=0)
    term_up = jnp.einsum("rnk,rjk->rnj", upper_rows, couple, precision=highest)
    lower_rows = jnp.concatenate([from_prior[None], down_all[:-1]], axis=0)
    applied_blocks = diag_term + term_up + lower_rows
    gram_plain = jnp.einsum("rnk,rmk->nm", filtered_blocks, filtered_blocks, precision=highest)
    gram_matrix = jnp.einsum("rnk,rmk->nm", filtered_blocks, applied_blocks, precision=highest)
    summed = chain_sum(jnp.stack([gram_plain, gram_matrix]), "chain")
    grams = summed / (blocks_dev * block_width * chain_size)
    filtered = filtered_blocks.transpose(1, 0, 2).reshape(vectors, blocks_dev * block_width)
    applied = applied_blocks.transpose(1, 0, 2).reshape(vectors, blocks_dev * block_width)
    return (filtered, applied, grams)


def solution(mesh):
    placed = (
        P("parts", "chain"),
        P("parts", "chain", None, None, None),
        P("chain", "parts", None),
        P("chain", "parts", None),
        P("parts", None),
    )
    return jax.shard_map(
        shards,
        mesh=mesh,
        in_specs=placed,
        out_specs=(P("parts", "chain"), P("parts", "chain"), P(None, "parts", None)),
        check_vma=False,
    )
```

```python
import jax
import jax.numpy as jnp
from jax import lax
from jax.sharding import PartitionSpec as P

highest = lax.Precision.HIGHEST
sweep_precision = lax.Precision.HIGHEST
hop_precision = lax.Precision.HIGHEST


def passed_along(shard, axis, by):
    peers = lax.axis_size(axis)
    pairs = [(i, i + by) for i in range(peers) if 0 <= i + by < peers]
    return lax.ppermute(shard, axis, pairs)


def chain_sum(value, axis):
    peers = lax.axis_size(axis)
    if peers & (peers - 1):
        return lax.psum(value, axis)
    stride = 1
    while stride < peers:
        value = value + lax.ppermute(value, axis, [(i, i ^ stride) for i in range(peers)])
        stride *= 2
    return value


def split_signs(vecs, axis):
    real_rows = jnp.stack(
        [lax.index_in_dim(vecs, 0, axis, False), -lax.index_in_dim(vecs, 1, axis, False)], axis
    )
    imag_rows = jnp.stack(
        [lax.index_in_dim(vecs, 1, axis, False), lax.index_in_dim(vecs, 0, axis, False)], axis
    )
    return real_rows, imag_rows


def signed_rows(vecs):
    real_rows, imag_rows = split_signs(vecs, 1)
    return jnp.stack([real_rows, imag_rows], axis=1)


def inverse_apply(pivot_inv, vecs):
    return jnp.einsum(
        "qocnk,qcjk->qonj", signed_rows(vecs), pivot_inv, precision=sweep_precision
    )


def couple_down(coupling_blk, vecs):
    return jnp.einsum("qcnk,kj->qcnj", vecs, coupling_blk, precision=sweep_precision)


def couple_up(coupling_blk, vecs):
    return jnp.einsum("qcnk,jk->qcnj", vecs, coupling_blk, precision=sweep_precision)


def sweep_forward(pivots, couple, start_rows, source, rhs_rows, store_all, first=0):
    blocks_dev = couple.shape[0]

    def advance(carried, position):
        pivot_inv = lax.dynamic_index_in_dim(pivots, position, 1, keepdims=False)
        coupling_blk = lax.dynamic_index_in_dim(couple, position, 0, keepdims=False)
        combined = carried
        if source is not None:
            rhs_block = lax.dynamic_index_in_dim(source, position, 0, keepdims=False)
            rhs_full = jnp.stack([rhs_block, jnp.zeros_like(rhs_block)])
            rhs_full = jnp.broadcast_to(rhs_full[None], (combined.shape[0],) + rhs_full.shape)
            combined = combined.at[:, :, rhs_rows:].add(rhs_full)
        solved = inverse_apply(pivot_inv, combined)
        return (couple_down(coupling_blk, solved), solved if store_all else None)

    return lax.scan(advance, start_rows, jnp.arange(first, blocks_dev))


def sweep_backward(pivots, couple, start_rows, solved_all, rhs_rows, store_all):
    blocks_dev = couple.shape[0]

    def retreat(carried, position):
        pivot_inv = lax.dynamic_index_in_dim(pivots, position, 1, keepdims=False)
        coupling_blk = lax.dynamic_index_in_dim(couple, position, 0, keepdims=False)
        correction = inverse_apply(pivot_inv, couple_up(coupling_blk, carried))
        if solved_all is not None:
            known = lax.dynamic_index_in_dim(solved_all, position, 0, keepdims=False)
            correction = correction.at[:, :, rhs_rows:].add(known)
        return (correction, correction if store_all else None)

    return lax.scan(retreat, start_rows, jnp.arange(blocks_dev), reverse=True)


def block_real(matrix):
    top = jnp.concatenate([matrix[:, 0], matrix[:, 1]], axis=2)
    bottom = jnp.concatenate([-matrix[:, 1], matrix[:, 0]], axis=2)
    return jnp.concatenate([top, bottom], axis=1)


def flat_rows(vecs):
    return jnp.concatenate([vecs[:, 0], vecs[:, 1]], axis=2)


def unflat_rows(flat, width):
    return jnp.stack([flat[..., :width], flat[..., width:]], axis=1)


def right_apply(vecs, matrix):
    return jnp.einsum("qocnk,qckj->qonj", signed_rows(vecs), matrix, precision=highest)


def right_apply_all(vecs, states):
    return jnp.einsum("qocnk,rqckj->rqonj", signed_rows(vecs), states, precision=highest)


def pipelined_chain(maps, tips, pairs, depth, stages, active=True):
    points = tips.shape[0]

    def step(stage, inbox):
        point = jnp.clip(stage - depth, 0, points - 1)
        rows = lax.dynamic_index_in_dim(inbox, point, 0, keepdims=False)

        def hop():
            return jnp.dot(
                rows,
                lax.dynamic_index_in_dim(maps, point, 0, keepdims=False),
                precision=hop_precision,
            ) + lax.dynamic_index_in_dim(tips, point, 0, keepdims=False)

        out = lax.cond(active, hop, lambda: jnp.zeros_like(rows))
        got = lax.ppermute(out, "chain", pairs)
        slot = stage + 1 - depth
        keep = (slot >= 0) & (slot < points)
        slot = jnp.clip(slot, 0, points - 1)
        current = lax.dynamic_index_in_dim(inbox, slot, 0, keepdims=False)
        return lax.dynamic_update_index_in_dim(inbox, jnp.where(keep, got, current), slot, 0)

    return lax.fori_loop(0, stages, step, jnp.zeros_like(tips))


def chain_incoming(own_both, width, by):
    own_map = own_both[:, :, :width]
    own_tip = own_both[:, :, width:]
    points = own_tip.shape[0]
    peers = lax.axis_size("chain")
    rank = lax.axis_index("chain")
    if peers % 2:
        depth = rank if by > 0 else peers - 1 - rank
        pairs = [(i, i + by) for i in range(peers) if 0 <= i + by < peers]
        inbox = pipelined_chain(
            block_real(own_map), flat_rows(own_tip), pairs, depth, peers + points - 2
        )
        return unflat_rows(inbox, width)
    halves = peers // 2
    lead = 0 if by > 0 else 1
    node = 1 - lead
    to_node = [(2 * j + lead, 2 * j + node) for j in range(halves)]
    to_lead = [(2 * j + node, 2 * j + lead) for j in range(halves)]
    prev_both = lax.ppermute(own_both, "chain", to_node)
    prev_map = prev_both[:, :, :width]
    prev_tip = prev_both[:, :, width:]
    is_node = rank % 2 == node

    def compose():
        pair_both = right_apply(prev_both, own_map)
        pair_tip = pair_both[:, :, width:] + own_tip
        return block_real(pair_both[:, :, :width]), flat_rows(pair_tip)

    def idle():
        return (
            jnp.zeros((points, 2 * width, 2 * width), jnp.float32),
            jnp.zeros(own_tip.shape[:1] + own_tip.shape[2:3] + (2 * width,), jnp.float32),
        )

    pair_maps, pair_tips = lax.cond(is_node, compose, idle)
    pair_rank = rank // 2
    depth = pair_rank if by > 0 else halves - 1 - pair_rank
    pairs = [
        (2 * j + node, 2 * (j + by) + node) for j in range(halves) if 0 <= j + by < halves
    ]
    inbox = pipelined_chain(pair_maps, pair_tips, pairs, depth, halves + points - 2, is_node)
    node_in = unflat_rows(inbox, width)
    lead_in = lax.ppermute(node_in, "chain", to_lead)
    node_own = right_apply(node_in, prev_map) + prev_tip
    return jnp.where(is_node, node_own, lead_in)


def shards(subspace, s_inv, couple, diag_blocks, weights):
    points = s_inv.shape[0]
    blocks_dev = couple.shape[0]
    block_width = couple.shape[1]
    vectors = subspace.shape[0]
    source = subspace.reshape(vectors, blocks_dev, block_width).transpose(1, 0, 2)
    zero_rows = jnp.zeros((points, 2, vectors, block_width), jnp.float32)
    plain_eye = jnp.stack(
        [
            jnp.eye(block_width, dtype=jnp.float32),
            jnp.zeros((block_width, block_width), jnp.float32),
        ]
    )
    identity_map = jnp.broadcast_to(plain_eye, (points, 2, block_width, block_width))
    chain_size = lax.axis_size("chain")

    forward_start = jnp.concatenate([identity_map, zero_rows], axis=2)
    first_pivot = s_inv[:, 0]
    first_rhs = jnp.broadcast_to(
        jnp.stack([source[0], jnp.zeros_like(source[0])])[None], zero_rows.shape
    )
    first_solved = jnp.concatenate(
        [jnp.swapaxes(first_pivot, -1, -2), inverse_apply(first_pivot, first_rhs)], axis=2
    )
    forward_both, rest_states = sweep_forward(
        s_inv, couple, couple_down(couple[0], first_solved), source, block_width, True, 1
    )
    forward_states = jnp.concatenate([first_solved[None], rest_states], axis=0)
    incoming = chain_incoming(forward_both, block_width, 1)
    solved_all = forward_states[:, :, :, block_width:] + right_apply_all(
        incoming, forward_states[:, :, :, :block_width]
    )

    backward_start = jnp.concatenate([identity_map, zero_rows], axis=2)
    backward_both, backward_all = sweep_backward(
        s_inv, couple, backward_start, solved_all, block_width, True
    )
    outgoing = chain_incoming(backward_both, block_width, -1)
    result = backward_all[:, :, :, block_width:] + right_apply_all(
        outgoing, backward_all[:, :, :, :block_width]
    )

    signed = weights * jnp.array([1.0, -1.0], jnp.float32)
    filtered_blocks = jnp.einsum("rqcnk,qc->rnk", result, signed, precision=highest)
    down_all = jnp.einsum("rnk,rkj->rnj", filtered_blocks, couple, precision=highest)
    from_next = passed_along(filtered_blocks[0], "chain", -1)
    from_prior = passed_along(down_all[-1], "chain", 1)
    diag_term = jnp.einsum("rnk,rjk->rnj", filtered_blocks, diag_blocks, precision=highest)
    upper_rows = jnp.concatenate([filtered_blocks[1:], from_next[None]], axis=0)
    term_up = jnp.einsum("rnk,rjk->rnj", upper_rows, couple, precision=highest)
    lower_rows = jnp.concatenate([from_prior[None], down_all[:-1]], axis=0)
    applied_blocks = diag_term + term_up + lower_rows
    both_rows = jnp.stack([filtered_blocks, applied_blocks])
    summed = chain_sum(
        jnp.einsum("rnk,grmk->gnm", filtered_blocks, both_rows, precision=highest), "chain"
    )
    grams = summed / (blocks_dev * block_width * chain_size)
    filtered = filtered_blocks.transpose(1, 0, 2).reshape(vectors, blocks_dev * block_width)
    applied = applied_blocks.transpose(1, 0, 2).reshape(vectors, blocks_dev * block_width)
    return (filtered, applied, grams)


def solution(mesh):
    placed = (
        P("parts", "chain"),
        P("parts", "chain", None, None, None),
        P("chain", "parts", None),
        P("chain", "parts", None),
        P("parts", None),
    )
    return jax.shard_map(
        shards,
        mesh=mesh,
        in_specs=placed,
        out_specs=(P("parts", "chain"), P("parts", "chain"), P(None, "parts", None)),
        check_vma=False,
    )
```
